256 devices in a mesh: gx: 32 (over x, z_hi, core), gy: 8 (over y, z_lo).
Axes of the slice: x: 4, y: 4, z: 8 (z_hi: 4, z_lo: 2; z = z_hi * 2 + z_lo), core: 2. Of those that a mesh axis runs over, the one named last changes fastest.
Arguments:
- state: float32 [1024, 512, 384], P('gx', 'gy'), may hold values from -3 to 3
- obs_owner: int32 [2, 4096], replicated, may hold values from 0 to 255
- obs_cell: int32 [2, 4096], replicated, may hold values from 0 to 2047
- obs_level: int32 [2, 4096], replicated, may hold values from 0 to 3
- obs_coef: float32 [2, 3, 4096], replicated, may hold values from -1 to 1
- obs_value: float32 [2, 4096], replicated, may hold values from -8 to 8
- obs_error: float32 [2, 4096], replicated, may hold values from 0.5 to 2
- pattern: int32 [32, 8, 2, 16], P('gx', 'gy'), may hold values 0 or 1
Outputs:
- analysis: float32 [1024, 512, 384], P('gx', 'gy')
The draws below stay inside these ranges and needn't reach their ends.
Inputs may be any that keep to these rules, and one draw needn't show every extreme that they name: `obs_owner`: the tile numbered (its gx index) * 8 + (its gy index). `obs_cell`: cell i * 64 + j of the owner tile, i along the first dimension. `pattern`: 1 where the tile uses the block.
All inputs are finite; a program needn't handle non-finite values. Where the reference program divides by a largest or mean magnitude, that divisor is 1e-20 or more.
Results may differ from the reference program's by a relative error of at most 0.0003.
Values sent between devices are 32-bit elements; how exact they have to be, the bound alone decides.
No kernel may reach another device: no remote copies, remote signals or barrier semaphores. Data moves between devices by JAX's collectives and lax.ppermute only.
A program may use at most 128 MiB of HBM per device.

```python
import math
import jax
import jax.numpy as jnp
import numpy as np
from jax import lax

CX = 32
CY = 64
NOBS = 4096
ENS = 32
LEV = 4
COMP = 3
NBAT = 2
OBLK = 16
NSIT = 4
TX = 32
TY = 8
TILES = 256
NX = 1024
NY = 512
FEAT = 384


def touch_ends(entries, own_key, low, top_value):
    shape = entries.shape
    index_at = [jax.random.randint(jax.random.fold_in(own_key, axis), (), 0, shape[axis]) for axis in range(len(shape))]
    entries = entries.at[tuple(index_at)].set(low)
    longest = shape.index(max(shape))
    index_at[longest] = (index_at[longest] + 1) % shape[longest]
    return entries.at[tuple(index_at)].set(top_value)


def steps_of(own_key, shape, cuts, least, largest):
    loudness = 1.0
    for position, parts in cuts:
        draws = jax.random.uniform(jax.random.fold_in(jax.random.fold_in(own_key, 6), position), (parts,), jnp.float32, least / len(cuts), largest / len(cuts))
        loudness = loudness * jnp.repeat(jnp.exp(draws), shape[position] // parts).reshape((-1,) + (1,) * (len(shape) - 1 - position))
    return loudness


def cumulative_ranks(number_of, slope):
    weights = [(1 << 20) // math.isqrt(standing ** slope) + 1 for standing in range(1, number_of + 1)]
    spread = 1 + sum(weights) // (1 << 30)
    return np.cumsum(np.array([max(1, weight // spread) for weight in weights]))


def skewed_ids(own_key, extent, number_of, slope):
    grid = cumulative_ranks(number_of, slope)
    lot = jax.random.randint(jax.random.fold_in(own_key, 1), extent, 0, int(grid[number_of - 1]))
    rank = jnp.searchsorted(jnp.asarray(grid, jnp.int32), lot, side="right")
    return jax.random.permutation(jax.random.fold_in(own_key, 2), number_of)[rank].astype(jnp.int32)


def gaussian(key, dims, spread, most, cuts=(), kind=jnp.bfloat16):
    array = jax.random.normal(key, dims, jnp.float32) * spread
    if len(cuts) > 0:
        array = steps_of(key, dims, cuts, -0.22, 0.18) * array
    return jnp.clip(array, min=-most, max=most).astype(kind)


def setup_inputs(seed: int = 0) -> dict:
    arg_keys = jax.random.split(jax.random.key(seed), 9)
    return {
        "state": gaussian(arg_keys[0], (NX, NY, FEAT), 1.0, 3.0, ((0, 32), (1, 8)), jnp.float32),
        "obs_owner": touch_ends(skewed_ids(arg_keys[1], (NBAT, NOBS), TILES, 2), jax.random.fold_in(arg_keys[1], 3), 0, TILES - 1).astype(jnp.int32),
        "obs_cell": touch_ends(jax.random.randint(arg_keys[2], (NBAT, NOBS), 0, CX * CY), jax.random.fold_in(arg_keys[2], 1), 0, (CX * CY) - 1).astype(jnp.int32),
        "obs_level": touch_ends(jax.random.randint(arg_keys[3], (NBAT, NOBS), 0, LEV), jax.random.fold_in(arg_keys[3], 1), 0, LEV - 1).astype(jnp.int32),
        "obs_coef": jnp.clip(jax.random.uniform(arg_keys[4], (NBAT, COMP, NOBS), jnp.float32, -1.0, 1.0), -1.0, 1.0),
        "obs_value": gaussian(arg_keys[5], (NBAT, NOBS), 1.5, 8.0, (), jnp.float32),
        "obs_error": jnp.clip(jnp.exp(jax.random.uniform(arg_keys[6], (NBAT, NOBS), jnp.float32, math.log(0.5), math.log(2.0))), 0.5, 2.0),
        "pattern": touch_ends((jax.random.randint(arg_keys[7], (TX, TY, NBAT, OBLK), 0, 2) < 1).astype(jnp.int32), jax.random.fold_in(arg_keys[7], 1), 0, 1),
    }


courant = 0.1
diffusion = 0.08
radius_share = 0.25

def update(centre, west_cell, east_cell, south_cell, north_cell):
    speed_east = centre[:, :, 0:1]
    speed_north = centre[:, :, 1:2]
    upwind_flux = jnp.maximum(speed_east, 0.0) * (centre - west_cell) + jnp.minimum(speed_east, 0.0) * (east_cell - centre) + jnp.maximum(speed_north, 0.0) * (centre - south_cell) + jnp.minimum(speed_north, 0.0) * (north_cell - centre)
    return centre - courant * upwind_flux + diffusion * (west_cell + east_cell + (south_cell + north_cell) - 4.0 * centre)

def advance(grid_field):
    pieces = []
    for level_index in range(LEV):
        level_slab = grid_field[:, :, :, level_index * ENS:(level_index + 1) * ENS]
        pieces.append(update(level_slab, jnp.roll(level_slab, 1, axis=0), jnp.roll(level_slab, -1, axis=0), jnp.roll(level_slab, 1, axis=1), jnp.roll(level_slab, -1, axis=1)))
    return jnp.concatenate(pieces, axis=3)

def product(left, right):
    return jnp.dot(left, right, precision=lax.Precision.HIGHEST, preferred_element_type=jnp.float32)

def innovations(predicted, obs_value, obs_error):
    centre_obs = lax.optimization_barrier(jnp.mean(predicted, axis=1, keepdims=True))
    deviation = (predicted - centre_obs) / obs_error[:, None]
    innovation = (obs_value - centre_obs[:, 0]) / obs_error
    return (deviation, innovation)

def localize(owners, obs_cells, block_mask, tile_east, tile_north, span_east, span_north, tiles_north, grid_east, grid_north):
    place_east = (owners // tiles_north * span_east + obs_cells // span_north).astype(jnp.float32)
    place_north = (owners % tiles_north * span_north + obs_cells % span_north).astype(jnp.float32)
    centre_east = (tile_east * span_east).astype(jnp.float32) + (span_east - 1) / 2.0
    centre_north = (tile_north * span_north).astype(jnp.float32) + (span_north - 1) / 2.0
    gap_east = jnp.remainder(place_east - centre_east + grid_east / 2.0, grid_east) - grid_east / 2.0
    gap_north = jnp.remainder(place_north - centre_north + grid_north / 2.0, grid_north) - grid_north / 2.0
    scale_east = gap_east / (radius_share * grid_east)
    scale_north = gap_north / (radius_share * grid_north)
    weight = jnp.exp(-0.5 * (scale_east * scale_east + scale_north * scale_north))
    blocks = block_mask.shape[0]
    return (weight.reshape(blocks, -1) * block_mask.astype(jnp.float32)[:, None]).reshape(-1)

def transform(deviation, innovation, weight_obs):
    members = deviation.shape[1]
    weighted = deviation * weight_obs[:, None]
    covariance = product(weighted.T, deviation)
    projection = product(weighted.T, innovation[:, None])[:, 0]
    unit_matrix = jnp.eye(members, dtype=jnp.float32)
    system = (members - 1.0) * unit_matrix + covariance
    row_bound = jnp.max(lax.optimization_barrier(jnp.sum(jnp.abs(system), axis=1)))

    def refine(sweep_index, iterates):
        approach, inverse_root = iterates
        middle = 1.5 * unit_matrix - 0.5 * product(inverse_root, approach)
        return (product(approach, middle), product(middle, inverse_root))
    approach, inverse_root = lax.fori_loop(0, NSIT, refine, (system / row_bound, unit_matrix))
    inverse = product(inverse_root, inverse_root) / row_bound
    weights = product(inverse, projection[:, None])[:, 0]
    centring = unit_matrix - 1.0 / members
    shifts = weights[:, None] + math.sqrt(members - 1.0) * inverse_root / jnp.sqrt(row_bound)
    return 1.0 / members + product(centring, shifts)

def predict(grid_field, owners, obs_cells, levels, obs_coefs):
    place_east = owners // TY * CX + obs_cells // CY
    place_north = owners % TY * CY + obs_cells % CY
    picked = grid_field[place_east, place_north, :, levels, :]
    return obs_coefs[0][:, None] * picked[:, 0] + obs_coefs[1][:, None] * picked[:, 1] + obs_coefs[2][:, None] * picked[:, 2]

def reference(state, obs_owner, obs_cell, obs_level, obs_coef, obs_value, obs_error, pattern):
    grid_field = state.reshape(NX, NY, COMP, LEV * ENS)
    for substep in range(2):
        grid_field = advance(grid_field)
    grid_field = grid_field.reshape(NX, NY, COMP, LEV, ENS)
    for batch_index in range(NBAT):
        predicted = predict(grid_field, obs_owner[batch_index], obs_cell[batch_index], obs_level[batch_index], obs_coef[batch_index])
        deviation, innovation = innovations(predicted, obs_value[batch_index], obs_error[batch_index])

        def one_tile(tile_index):
            tile_east = tile_index // TY
            tile_north = tile_index % TY
            weight_obs = localize(obs_owner[batch_index], obs_cell[batch_index], pattern[tile_east, tile_north, batch_index], tile_east, tile_north, CX, CY, TY, NX, NY)
            return transform(deviation, innovation, weight_obs)
        all_mixes = lax.map(one_tile, jnp.arange(TILES, dtype=jnp.int32))
        tiled = grid_field.reshape(TX, CX, TY, CY, COMP * LEV, ENS)
        grid_field = jnp.einsum('aibjke,abef->aibjkf', tiled, all_mixes.reshape(TX, TY, ENS, ENS), precision=lax.Precision.HIGHEST).reshape(NX, NY, COMP, LEV, ENS)
    return grid_field.reshape(NX, NY, FEAT)
```

```python
import math

import jax
import jax.numpy as jnp
from jax import lax
from jax.sharding import PartitionSpec as P

ENS = 32
LEV = 4
COMP = 3
NSIT = 4


courant = 0.1
diffusion = 0.08
radius_share = 0.25


def extended_2(shard, sides, width):
    for axis, dim in sides:
        size, length = (lax.axis_size(axis), shard.shape[dim])
        up = [(i, (i + 1) % size) for i in range(size)]
        down = [(j, i) for i, j in up]
        last = lax.slice_in_dim(shard, length - width, length, axis=dim)
        initial = lax.slice_in_dim(shard, 0, width, axis=dim)
        before = lax.ppermute(last, axis, up)
        after = lax.ppermute(initial, axis, down)
        shard = jnp.concatenate([before, shard, after], axis=dim)
    return shard


def update(centre, west_cell, east_cell, south_cell, north_cell):
    speed_east = centre[:, :, 0:1]
    speed_north = centre[:, :, 1:2]
    upwind_flux = (
        jnp.maximum(speed_east, 0.0) * (centre - west_cell)
        + jnp.minimum(speed_east, 0.0) * (east_cell - centre)
        + jnp.maximum(speed_north, 0.0) * (centre - south_cell)
        + jnp.minimum(speed_north, 0.0) * (north_cell - centre)
    )
    return (
        centre
        - courant * upwind_flux
        + diffusion * (west_cell + east_cell + (south_cell + north_cell) - 4.0 * centre)
    )


def interior(extended):
    return update(
        extended[1:-1, 1:-1],
        extended[:-2, 1:-1],
        extended[2:, 1:-1],
        extended[1:-1, :-2],
        extended[1:-1, 2:],
    )


def advance_once(cube_field):
    extended = extended_2(cube_field, (("gx", 0), ("gy", 1)), 1)
    return interior(extended)


def product(left, right):
    return jnp.dot(left, right, precision=lax.Precision.HIGHEST, preferred_element_type=jnp.float32)


def exchange_order():
    sizes = {axis: lax.axis_size(axis) for axis in ("gx", "gy")}
    if sizes == {"gx": 32, "gy": 8}:
        return [("gx", 0), ("gy", 0), ("gx", 3), ("gy", 1), ("gx", 1), ("gx", 4), ("gy", 2), ("gx", 2)]
    order = []
    for axis in ("gx", "gy"):
        order += [(axis, b) for b in range(int(math.log2(sizes[axis])))]
    return order


def summed_everywhere(rows):
    order = exchange_order()
    for axis, bit in order:
        size = lax.axis_size(axis)
        pairs = [(i, i ^ (1 << bit)) for i in range(size)]
        upper = ((lax.axis_index(axis) >> bit) & 1) == 1
        half = rows.shape[0] // 2
        low, high = rows[:half], rows[half:]
        sent = jnp.where(upper, low, high)
        kept = jnp.where(upper, high, low)
        rows = kept + lax.ppermute(sent, axis, pairs)
    for axis, bit in reversed(order):
        size = lax.axis_size(axis)
        pairs = [(i, i ^ (1 << bit)) for i in range(size)]
        upper = ((lax.axis_index(axis) >> bit) & 1) == 1
        other = lax.ppermute(rows, axis, pairs)
        rows = jnp.where(upper, jnp.concatenate([other, rows]), jnp.concatenate([rows, other]))
    return rows


def innovations(predicted, obs_value, obs_error):
    centre_obs = jnp.mean(predicted, axis=1, keepdims=True)
    deviation = (predicted - centre_obs) / obs_error[:, None]
    innovation = (obs_value - centre_obs[:, 0]) / obs_error
    return (deviation, innovation)


def localize(
    owners,
    obs_cells,
    block_mask,
    tile_east,
    tile_north,
    span_east,
    span_north,
    tiles_north,
    grid_east,
    grid_north,
):
    place_east = (owners // tiles_north * span_east + obs_cells // span_north).astype(jnp.float32)
    place_north = (owners % tiles_north * span_north + obs_cells % span_north).astype(jnp.float32)
    centre_east = (tile_east * span_east).astype(jnp.float32) + (span_east - 1) / 2.0
    centre_north = (tile_north * span_north).astype(jnp.float32) + (span_north - 1) / 2.0
    gap_east = (
        jnp.remainder(place_east - centre_east + grid_east / 2.0, grid_east) - grid_east / 2.0
    )
    gap_north = (
        jnp.remainder(place_north - centre_north + grid_north / 2.0, grid_north) - grid_north / 2.0
    )
    scale_east = gap_east / (radius_share * grid_east)
    scale_north = gap_north / (radius_share * grid_north)
    weight = jnp.exp(-0.5 * (scale_east * scale_east + scale_north * scale_north))
    blocks = block_mask.shape[0]
    return (weight.reshape(blocks, -1) * block_mask.astype(jnp.float32)[:, None]).reshape(-1)


def transform(deviation, innovation, weight_obs):
    members = deviation.shape[1]
    weighted = deviation * weight_obs[:, None]
    covariance = product(weighted.T, deviation)
    projection = product(weighted.T, innovation[:, None])[:, 0]
    unit_matrix = jnp.eye(members, dtype=jnp.float32)
    system = (members - 1.0) * unit_matrix + covariance
    row_bound = jnp.max(jnp.sum(jnp.abs(system), axis=1))

    def refine(sweep_index, iterates):
        approach, inverse_root = iterates
        middle = 1.5 * unit_matrix - 0.5 * product(inverse_root, approach)
        return (product(approach, middle), product(middle, inverse_root))

    approach, inverse_root = lax.fori_loop(0, NSIT, refine, (system / row_bound, unit_matrix))
    inverse = product(inverse_root, inverse_root) / row_bound
    weights = product(inverse, projection[:, None])[:, 0]
    centring = unit_matrix - 1.0 / members
    shifts = weights[:, None] + math.sqrt(members - 1.0) * inverse_root / jnp.sqrt(row_bound)
    return 1.0 / members + product(centring, shifts)


def block_diagonal(mix, copies):
    return jnp.kron(jnp.eye(copies, dtype=mix.dtype), mix)


def local(state, obs_owner, obs_cell, obs_level, obs_coef, obs_value, obs_error, pattern):
    span_east, span_north, features = state.shape
    tiles_east = lax.axis_size("gx")
    tiles_north = lax.axis_size("gy")
    tile_east = lax.axis_index("gx")
    tile_north = lax.axis_index("gy")
    own_tile = tile_east * tiles_north + tile_north
    cube_field = state.reshape(span_east, span_north, COMP, features // COMP)
    for substep in range(2):
        cube_field = advance_once(cube_field)
    cells = cube_field.reshape(span_east * span_north, COMP, features // COMP)

    def observed(batch_index):
        picked = cells[obs_cell[batch_index]]
        coefs = obs_coef[batch_index]
        lanes = (
            coefs[0][:, None] * picked[:, 0]
            + coefs[1][:, None] * picked[:, 1]
            + coefs[2][:, None] * picked[:, 2]
        ).reshape(-1, LEV, ENS)
        level_hot = obs_level[batch_index][:, None] == jnp.arange(LEV)[None, :]
        predicted = jnp.sum(jnp.where(level_hot[:, :, None], lanes, 0.0), axis=1)
        return jnp.where((obs_owner[batch_index] == own_tile)[:, None], predicted, 0.0)

    def mixing(local_terms, batch_index):
        count = local_terms.shape[0]
        predicted = summed_everywhere(local_terms.reshape(-1, 128)).reshape(count, ENS)
        deviation, innovation = innovations(
            predicted, obs_value[batch_index], obs_error[batch_index]
        )
        weight_obs = localize(
            obs_owner[batch_index],
            obs_cell[batch_index],
            pattern[0, 0, batch_index],
            tile_east,
            tile_north,
            span_east,
            span_north,
            tiles_north,
            span_east * tiles_east,
            span_north * tiles_north,
        )
        return transform(deviation, innovation, weight_obs)

    first_terms = observed(0)
    second_picked = observed(1)
    first_mix = mixing(first_terms, 0)
    second_mix = mixing(product(second_picked, first_mix), 1)
    rows = cells.reshape(-1, features // COMP)
    lanes_per_row = features // COMP // ENS
    rows = product(rows, block_diagonal(first_mix, lanes_per_row))
    rows = product(rows, block_diagonal(second_mix, lanes_per_row))
    return rows.reshape(span_east, span_north, features)


def solution(mesh):
    placed = (P("gx", "gy", None), P(), P(), P(), P(), P(), P(), P("gx", "gy", None, None))
    return jax.shard_map(
        local, mesh=mesh, in_specs=placed, out_specs=P("gx", "gy", None), check_vma=False
    )
```

```python
import math

import jax
import jax.numpy as jnp
from jax import lax
from jax.experimental import pallas as pl
from jax.experimental.pallas import tpu as pltpu
from jax.sharding import PartitionSpec as P

ENS = 32
LEV = 4
COMP = 3
NSIT = 4


courant = 0.1
diffusion = 0.08
radius_share = 0.25


def advance_once(field):
    halos = []
    for axis, dim in (("gx", 0), ("gy", 1)):
        size, length = lax.axis_size(axis), field.shape[dim]
        up = [(i, (i + 1) % size) for i in range(size)]
        down = [(j, i) for i, j in up]
        last = lax.slice_in_dim(field, length - 1, length, axis=dim)
        initial = lax.slice_in_dim(field, 0, 1, axis=dim)
        halos += [lax.ppermute(last, axis, up), lax.ppermute(initial, axis, down)]
    return step(field, *halos)


def gather_kernel(cell_ref, level_ref, coef_ref, field_ref, out_ref):
    count = cell_ref.shape[0]
    width = field_ref.shape[1] // 3
    lane_level = lax.broadcasted_iota(jnp.int32, (1, width), 1) // ENS
    sublane = lax.broadcasted_iota(jnp.int32, (8, width), 0)
    groups = width // ENS

    def body(block, carry):
        gathered = [jnp.zeros((8, width), jnp.float32) for k in range(groups)]
        for i in range(8):
            for k in range(groups):
                j = (block * 8 + i) * groups + k
                picked = field_ref[pl.ds(cell_ref[j], 1), :]
                value = (
                    coef_ref[j] * picked[:, 0:width]
                    + coef_ref[count + j] * picked[:, width:2 * width]
                    + coef_ref[2 * count + j] * picked[:, 2 * width:3 * width]
                )
                value = jnp.where(lane_level == level_ref[j], value, 0.0)
                gathered[k] = jnp.where(sublane == i, value, gathered[k])
        first = pl.multiple_of(block * 8, 8)
        for k in range(groups):
            out_ref[pl.ds(first, 8), k * width:(k + 1) * width] = gathered[k]
        return carry

    lax.fori_loop(0, count // (8 * groups), body, 0)


def gather_rows(cells, levels, coefs, field):
    count = cells.shape[0]
    width = field.shape[1] // 3
    groups = width // ENS
    smem = pl.BlockSpec(memory_space=pltpu.SMEM)
    vmem = pl.BlockSpec(memory_space=pltpu.VMEM)
    return pl.pallas_call(
        gather_kernel,
        out_shape=jax.ShapeDtypeStruct((count // groups, groups * width), jnp.float32),
        in_specs=[smem, smem, smem, vmem],
        out_specs=vmem,
    )(cells, levels, coefs.reshape(-1), field)

def step_kernel(field_ref, west_ref, east_ref, south_ref, north_ref, out_ref):
    nx, ny, feat = field_ref.shape
    width = feat // 3
    row_id = lax.broadcasted_iota(jnp.int32, (ny, width), 0)

    def body(x, carry):
        centre = field_ref[x]
        west = jnp.where(x == 0, west_ref[0], field_ref[jnp.maximum(x - 1, 0)])
        east = jnp.where(x == nx - 1, east_ref[0], field_ref[jnp.minimum(x + 1, nx - 1)])
        south_edge = south_ref[x]
        north_edge = north_ref[x]
        u = centre[:, 0:width]
        v = centre[:, width:2 * width]
        pu, mu = jnp.maximum(u, 0.0), jnp.minimum(u, 0.0)
        pv, mv = jnp.maximum(v, 0.0), jnp.minimum(v, 0.0)
        for b in range(3):
            lanes = slice(b * width, (b + 1) * width)
            c = centre[:, lanes]
            w = west[:, lanes]
            e = east[:, lanes]
            s = jnp.where(row_id == 0, south_edge[:, lanes], pltpu.roll(c, 1, 0))
            n = jnp.where(row_id == ny - 1, north_edge[:, lanes], pltpu.roll(c, ny - 1, 0))
            flux = pu * (c - w) + mu * (e - c) + pv * (c - s) + mv * (n - c)
            out_ref[x, :, lanes] = c - courant * flux + diffusion * (w + e + (s + n) - 4.0 * c)
        return carry

    lax.fori_loop(0, nx, body, 0)

def step(field, west, east, south, north):
    vmem = pl.BlockSpec(memory_space=pltpu.VMEM)
    return pl.pallas_call(
        step_kernel,
        out_shape=jax.ShapeDtypeStruct(field.shape, field.dtype),
        in_specs=[vmem] * 5,
        out_specs=vmem,
    )(field, west, east, south, north)


def product(left, right):
    return jnp.dot(left, right, precision=lax.Precision.HIGHEST, preferred_element_type=jnp.float32)


def exchange_order():
    sizes = {axis: lax.axis_size(axis) for axis in ("gx", "gy")}
    if sizes == {"gx": 32, "gy": 8}:
        return [("gx", 0), ("gy", 0), ("gx", 3), ("gy", 1), ("gx", 1), ("gx", 4), ("gy", 2), ("gx", 2)]
    order = []
    for axis in ("gx", "gy"):
        order += [(axis, b) for b in range(int(math.log2(sizes[axis])))]
    return order


def summed_everywhere(rows):
    order = exchange_order()
    for axis, bit in order:
        size = lax.axis_size(axis)
        pairs = [(i, i ^ (1 << bit)) for i in range(size)]
        upper = ((lax.axis_index(axis) >> bit) & 1) == 1
        half = rows.shape[0] // 2
        low, high = rows[:half], rows[half:]
        sent = jnp.where(upper, low, high)
        kept = jnp.where(upper, high, low)
        rows = kept + lax.ppermute(sent, axis, pairs)
    for axis, bit in reversed(order):
        size = lax.axis_size(axis)
        pairs = [(i, i ^ (1 << bit)) for i in range(size)]
        upper = ((lax.axis_index(axis) >> bit) & 1) == 1
        other = lax.ppermute(rows, axis, pairs)
        rows = jnp.where(upper, jnp.concatenate([other, rows]), jnp.concatenate([rows, other]))
    return rows


def innovations(predicted, obs_value, obs_error):
    centre_obs = jnp.mean(predicted, axis=1, keepdims=True)
    deviation = (predicted - centre_obs) / obs_error[:, None]
    innovation = (obs_value - centre_obs[:, 0]) / obs_error
    return (deviation, innovation)


def localize(
    owners,
    obs_cells,
    block_mask,
    tile_east,
    tile_north,
    span_east,
    span_north,
    tiles_north,
    grid_east,
    grid_north,
):
    place_east = (owners // tiles_north * span_east + obs_cells // span_north).astype(jnp.float32)
    place_north = (owners % tiles_north * span_north + obs_cells % span_north).astype(jnp.float32)
    centre_east = (tile_east * span_east).astype(jnp.float32) + (span_east - 1) / 2.0
    centre_north = (tile_north * span_north).astype(jnp.float32) + (span_north - 1) / 2.0
    gap_east = (
        jnp.remainder(place_east - centre_east + grid_east / 2.0, grid_east) - grid_east / 2.0
    )
    gap_north = (
        jnp.remainder(place_north - centre_north + grid_north / 2.0, grid_north) - grid_north / 2.0
    )
    scale_east = gap_east / (radius_share * grid_east)
    scale_north = gap_north / (radius_share * grid_north)
    weight = jnp.exp(-0.5 * (scale_east * scale_east + scale_north * scale_north))
    blocks = block_mask.shape[0]
    return (weight.reshape(blocks, -1) * block_mask.astype(jnp.float32)[:, None]).reshape(-1)


def transform(deviation, innovation, weight_obs):
    members = deviation.shape[1]
    weighted = deviation * weight_obs[:, None]
    covariance = product(weighted.T, deviation)
    projection = product(weighted.T, innovation[:, None])[:, 0]
    unit_matrix = jnp.eye(members, dtype=jnp.float32)
    system = (members - 1.0) * unit_matrix + covariance
    row_bound = jnp.max(jnp.sum(jnp.abs(system), axis=1))

    def refine(sweep_index, iterates):
        approach, inverse_root = iterates
        middle = 1.5 * unit_matrix - 0.5 * product(inverse_root, approach)
        return (product(approach, middle), product(middle, inverse_root))

    approach, inverse_root = lax.fori_loop(0, NSIT, refine, (system / row_bound, unit_matrix))
    inverse = product(inverse_root, inverse_root) / row_bound
    weights = product(inverse, projection[:, None])[:, 0]
    centring = unit_matrix - 1.0 / members
    shifts = weights[:, None] + math.sqrt(members - 1.0) * inverse_root / jnp.sqrt(row_bound)
    return 1.0 / members + product(centring, shifts)


def block_diagonal(mix, copies):
    return jnp.kron(jnp.eye(copies, dtype=mix.dtype), mix)


def local(state, obs_owner, obs_cell, obs_level, obs_coef, obs_value, obs_error, pattern):
    span_east, span_north, features = state.shape
    tiles_east = lax.axis_size("gx")
    tiles_north = lax.axis_size("gy")
    tile_east = lax.axis_index("gx")
    tile_north = lax.axis_index("gy")
    own_tile = tile_east * tiles_north + tile_north
    field = state
    for substep in range(2):
        field = advance_once(field)
    cells = field.reshape(span_east * span_north, features)
    width = features // COMP
    groups = width // ENS
    owned = (obs_owner == own_tile).astype(jnp.float32)
    masked_coefs = jnp.transpose(obs_coef * owned[:, None, :], (1, 0, 2)).reshape(COMP, -1)
    spread = gather_rows(obs_cell.reshape(-1), obs_level.reshape(-1), masked_coefs, cells)
    spread_lane = lax.broadcasted_iota(jnp.int32, (groups * width, groups * ENS), 0)
    dense_lane = lax.broadcasted_iota(jnp.int32, (groups * width, groups * ENS), 1)
    fold = (
        (spread_lane // width == dense_lane // ENS) & (spread_lane % ENS == dense_lane % ENS)
    ).astype(jnp.float32)
    dense = product(spread, fold)
    per_batch = dense.shape[0] // 2

    def mixing(local_terms, batch_index):
        count = obs_owner.shape[1]
        predicted = summed_everywhere(local_terms).reshape(count, ENS)
        deviation, innovation = innovations(
            predicted, obs_value[batch_index], obs_error[batch_index]
        )
        weight_obs = localize(
            obs_owner[batch_index],
            obs_cell[batch_index],
            pattern[0, 0, batch_index],
            tile_east,
            tile_north,
            span_east,
            span_north,
            tiles_north,
            span_east * tiles_east,
            span_north * tiles_north,
        )
        return transform(deviation, innovation, weight_obs)

    first_mix = mixing(dense[:per_batch], 0)
    second_terms = product(dense[per_batch:], block_diagonal(first_mix, groups))
    second_mix = mixing(second_terms, 1)
    rows = product(cells, block_diagonal(first_mix, features // ENS))
    rows = product(rows, block_diagonal(second_mix, features // ENS))
    return rows.reshape(span_east, span_north, features)


def solution(mesh):
    placed = (P("gx", "gy", None), P(), P(), P(), P(), P(), P(), P("gx", "gy", None, None))
    return jax.shard_map(
        local, mesh=mesh, in_specs=placed, out_specs=P("gx", "gy", None), check_vma=False
    )
```

```python
import math

import jax
import jax.numpy as jnp
from jax import lax
from jax.experimental import pallas as pl
from jax.experimental.pallas import tpu as pltpu
from jax.sharding import PartitionSpec as P

ENS = 32
LEV = 4
COMP = 3
NSIT = 4


courant = 0.1
diffusion = 0.08
radius_share = 0.25


def advance_once(field):
    halos = []
    for axis, dim in (("gx", 0), ("gy", 1)):
        size, length = lax.axis_size(axis), field.shape[dim]
        up = [(i, (i + 1) % size) for i in range(size)]
        down = [(j, i) for i, j in up]
        last = lax.slice_in_dim(field, length - 1, length, axis=dim)
        initial = lax.slice_in_dim(field, 0, 1, axis=dim)
        halos += [lax.ppermute(last, axis, up), lax.ppermute(initial, axis, down)]
    return step(field, *halos)


def gather_kernel(cell_ref, level_ref, coef_ref, field_ref, out_ref):
    count = cell_ref.shape[0]
    width = field_ref.shape[1] // 3
    lane_level = lax.broadcasted_iota(jnp.int32, (1, width), 1) // ENS
    sublane = lax.broadcasted_iota(jnp.int32, (8, width), 0)
    groups = width // ENS

    def body(block, carry):
        gathered = [jnp.zeros((8, width), jnp.float32) for k in range(groups)]
        for i in range(8):
            for k in range(groups):
                j = (block * 8 + i) * groups + k
                picked = field_ref[pl.ds(cell_ref[j], 1), :]
                value = (
                    coef_ref[j] * picked[:, 0:width]
                    + coef_ref[count + j] * picked[:, width:2 * width]
                    + coef_ref[2 * count + j] * picked[:, 2 * width:3 * width]
                )
                value = jnp.where(lane_level == level_ref[j], value, 0.0)
                gathered[k] = jnp.where(sublane == i, value, gathered[k])
        first = pl.multiple_of(block * 8, 8)
        for k in range(groups):
            out_ref[pl.ds(first, 8), k * width:(k + 1) * width] = gathered[k]
        return carry

    lax.fori_loop(0, count // (8 * groups), body, 0)


def gather_rows(cells, levels, coefs, field):
    count = cells.shape[0]
    width = field.shape[1] // 3
    groups = width // ENS
    smem = pl.BlockSpec(memory_space=pltpu.SMEM)
    vmem = pl.BlockSpec(memory_space=pltpu.VMEM)
    return pl.pallas_call(
        gather_kernel,
        out_shape=jax.ShapeDtypeStruct((count // groups, groups * width), jnp.float32),
        in_specs=[smem, smem, smem, vmem],
        out_specs=vmem,
    )(cells, levels, coefs.reshape(-1), field)

def step_kernel(field_ref, west_ref, east_ref, south_ref, north_ref, out_ref):
    nx, ny, feat = field_ref.shape
    width = feat // 3
    row_id = lax.broadcasted_iota(jnp.int32, (ny, width), 0)

    def body(x, carry):
        centre = field_ref[x]
        west = jnp.where(x == 0, west_ref[0], field_ref[jnp.maximum(x - 1, 0)])
        east = jnp.where(x == nx - 1, east_ref[0], field_ref[jnp.minimum(x + 1, nx - 1)])
        south_edge = south_ref[x]
        north_edge = north_ref[x]
        u = centre[:, 0:width]
        v = centre[:, width:2 * width]
        pu, mu = jnp.maximum(u, 0.0), jnp.minimum(u, 0.0)
        pv, mv = jnp.maximum(v, 0.0), jnp.minimum(v, 0.0)
        for b in range(3):
            lanes = slice(b * width, (b + 1) * width)
            c = centre[:, lanes]
            w = west[:, lanes]
            e = east[:, lanes]
            s = jnp.where(row_id == 0, south_edge[:, lanes], pltpu.roll(c, 1, 0))
            n = jnp.where(row_id == ny - 1, north_edge[:, lanes], pltpu.roll(c, ny - 1, 0))
            flux = pu * (c - w) + mu * (e - c) + pv * (c - s) + mv * (n - c)
            out_ref[x, :, lanes] = c - courant * flux + diffusion * (w + e + (s + n) - 4.0 * c)
        return carry

    lax.fori_loop(0, nx, body, 0)

def step(field, west, east, south, north):
    vmem = pl.BlockSpec(memory_space=pltpu.VMEM)
    return pl.pallas_call(
        step_kernel,
        out_shape=jax.ShapeDtypeStruct(field.shape, field.dtype),
        in_specs=[vmem] * 5,
        out_specs=vmem,
    )(field, west, east, south, north)


def product(left, right):
    return jnp.dot(left, right, precision=lax.Precision.HIGHEST, preferred_element_type=jnp.float32)


def summed_everywhere(rows):
    axes = ("gx", "gy")
    devices = lax.axis_size("gx") * lax.axis_size("gy")
    parts = lax.all_to_all(rows, axes, 0, 0, tiled=True)
    chunk = parts.reshape((devices, rows.shape[0] // devices) + rows.shape[1:]).sum(axis=0)
    copies = jnp.broadcast_to(chunk[None], (devices,) + chunk.shape).reshape(rows.shape)
    return lax.all_to_all(copies, axes, 0, 0, tiled=True)


def innovations(predicted, obs_value, obs_error):
    centre_obs = jnp.mean(predicted, axis=1, keepdims=True)
    deviation = (predicted - centre_obs) / obs_error[:, None]
    innovation = (obs_value - centre_obs[:, 0]) / obs_error
    return (deviation, innovation)


def localize(
    owners,
    obs_cells,
    block_mask,
    tile_east,
    tile_north,
    span_east,
    span_north,
    tiles_north,
    grid_east,
    grid_north,
):
    place_east = (owners // tiles_north * span_east + obs_cells // span_north).astype(jnp.float32)
    place_north = (owners % tiles_north * span_north + obs_cells % span_north).astype(jnp.float32)
    centre_east = (tile_east * span_east).astype(jnp.float32) + (span_east - 1) / 2.0
    centre_north = (tile_north * span_north).astype(jnp.float32) + (span_north - 1) / 2.0
    gap_east = (
        jnp.remainder(place_east - centre_east + grid_east / 2.0, grid_east) - grid_east / 2.0
    )
    gap_north = (
        jnp.remainder(place_north - centre_north + grid_north / 2.0, grid_north) - grid_north / 2.0
    )
    scale_east = gap_east / (radius_share * grid_east)
    scale_north = gap_north / (radius_share * grid_north)
    weight = jnp.exp(-0.5 * (scale_east * scale_east + scale_north * scale_north))
    blocks = block_mask.shape[0]
    return (weight.reshape(blocks, -1) * block_mask.astype(jnp.float32)[:, None]).reshape(-1)


def transform(deviation, innovation, weight_obs):
    members = deviation.shape[1]
    weighted = deviation * weight_obs[:, None]
    covariance = product(weighted.T, deviation)
    projection = product(weighted.T, innovation[:, None])[:, 0]
    unit_matrix = jnp.eye(members, dtype=jnp.float32)
    system = (members - 1.0) * unit_matrix + covariance
    row_bound = jnp.max(jnp.sum(jnp.abs(system), axis=1))

    def refine(sweep_index, iterates):
        approach, inverse_root = iterates
        middle = 1.5 * unit_matrix - 0.5 * product(inverse_root, approach)
        return (product(approach, middle), product(middle, inverse_root))

    approach, inverse_root = lax.fori_loop(0, NSIT, refine, (system / row_bound, unit_matrix))
    inverse = product(inverse_root, inverse_root) / row_bound
    weights = product(inverse, projection[:, None])[:, 0]
    centring = unit_matrix - 1.0 / members
    shifts = weights[:, None] + math.sqrt(members - 1.0) * inverse_root / jnp.sqrt(row_bound)
    return 1.0 / members + product(centring, shifts)


def block_diagonal(mix, copies):
    return jnp.kron(jnp.eye(copies, dtype=mix.dtype), mix)


def local(state, obs_owner, obs_cell, obs_level, obs_coef, obs_value, obs_error, pattern):
    span_east, span_north, features = state.shape
    tiles_east = lax.axis_size("gx")
    tiles_north = lax.axis_size("gy")
    tile_east = lax.axis_index("gx")
    tile_north = lax.axis_index("gy")
    own_tile = tile_east * tiles_north + tile_north
    field = state
    for substep in range(2):
        field = advance_once(field)
    cells = field.reshape(span_east * span_north, features)
    width = features // COMP
    groups = width // ENS
    owned = (obs_owner == own_tile).astype(jnp.float32)
    masked_coefs = jnp.transpose(obs_coef * owned[:, None, :], (1, 0, 2)).reshape(COMP, -1)
    spread = gather_rows(obs_cell.reshape(-1), obs_level.reshape(-1), masked_coefs, cells)
    spread_lane = lax.broadcasted_iota(jnp.int32, (groups * width, groups * ENS), 0)
    dense_lane = lax.broadcasted_iota(jnp.int32, (groups * width, groups * ENS), 1)
    fold = (
        (spread_lane // width == dense_lane // ENS) & (spread_lane % ENS == dense_lane % ENS)
    ).astype(jnp.float32)
    dense = product(spread, fold)
    per_batch = dense.shape[0] // 2

    def mixing(local_terms, batch_index):
        count = obs_owner.shape[1]
        predicted = summed_everywhere(local_terms).reshape(count, ENS)
        deviation, innovation = innovations(
            predicted, obs_value[batch_index], obs_error[batch_index]
        )
        weight_obs = localize(
            obs_owner[batch_index],
            obs_cell[batch_index],
            pattern[0, 0, batch_index],
            tile_east,
            tile_north,
            span_east,
            span_north,
            tiles_north,
            span_east * tiles_east,
            span_north * tiles_north,
        )
        return transform(deviation, innovation, weight_obs)

    first_mix = mixing(dense[:per_batch], 0)
    second_terms = product(dense[per_batch:], block_diagonal(first_mix, groups))
    second_mix = mixing(second_terms, 1)
    rows = product(cells, block_diagonal(first_mix, features // ENS))
    rows = product(rows, block_diagonal(second_mix, features // ENS))
    return rows.reshape(span_east, span_north, features)


def solution(mesh):
    placed = (P("gx", "gy", None), P(), P(), P(), P(), P(), P(), P("gx", "gy", None, None))
    return jax.shard_map(
        local, mesh=mesh, in_specs=placed, out_specs=P("gx", "gy", None), check_vma=False
    )
```

```python
import math

import jax
import jax.numpy as jnp
from jax import lax
from jax.experimental import pallas as pl
from jax.experimental.pallas import tpu as pltpu
from jax.sharding import PartitionSpec as P

ENS = 32
LEV = 4
COMP = 3
NSIT = 4


courant = 0.1
diffusion = 0.08
radius_share = 0.25


def advance_once(field):
    halos = []
    for axis, dim in (("gx", 0), ("gy", 1)):
        size, length = lax.axis_size(axis), field.shape[dim]
        up = [(i, (i + 1) % size) for i in range(size)]
        down = [(j, i) for i, j in up]
        last = lax.slice_in_dim(field, length - 1, length, axis=dim)
        initial = lax.slice_in_dim(field, 0, 1, axis=dim)
        halos += [lax.ppermute(last, axis, up), lax.ppermute(initial, axis, down)]
    return step(field, *halos)


def gather_kernel(cell_ref, level_ref, coef_ref, field_ref, out_ref):
    count = cell_ref.shape[0]
    width = field_ref.shape[1] // 3
    lane_level = lax.broadcasted_iota(jnp.int32, (1, width), 1) // ENS
    sublane = lax.broadcasted_iota(jnp.int32, (8, width), 0)
    groups = width // ENS

    def body(block, carry):
        gathered = [jnp.zeros((8, width), jnp.float32) for k in range(groups)]
        for i in range(8):
            for k in range(groups):
                j = (block * 8 + i) * groups + k
                picked = field_ref[pl.ds(cell_ref[j], 1), :]
                value = (
                    coef_ref[j] * picked[:, 0:width]
                    + coef_ref[count + j] * picked[:, width:2 * width]
                    + coef_ref[2 * count + j] * picked[:, 2 * width:3 * width]
                )
                value = jnp.where(lane_level == level_ref[j], value, 0.0)
                gathered[k] = jnp.where(sublane == i, value, gathered[k])
        first = pl.multiple_of(block * 8, 8)
        for k in range(groups):
            out_ref[pl.ds(first, 8), k * width:(k + 1) * width] = gathered[k]
        return carry

    lax.fori_loop(0, count // (8 * groups), body, 0)


def gather_rows(cells, levels, coefs, field):
    count = cells.shape[0]
    width = field.shape[1] // 3
    groups = width // ENS
    smem = pl.BlockSpec(memory_space=pltpu.SMEM)
    vmem = pl.BlockSpec(memory_space=pltpu.VMEM)
    return pl.pallas_call(
        gather_kernel,
        out_shape=jax.ShapeDtypeStruct((count // groups, groups * width), jnp.float32),
        in_specs=[smem, smem, smem, vmem],
        out_specs=vmem,
    )(cells, levels, coefs.reshape(-1), field)

def step_kernel(field_ref, west_ref, east_ref, south_ref, north_ref, out_ref):
    nx, ny, feat = field_ref.shape
    width = feat // 3
    row_id = lax.broadcasted_iota(jnp.int32, (ny, width), 0)

    def body(x, carry):
        centre = field_ref[x]
        west = jnp.where(x == 0, west_ref[0], field_ref[jnp.maximum(x - 1, 0)])
        east = jnp.where(x == nx - 1, east_ref[0], field_ref[jnp.minimum(x + 1, nx - 1)])
        south_edge = south_ref[x]
        north_edge = north_ref[x]
        u = centre[:, 0:width]
        v = centre[:, width:2 * width]
        pu, mu = jnp.maximum(u, 0.0), jnp.minimum(u, 0.0)
        pv, mv = jnp.maximum(v, 0.0), jnp.minimum(v, 0.0)
        for b in range(3):
            lanes = slice(b * width, (b + 1) * width)
            c = centre[:, lanes]
            w = west[:, lanes]
            e = east[:, lanes]
            s = jnp.where(row_id == 0, south_edge[:, lanes], pltpu.roll(c, 1, 0))
            n = jnp.where(row_id == ny - 1, north_edge[:, lanes], pltpu.roll(c, ny - 1, 0))
            flux = pu * (c - w) + mu * (e - c) + pv * (c - s) + mv * (n - c)
            out_ref[x, :, lanes] = c - courant * flux + diffusion * (w + e + (s + n) - 4.0 * c)
        return carry

    lax.fori_loop(0, nx, body, 0)

def step(field, west, east, south, north):
    vmem = pl.BlockSpec(memory_space=pltpu.VMEM)
    return pl.pallas_call(
        step_kernel,
        out_shape=jax.ShapeDtypeStruct(field.shape, field.dtype),
        in_specs=[vmem] * 5,
        out_specs=vmem,
    )(field, west, east, south, north)


def product(left, right):
    return jnp.dot(left, right, precision=lax.Precision.HIGHEST, preferred_element_type=jnp.float32)


def mix_kernel(rows_ref, first_ref, second_ref, out_ref):
    width = first_ref.shape[0]
    for block in range(rows_ref.shape[1] // width):
        lanes = slice(block * width, (block + 1) * width)
        once = product(rows_ref[:, lanes], first_ref[...])
        out_ref[:, lanes] = product(once, second_ref[...])


def mixed_twice(rows, first, second):
    count, features = rows.shape
    width = first.shape[0]
    tile = 256
    return pl.pallas_call(
        mix_kernel,
        out_shape=jax.ShapeDtypeStruct(rows.shape, rows.dtype),
        grid=(count // tile,),
        in_specs=[
            pl.BlockSpec((tile, features), lambda i: (i, 0)),
            pl.BlockSpec((width, width), lambda i: (0, 0)),
            pl.BlockSpec((width, width), lambda i: (0, 0)),
        ],
        out_specs=pl.BlockSpec((tile, features), lambda i: (i, 0)),
    )(rows, first, second)


def summed_everywhere(rows):
    axes = ("gx", "gy")
    devices = lax.axis_size("gx") * lax.axis_size("gy")
    parts = lax.all_to_all(rows, axes, 0, 0, tiled=True)
    chunk = parts.reshape((devices, rows.shape[0] // devices) + rows.shape[1:]).sum(axis=0)
    copies = jnp.broadcast_to(chunk[None], (devices,) + chunk.shape).reshape(rows.shape)
    return lax.all_to_all(copies, axes, 0, 0, tiled=True)


def localize(
    owners,
    obs_cells,
    block_mask,
    tile_east,
    tile_north,
    span_east,
    span_north,
    tiles_north,
    grid_east,
    grid_north,
):
    place_east = (owners // tiles_north * span_east + obs_cells // span_north).astype(jnp.float32)
    place_north = (owners % tiles_north * span_north + obs_cells % span_north).astype(jnp.float32)
    centre_east = (tile_east * span_east).astype(jnp.float32) + (span_east - 1) / 2.0
    centre_north = (tile_north * span_north).astype(jnp.float32) + (span_north - 1) / 2.0
    gap_east = (
        jnp.remainder(place_east - centre_east + grid_east / 2.0, grid_east) - grid_east / 2.0
    )
    gap_north = (
        jnp.remainder(place_north - centre_north + grid_north / 2.0, grid_north) - grid_north / 2.0
    )
    scale_east = gap_east / (radius_share * grid_east)
    scale_north = gap_north / (radius_share * grid_north)
    weight = jnp.exp(-0.5 * (scale_east * scale_east + scale_north * scale_north))
    blocks = block_mask.shape[0]
    return (weight.reshape(blocks, -1) * block_mask.astype(jnp.float32)[:, None]).reshape(-1)


def transform(predicted, obs_value, obs_error, weight_obs):
    rows, width = predicted.shape
    groups = width // ENS
    members = ENS

    def spread(per_obs):
        return jnp.broadcast_to(per_obs.reshape(rows, groups, 1), (rows, groups, ENS)).reshape(rows, width)

    lane_in = lax.broadcasted_iota(jnp.int32, (width, width), 0) // ENS
    lane_out = lax.broadcasted_iota(jnp.int32, (width, width), 1) // ENS
    averaging = jnp.where(lane_in == lane_out, 1.0 / members, 0.0).astype(jnp.float32)
    centre_obs = product(predicted, averaging)
    error = spread(obs_error)
    deviation = (predicted - centre_obs) / error
    innovation = (spread(obs_value) - centre_obs) / error
    weighted = deviation * spread(weight_obs)
    blocks = product(weighted.T, deviation)
    covariance = sum(blocks[k * ENS:(k + 1) * ENS, k * ENS:(k + 1) * ENS] for k in range(groups))
    projected = jnp.sum(weighted * innovation, axis=0)
    projection = sum(projected[k * ENS:(k + 1) * ENS] for k in range(groups))
    unit_matrix = jnp.eye(members, dtype=jnp.float32)
    system = (members - 1.0) * unit_matrix + covariance
    row_bound = jnp.max(jnp.sum(jnp.abs(system), axis=1))

    def refine(sweep_index, iterates):
        approach, inverse_root = iterates
        middle = 1.5 * unit_matrix - 0.5 * product(inverse_root, approach)
        return (product(approach, middle), product(middle, inverse_root))

    approach, inverse_root = lax.fori_loop(0, NSIT, refine, (system / row_bound, unit_matrix))
    inverse = product(inverse_root, inverse_root) / row_bound
    weights = product(inverse, projection[:, None])[:, 0]
    centring = unit_matrix - 1.0 / members
    shifts = weights[:, None] + math.sqrt(members - 1.0) * inverse_root / jnp.sqrt(row_bound)
    return 1.0 / members + product(centring, shifts)


def block_diagonal(mix, copies):
    return jnp.kron(jnp.eye(copies, dtype=mix.dtype), mix)


def local(state, obs_owner, obs_cell, obs_level, obs_coef, obs_value, obs_error, pattern):
    span_east, span_north, features = state.shape
    tiles_east = lax.axis_size("gx")
    tiles_north = lax.axis_size("gy")
    tile_east = lax.axis_index("gx")
    tile_north = lax.axis_index("gy")
    own_tile = tile_east * tiles_north + tile_north
    field = state
    for substep in range(2):
        field = advance_once(field)
    cells = field.reshape(span_east * span_north, features)
    width = features // COMP
    groups = width // ENS
    owned = (obs_owner == own_tile).astype(jnp.float32)
    masked_coefs = jnp.transpose(obs_coef * owned[:, None, :], (1, 0, 2)).reshape(COMP, -1)
    spread = gather_rows(obs_cell.reshape(-1), obs_level.reshape(-1), masked_coefs, cells)
    spread_lane = lax.broadcasted_iota(jnp.int32, (groups * width, groups * ENS), 0)
    dense_lane = lax.broadcasted_iota(jnp.int32, (groups * width, groups * ENS), 1)
    fold = (
        (spread_lane // width == dense_lane // ENS) & (spread_lane % ENS == dense_lane % ENS)
    ).astype(jnp.float32)
    dense = product(spread, fold)
    per_batch = dense.shape[0] // 2

    def mixing(local_terms, batch_index):
        predicted = summed_everywhere(local_terms)
        weight_obs = localize(
            obs_owner[batch_index],
            obs_cell[batch_index],
            pattern[0, 0, batch_index],
            tile_east,
            tile_north,
            span_east,
            span_north,
            tiles_north,
            span_east * tiles_east,
            span_north * tiles_north,
        )
        return transform(predicted, obs_value[batch_index], obs_error[batch_index], weight_obs)

    first_mix = mixing(dense[:per_batch], 0)
    second_terms = product(dense[per_batch:], block_diagonal(first_mix, groups))
    second_mix = mixing(second_terms, 1)
    rows = mixed_twice(cells, block_diagonal(first_mix, groups), block_diagonal(second_mix, groups))
    return rows.reshape(span_east, span_north, features)


def solution(mesh):
    placed = (P("gx", "gy", None), P(), P(), P(), P(), P(), P(), P("gx", "gy", None, None))
    return jax.shard_map(
        local, mesh=mesh, in_specs=placed, out_specs=P("gx", "gy", None), check_vma=False
    )
```

```python
import math

import jax
import jax.numpy as jnp
from jax import lax
from jax.experimental import pallas as pl
from jax.experimental.pallas import tpu as pltpu
from jax.sharding import PartitionSpec as P

ENS = 32
LEV = 4
COMP = 3
NSIT = 4


courant = 0.1
diffusion = 0.08
radius_share = 0.25


def advance_once(field):
    halos = []
    for axis, dim in (("gx", 0), ("gy", 1)):
        size, length = lax.axis_size(axis), field.shape[dim]
        up = [(i, (i + 1) % size) for i in range(size)]
        down = [(j, i) for i, j in up]
        last = lax.slice_in_dim(field, length - 1, length, axis=dim)
        initial = lax.slice_in_dim(field, 0, 1, axis=dim)
        halos += [lax.ppermute(last, axis, up), lax.ppermute(initial, axis, down)]
    return step(field, *halos)


def gather_kernel(cell_ref, level_ref, coef_ref, field_ref, out_ref):
    count = cell_ref.shape[0]
    width = field_ref.shape[1] // 3
    lane_level = lax.broadcasted_iota(jnp.int32, (1, width), 1) // ENS
    sublane = lax.broadcasted_iota(jnp.int32, (8, width), 0)
    groups = width // ENS

    def body(block, carry):
        gathered = [jnp.zeros((8, width), jnp.float32) for k in range(groups)]
        for i in range(8):
            for k in range(groups):
                j = (block * 8 + i) * groups + k
                picked = field_ref[pl.ds(cell_ref[j], 1), :]
                value = (
                    coef_ref[j] * picked[:, 0:width]
                    + coef_ref[count + j] * picked[:, width:2 * width]
                    + coef_ref[2 * count + j] * picked[:, 2 * width:3 * width]
                )
                value = jnp.where(lane_level == level_ref[j], value, 0.0)
                gathered[k] = jnp.where(sublane == i, value, gathered[k])
        first = pl.multiple_of(block * 8, 8)
        for k in range(groups):
            out_ref[pl.ds(first, 8), k * width:(k + 1) * width] = gathered[k]
        return carry

    lax.fori_loop(0, count // (8 * groups), body, 0)


def gather_rows(cells, levels, coefs, field):
    count = cells.shape[0]
    width = field.shape[1] // 3
    groups = width // ENS
    smem = pl.BlockSpec(memory_space=pltpu.SMEM)
    vmem = pl.BlockSpec(memory_space=pltpu.VMEM)
    return pl.pallas_call(
        gather_kernel,
        out_shape=jax.ShapeDtypeStruct((count // groups, groups * width), jnp.float32),
        in_specs=[smem, smem, smem, vmem],
        out_specs=vmem,
    )(cells, levels, coefs.reshape(-1), field)

def step_kernel(field_ref, west_ref, east_ref, south_ref, north_ref, out_ref):
    nx, ny, feat = field_ref.shape
    width = feat // 3
    row_id = lax.broadcasted_iota(jnp.int32, (ny, width), 0)

    def body(x, carry):
        centre = field_ref[x]
        west = jnp.where(x == 0, west_ref[0], field_ref[jnp.maximum(x - 1, 0)])
        east = jnp.where(x == nx - 1, east_ref[0], field_ref[jnp.minimum(x + 1, nx - 1)])
        south_edge = south_ref[x]
        north_edge = north_ref[x]
        u = centre[:, 0:width]
        v = centre[:, width:2 * width]
        pu, mu = jnp.maximum(u, 0.0), jnp.minimum(u, 0.0)
        pv, mv = jnp.maximum(v, 0.0), jnp.minimum(v, 0.0)
        for b in range(3):
            lanes = slice(b * width, (b + 1) * width)
            c = centre[:, lanes]
            w = west[:, lanes]
            e = east[:, lanes]
            s = jnp.where(row_id == 0, south_edge[:, lanes], pltpu.roll(c, 1, 0))
            n = jnp.where(row_id == ny - 1, north_edge[:, lanes], pltpu.roll(c, ny - 1, 0))
            flux = pu * (c - w) + mu * (e - c) + pv * (c - s) + mv * (n - c)
            out_ref[x, :, lanes] = c - courant * flux + diffusion * (w + e + (s + n) - 4.0 * c)
        return carry

    lax.fori_loop(0, nx, body, 0)

def step(field, west, east, south, north):
    vmem = pl.BlockSpec(memory_space=pltpu.VMEM)
    return pl.pallas_call(
        step_kernel,
        out_shape=jax.ShapeDtypeStruct(field.shape, field.dtype),
        in_specs=[vmem] * 5,
        out_specs=vmem,
    )(field, west, east, south, north)


def product(left, right):
    return jnp.dot(left, right, precision=lax.Precision.HIGHEST, preferred_element_type=jnp.float32)


def mix_kernel(rows_ref, mix_ref, out_ref):
    width = mix_ref.shape[0]
    for block in range(rows_ref.shape[1] // width):
        lanes = slice(block * width, (block + 1) * width)
        out_ref[:, lanes] = product(rows_ref[:, lanes], mix_ref[...])


def mixed_once(rows, mix):
    count, features = rows.shape
    width = mix.shape[0]
    tile = 256
    return pl.pallas_call(
        mix_kernel,
        out_shape=jax.ShapeDtypeStruct(rows.shape, rows.dtype),
        grid=(count // tile,),
        in_specs=[
            pl.BlockSpec((tile, features), lambda i: (i, 0)),
            pl.BlockSpec((width, width), lambda i: (0, 0)),
        ],
        out_specs=pl.BlockSpec((tile, features), lambda i: (i, 0)),
    )(rows, mix)


def summed_everywhere(rows):
    axes = ("gx", "gy")
    devices = lax.axis_size("gx") * lax.axis_size("gy")
    parts = lax.all_to_all(rows, axes, 0, 0, tiled=True)
    chunk = parts.reshape((devices, rows.shape[0] // devices) + rows.shape[1:]).sum(axis=0)
    copies = jnp.broadcast_to(chunk[None], (devices,) + chunk.shape).reshape(rows.shape)
    return lax.all_to_all(copies, axes, 0, 0, tiled=True)


def localize(
    owners,
    obs_cells,
    block_mask,
    tile_east,
    tile_north,
    span_east,
    span_north,
    tiles_north,
    grid_east,
    grid_north,
):
    place_east = (owners // tiles_north * span_east + obs_cells // span_north).astype(jnp.float32)
    place_north = (owners % tiles_north * span_north + obs_cells % span_north).astype(jnp.float32)
    centre_east = (tile_east * span_east).astype(jnp.float32) + (span_east - 1) / 2.0
    centre_north = (tile_north * span_north).astype(jnp.float32) + (span_north - 1) / 2.0
    gap_east = (
        jnp.remainder(place_east - centre_east + grid_east / 2.0, grid_east) - grid_east / 2.0
    )
    gap_north = (
        jnp.remainder(place_north - centre_north + grid_north / 2.0, grid_north) - grid_north / 2.0
    )
    scale_east = gap_east / (radius_share * grid_east)
    scale_north = gap_north / (radius_share * grid_north)
    weight = jnp.exp(-0.5 * (scale_east * scale_east + scale_north * scale_north))
    blocks = block_mask.shape[0]
    return (weight.reshape(blocks, -1) * block_mask.astype(jnp.float32)[:, None]).reshape(-1)


def transform(predicted, obs_value, obs_error, weight_obs):
    rows, width = predicted.shape
    groups = width // ENS
    members = ENS

    def spread(per_obs):
        return jnp.broadcast_to(per_obs.reshape(rows, groups, 1), (rows, groups, ENS)).reshape(rows, width)

    lane_in = lax.broadcasted_iota(jnp.int32, (width, width), 0) // ENS
    lane_out = lax.broadcasted_iota(jnp.int32, (width, width), 1) // ENS
    averaging = jnp.where(lane_in == lane_out, 1.0 / members, 0.0).astype(jnp.float32)
    centre_obs = product(predicted, averaging)
    error = spread(obs_error)
    deviation = (predicted - centre_obs) / error
    innovation = (spread(obs_value) - centre_obs) / error
    weighted = deviation * spread(weight_obs)
    blocks = product(weighted.T, deviation)
    covariance = sum(blocks[k * ENS:(k + 1) * ENS, k * ENS:(k + 1) * ENS] for k in range(groups))
    projected = jnp.sum(weighted * innovation, axis=0)
    projection = sum(projected[k * ENS:(k + 1) * ENS] for k in range(groups))
    unit_matrix = jnp.eye(members, dtype=jnp.float32)
    system = (members - 1.0) * unit_matrix + covariance
    row_bound = jnp.max(jnp.sum(jnp.abs(system), axis=1))

    def refine(sweep_index, iterates):
        approach, inverse_root = iterates
        middle = 1.5 * unit_matrix - 0.5 * product(inverse_root, approach)
        return (product(approach, middle), product(middle, inverse_root))

    approach, inverse_root = lax.fori_loop(0, NSIT, refine, (system / row_bound, unit_matrix))
    inverse = product(inverse_root, inverse_root) / row_bound
    weights = product(inverse, projection[:, None])[:, 0]
    centring = unit_matrix - 1.0 / members
    shifts = weights[:, None] + math.sqrt(members - 1.0) * inverse_root / jnp.sqrt(row_bound)
    return 1.0 / members + product(centring, shifts)


def block_diagonal(mix, copies):
    return jnp.kron(jnp.eye(copies, dtype=mix.dtype), mix)


def local(state, obs_owner, obs_cell, obs_level, obs_coef, obs_value, obs_error, pattern):
    span_east, span_north, features = state.shape
    tiles_east = lax.axis_size("gx")
    tiles_north = lax.axis_size("gy")
    tile_east = lax.axis_index("gx")
    tile_north = lax.axis_index("gy")
    own_tile = tile_east * tiles_north + tile_north
    field = state
    for substep in range(2):
        field = advance_once(field)
    cells = field.reshape(span_east * span_north, features)
    width = features // COMP
    groups = width // ENS
    owned = (obs_owner == own_tile).astype(jnp.float32)
    spread_lane = lax.broadcasted_iota(jnp.int32, (groups * width, groups * ENS), 0)
    dense_lane = lax.broadcasted_iota(jnp.int32, (groups * width, groups * ENS), 1)
    fold = (
        (spread_lane // width == dense_lane // ENS) & (spread_lane % ENS == dense_lane % ENS)
    ).astype(jnp.float32)

    def observed(batch_index):
        masked_coefs = obs_coef[batch_index] * owned[batch_index][None, :]
        spread = gather_rows(obs_cell[batch_index], obs_level[batch_index], masked_coefs, cells)
        return product(spread, fold)


    def mixing(local_terms, batch_index):
        predicted = summed_everywhere(local_terms)
        weight_obs = localize(
            obs_owner[batch_index],
            obs_cell[batch_index],
            pattern[0, 0, batch_index],
            tile_east,
            tile_north,
            span_east,
            span_north,
            tiles_north,
            span_east * tiles_east,
            span_north * tiles_north,
        )
        return transform(predicted, obs_value[batch_index], obs_error[batch_index], weight_obs)

    first_mix = mixing(observed(0), 0)
    second_terms = product(observed(1), block_diagonal(first_mix, groups))
    second_mix = mixing(second_terms, 1)
    rows = mixed_once(cells, block_diagonal(product(first_mix, second_mix), groups))
    return rows.reshape(span_east, span_north, features)


def solution(mesh):
    placed = (P("gx", "gy", None), P(), P(), P(), P(), P(), P(), P("gx", "gy", None, None))
    return jax.shard_map(
        local, mesh=mesh, in_specs=placed, out_specs=P("gx", "gy", None), check_vma=False
    )
```

```python
import math

import jax
import jax.numpy as jnp
from jax import lax
from jax.experimental import pallas as pl
from jax.experimental.pallas import tpu as pltpu
from jax.sharding import PartitionSpec as P

ENS = 32
LEV = 4
COMP = 3
NSIT = 4


courant = 0.1
diffusion = 0.08
radius_share = 0.25


def advance_once(field):
    halos = []
    for axis, dim in (("gx", 0), ("gy", 1)):
        size, length = lax.axis_size(axis), field.shape[dim]
        up = [(i, (i + 1) % size) for i in range(size)]
        down = [(j, i) for i, j in up]
        last = lax.slice_in_dim(field, length - 1, length, axis=dim)
        initial = lax.slice_in_dim(field, 0, 1, axis=dim)
        halos += [lax.ppermute(last, axis, up), lax.ppermute(initial, axis, down)]
    return step(field, *halos)


def gather_kernel(flag_ref, cell_ref, level_ref, coef_ref, field_ref, out_ref, chosen_ref):
    count = cell_ref.shape[0]
    groups, rows, width = out_ref.shape
    lane_level = lax.broadcasted_iota(jnp.int32, (1, width), 1) // ENS
    sublane = lax.broadcasted_iota(jnp.int32, (8, width), 0)
    out_ref[...] = jnp.zeros(out_ref.shape, out_ref.dtype)

    def choose(j, taken):
        chosen_ref[taken] = j
        return taken + flag_ref[j]

    taken = lax.fori_loop(0, count, choose, 0, unroll=8)

    def body(i, carry):
        j = chosen_ref[i]
        picked = field_ref[pl.ds(cell_ref[j], 1), :]
        value = (
            coef_ref[j] * picked[:, 0:width]
            + coef_ref[count + j] * picked[:, width:2 * width]
            + coef_ref[2 * count + j] * picked[:, 2 * width:3 * width]
        )
        value = jnp.where(lane_level == level_ref[j], value, 0.0)
        row = j // groups
        first = pl.multiple_of((row // 8) * 8, 8)
        tile = out_ref[j % groups, pl.ds(first, 8), :]
        out_ref[j % groups, pl.ds(first, 8), :] = jnp.where(sublane == row % 8, value, tile)
        return carry

    lax.fori_loop(0, taken, body, 0)


def gather_rows(flags, cells, levels, coefs, field):
    count = cells.shape[0]
    width = field.shape[1] // 3
    groups = width // ENS
    smem = pl.BlockSpec(memory_space=pltpu.SMEM)
    vmem = pl.BlockSpec(memory_space=pltpu.VMEM)
    return pl.pallas_call(
        gather_kernel,
        out_shape=jax.ShapeDtypeStruct((groups, count // groups, width), jnp.float32),
        in_specs=[smem, smem, smem, smem, vmem],
        out_specs=vmem,
        scratch_shapes=[pltpu.SMEM((count,), jnp.int32)],
    )(flags, cells, levels, coefs.reshape(-1), field)


def step_kernel(field_ref, west_ref, east_ref, south_ref, north_ref, out_ref):
    nx, ny, feat = field_ref.shape
    width = feat // 3
    row_id = lax.broadcasted_iota(jnp.int32, (ny, width), 0)

    def body(x, carry):
        centre = field_ref[x]
        west = jnp.where(x == 0, west_ref[0], field_ref[jnp.maximum(x - 1, 0)])
        east = jnp.where(x == nx - 1, east_ref[0], field_ref[jnp.minimum(x + 1, nx - 1)])
        south_edge = south_ref[x]
        north_edge = north_ref[x]
        u = centre[:, 0:width]
        v = centre[:, width:2 * width]
        pu, mu = jnp.maximum(u, 0.0), jnp.minimum(u, 0.0)
        pv, mv = jnp.maximum(v, 0.0), jnp.minimum(v, 0.0)
        for b in range(3):
            lanes = slice(b * width, (b + 1) * width)
            c = centre[:, lanes]
            w = west[:, lanes]
            e = east[:, lanes]
            s = jnp.where(row_id == 0, south_edge[:, lanes], pltpu.roll(c, 1, 0))
            n = jnp.where(row_id == ny - 1, north_edge[:, lanes], pltpu.roll(c, ny - 1, 0))
            flux = pu * (c - w) + mu * (e - c) + pv * (c - s) + mv * (n - c)
            out_ref[x, :, lanes] = c - courant * flux + diffusion * (w + e + (s + n) - 4.0 * c)
        return carry

    lax.fori_loop(0, nx, body, 0)

def step(field, west, east, south, north):
    vmem = pl.BlockSpec(memory_space=pltpu.VMEM)
    return pl.pallas_call(
        step_kernel,
        out_shape=jax.ShapeDtypeStruct(field.shape, field.dtype),
        in_specs=[vmem] * 5,
        out_specs=vmem,
    )(field, west, east, south, north)


def product(left, right):
    return jnp.dot(left, right, precision=lax.Precision.HIGHEST, preferred_element_type=jnp.float32)


def mix_kernel(rows_ref, mix_ref, out_ref):
    width = mix_ref.shape[0]
    for block in range(rows_ref.shape[1] // width):
        lanes = slice(block * width, (block + 1) * width)
        out_ref[:, lanes] = product(rows_ref[:, lanes], mix_ref[...])


def mixed_once(rows, mix):
    count, features = rows.shape
    width = mix.shape[0]
    tile = 512
    return pl.pallas_call(
        mix_kernel,
        out_shape=jax.ShapeDtypeStruct(rows.shape, rows.dtype),
        grid=(count // tile,),
        in_specs=[
            pl.BlockSpec((tile, features), lambda i: (i, 0)),
            pl.BlockSpec((width, width), lambda i: (0, 0)),
        ],
        out_specs=pl.BlockSpec((tile, features), lambda i: (i, 0)),
    )(rows, mix)


def summed_everywhere(rows):
    axes = ("gx", "gy")
    devices = lax.axis_size("gx") * lax.axis_size("gy")
    parts = lax.all_to_all(rows, axes, 0, 0, tiled=True)
    chunk = parts.reshape((devices, rows.shape[0] // devices) + rows.shape[1:]).sum(axis=0)
    copies = jnp.broadcast_to(chunk[None], (devices,) + chunk.shape).reshape(rows.shape)
    return lax.all_to_all(copies, axes, 0, 0, tiled=True)


def localize(
    owners,
    obs_cells,
    block_mask,
    tile_east,
    tile_north,
    span_east,
    span_north,
    tiles_north,
    grid_east,
    grid_north,
):
    place_east = (owners // tiles_north * span_east + obs_cells // span_north).astype(jnp.float32)
    place_north = (owners % tiles_north * span_north + obs_cells % span_north).astype(jnp.float32)
    centre_east = (tile_east * span_east).astype(jnp.float32) + (span_east - 1) / 2.0
    centre_north = (tile_north * span_north).astype(jnp.float32) + (span_north - 1) / 2.0
    gap_east = (
        jnp.remainder(place_east - centre_east + grid_east / 2.0, grid_east) - grid_east / 2.0
    )
    gap_north = (
        jnp.remainder(place_north - centre_north + grid_north / 2.0, grid_north) - grid_north / 2.0
    )
    scale_east = gap_east / (radius_share * grid_east)
    scale_north = gap_north / (radius_share * grid_north)
    weight = jnp.exp(-0.5 * (scale_east * scale_east + scale_north * scale_north))
    blocks = block_mask.shape[0]
    return (weight.reshape(blocks, -1) * block_mask.astype(jnp.float32)[:, None]).reshape(-1)


def transform(predicted, obs_value, obs_error, weight_obs):
    rows, width = predicted.shape
    groups = width // ENS
    members = ENS

    def spread(per_obs):
        return jnp.broadcast_to(per_obs.reshape(rows, groups, 1), (rows, groups, ENS)).reshape(rows, width)

    lane_in = lax.broadcasted_iota(jnp.int32, (width, width), 0) // ENS
    lane_out = lax.broadcasted_iota(jnp.int32, (width, width), 1) // ENS
    averaging = jnp.where(lane_in == lane_out, 1.0 / members, 0.0).astype(jnp.float32)
    centre_obs = product(predicted, averaging)
    error = spread(obs_error)
    deviation = (predicted - centre_obs) / error
    innovation = (spread(obs_value) - centre_obs) / error
    weighted = deviation * spread(weight_obs)
    blocks = product(weighted.T, deviation)
    covariance = sum(blocks[k * ENS:(k + 1) * ENS, k * ENS:(k + 1) * ENS] for k in range(groups))
    projected = jnp.sum(weighted * innovation, axis=0)
    projection = sum(projected[k * ENS:(k + 1) * ENS] for k in range(groups))
    unit_matrix = jnp.eye(members, dtype=jnp.float32)
    system = (members - 1.0) * unit_matrix + covariance
    row_bound = jnp.max(jnp.sum(jnp.abs(system), axis=1))

    def refine(sweep_index, iterates):
        approach, inverse_root = iterates
        middle = 1.5 * unit_matrix - 0.5 * product(inverse_root, approach)
        return (product(approach, middle), product(middle, inverse_root))

    approach, inverse_root = lax.fori_loop(0, NSIT, refine, (system / row_bound, unit_matrix))
    inverse = product(inverse_root, inverse_root) / row_bound
    weights = product(inverse, projection[:, None])[:, 0]
    centring = unit_matrix - 1.0 / members
    shifts = weights[:, None] + math.sqrt(members - 1.0) * inverse_root / jnp.sqrt(row_bound)
    return 1.0 / members + product(centring, shifts)


def block_diagonal(mix, copies):
    return jnp.kron(jnp.eye(copies, dtype=mix.dtype), mix)


def local(state, obs_owner, obs_cell, obs_level, obs_coef, obs_value, obs_error, pattern):
    span_east, span_north, features = state.shape
    tiles_east = lax.axis_size("gx")
    tiles_north = lax.axis_size("gy")
    tile_east = lax.axis_index("gx")
    tile_north = lax.axis_index("gy")
    own_tile = tile_east * tiles_north + tile_north
    field = state
    for substep in range(2):
        field = advance_once(field)
    cells = field.reshape(span_east * span_north, features)
    width = features // COMP
    groups = width // ENS
    owned = (obs_owner == own_tile).astype(jnp.float32)
    lane_in = lax.broadcasted_iota(jnp.int32, (groups, width, groups * ENS), 0)
    level_lane = lax.broadcasted_iota(jnp.int32, (groups, width, groups * ENS), 1)
    dense_lane = lax.broadcasted_iota(jnp.int32, (groups, width, groups * ENS), 2)
    fold = ((lane_in == dense_lane // ENS) & (level_lane % ENS == dense_lane % ENS)).astype(jnp.float32)

    def folded(spread):
        return jnp.einsum(
            "krl,klo->ro", spread, fold, precision=lax.Precision.HIGHEST,
            preferred_element_type=jnp.float32,
        )

    def observed(batch_index):
        masked_coefs = obs_coef[batch_index] * owned[batch_index][None, :]
        spread = gather_rows(
            owned[batch_index].astype(jnp.int32),
            obs_cell[batch_index],
            obs_level[batch_index],
            masked_coefs,
            cells,
        )
        return folded(spread)

    def mixing(local_terms, batch_index):
        predicted = summed_everywhere(local_terms)
        weight_obs = localize(
            obs_owner[batch_index],
            obs_cell[batch_index],
            pattern[0, 0, batch_index],
            tile_east,
            tile_north,
            span_east,
            span_north,
            tiles_north,
            span_east * tiles_east,
            span_north * tiles_north,
        )
        return transform(predicted, obs_value[batch_index], obs_error[batch_index], weight_obs)

    first_mix = mixing(observed(0), 0)
    second_terms = product(observed(1), block_diagonal(first_mix, groups))
    second_mix = mixing(second_terms, 1)
    rows = mixed_once(cells, block_diagonal(product(first_mix, second_mix), groups))
    return rows.reshape(span_east, span_north, features)


def solution(mesh):
    placed = (P("gx", "gy", None), P(), P(), P(), P(), P(), P(), P("gx", "gy", None, None))
    return jax.shard_map(
        local, mesh=mesh, in_specs=placed, out_specs=P("gx", "gy", None), check_vma=False
    )
```

```python
import math

import jax
import jax.numpy as jnp
from jax import lax
from jax.experimental import pallas as pl
from jax.experimental.pallas import tpu as pltpu
from jax.sharding import PartitionSpec as P

ENS = 32
LEV = 4
COMP = 3
NSIT = 4


courant = 0.1
diffusion = 0.08
radius_share = 0.25


def gather_kernel(flag_ref, cell_ref, level_ref, coef_ref, field_ref, out_ref, chosen_ref):
    count = cell_ref.shape[0]
    groups, rows, width = out_ref.shape
    lane_level = lax.broadcasted_iota(jnp.int32, (1, width), 1) // ENS
    sublane = lax.broadcasted_iota(jnp.int32, (8, width), 0)
    out_ref[...] = jnp.zeros(out_ref.shape, out_ref.dtype)

    def choose(j, taken):
        chosen_ref[taken] = j
        return taken + flag_ref[j]

    taken = lax.fori_loop(0, count, choose, 0, unroll=8)

    def body(i, carry):
        j = chosen_ref[i]
        picked = field_ref[pl.ds(cell_ref[j], 1), :]
        value = (
            coef_ref[j] * picked[:, 0:width]
            + coef_ref[count + j] * picked[:, width:2 * width]
            + coef_ref[2 * count + j] * picked[:, 2 * width:3 * width]
        )
        value = jnp.where(lane_level == level_ref[j], value, 0.0)
        row = j // groups
        first = pl.multiple_of((row // 8) * 8, 8)
        tile = out_ref[j % groups, pl.ds(first, 8), :]
        out_ref[j % groups, pl.ds(first, 8), :] = jnp.where(sublane == row % 8, value, tile)
        return carry

    lax.fori_loop(0, taken, body, 0)


def gather_rows(flags, cells, levels, coefs, field):
    count = cells.shape[0]
    width = field.shape[1] // 3
    groups = width // ENS
    smem = pl.BlockSpec(memory_space=pltpu.SMEM)
    vmem = pl.BlockSpec(memory_space=pltpu.VMEM)
    return pl.pallas_call(
        gather_kernel,
        out_shape=jax.ShapeDtypeStruct((groups, count // groups, width), jnp.float32),
        in_specs=[smem, smem, smem, smem, vmem],
        out_specs=vmem,
        scratch_shapes=[pltpu.SMEM((count,), jnp.int32)],
    )(flags, cells, levels, coefs.reshape(-1), field)


def advect_update(c, w, e, s, n, width):
    u = c[:, 0:width]
    v = c[:, width:2 * width]
    pu, mu = jnp.maximum(u, 0.0), jnp.minimum(u, 0.0)
    pv, mv = jnp.maximum(v, 0.0), jnp.minimum(v, 0.0)
    blocks = []
    for b in range(3):
        lanes = slice(b * width, (b + 1) * width)
        cc, ww, ee, ss, nn = c[:, lanes], w[:, lanes], e[:, lanes], s[:, lanes], n[:, lanes]
        flux = pu * (cc - ww) + mu * (ee - cc) + pv * (cc - ss) + mv * (nn - cc)
        blocks.append(cc - courant * flux + diffusion * (ww + ee + (ss + nn) - 4.0 * cc))
    return blocks


def shifted(values, edge, shift):
    count = values.shape[0]
    row = lax.broadcasted_iota(jnp.int32, values.shape, 0)
    fresh = 0 if shift == 1 else count - 1
    return jnp.where(row == fresh, edge, pltpu.roll(values, shift % count, 0))


def two_steps_kernel(
    field_ref, west_ref, east_ref, south0_ref, south1_ref, north0_ref, north1_ref,
    first_col_ref, last_col_ref, corner_ref, out_ref, mid_ref, ring_ref,
):
    nx, ny, feat = field_ref.shape
    width = feat // 3

    def store(ref, index, blocks):
        for b in range(3):
            ref[index, :, b * width:(b + 1) * width] = blocks[b]

    def first_pass(x, carry):
        centre = field_ref[x]
        west = jnp.where(x == 0, west_ref[1], field_ref[jnp.maximum(x - 1, 0)])
        east = jnp.where(x == nx - 1, east_ref[0], field_ref[jnp.minimum(x + 1, nx - 1)])
        south = shifted(centre, south1_ref[pl.ds(x, 1), :], 1)
        north = shifted(centre, north0_ref[pl.ds(x, 1), :], -1)
        store(mid_ref, x, advect_update(centre, west, east, south, north, width))
        return carry

    lax.fori_loop(0, nx, first_pass, 0)
    corner = corner_ref[...]
    centre = west_ref[1]
    ring_w = advect_update(centre, west_ref[0], field_ref[0], shifted(centre, corner[0:1], 1), shifted(centre, corner[1:2], -1), width)
    centre = east_ref[0]
    ring_e = advect_update(centre, field_ref[nx - 1], east_ref[1], shifted(centre, corner[2:3], 1), shifted(centre, corner[3:4], -1), width)
    centre = south1_ref[...]
    ring_s = advect_update(centre, shifted(centre, corner[0:1], 1), shifted(centre, corner[2:3], -1), south0_ref[...], first_col_ref[...], width)
    centre = north0_ref[...]
    ring_n = advect_update(centre, shifted(centre, corner[1:2], 1), shifted(centre, corner[3:4], -1), last_col_ref[...], north1_ref[...], width)
    store(ring_ref, 0, ring_w)
    store(ring_ref, 1, ring_e)
    for b in range(3):
        ring_ref[2, 0:nx, b * width:(b + 1) * width] = ring_s[b]
        ring_ref[3, 0:nx, b * width:(b + 1) * width] = ring_n[b]

    def second_pass(x, carry):
        centre = mid_ref[x]
        west = jnp.where(x == 0, ring_ref[0], mid_ref[jnp.maximum(x - 1, 0)])
        east = jnp.where(x == nx - 1, ring_ref[1], mid_ref[jnp.minimum(x + 1, nx - 1)])
        south = shifted(centre, ring_ref[2, pl.ds(x, 1), :], 1)
        north = shifted(centre, ring_ref[3, pl.ds(x, 1), :], -1)
        store(out_ref, x, advect_update(centre, west, east, south, north, width))
        return carry

    lax.fori_loop(0, nx, second_pass, 0)


def two_steps(field, west, east, south0, south1, north0, north1, first_col, last_col, corner):
    nx, ny, feat = field.shape
    vmem = pl.BlockSpec(memory_space=pltpu.VMEM)
    return pl.pallas_call(
        two_steps_kernel,
        out_shape=jax.ShapeDtypeStruct(field.shape, field.dtype),
        in_specs=[vmem] * 10,
        out_specs=vmem,
        scratch_shapes=[
            pltpu.VMEM(field.shape, jnp.float32),
            pltpu.VMEM((4, max(nx, ny), feat), jnp.float32),
        ],
    )(field, west, east, south0, south1, north0, north1, first_col, last_col, corner)


def advance_twice(field):
    nx, ny, feat = field.shape
    sx, sy = lax.axis_size("gx"), lax.axis_size("gy")
    up_x = [(i, (i + 1) % sx) for i in range(sx)]
    down_x = [(j, i) for i, j in up_x]
    up_y = [(i, (i + 1) % sy) for i in range(sy)]
    down_y = [(j, i) for i, j in up_y]
    west = lax.ppermute(field[nx - 2:], "gx", up_x)
    east = lax.ppermute(field[:2], "gx", down_x)
    south = lax.ppermute(field[:, ny - 2:], "gy", up_y)
    north = lax.ppermute(field[:, :2], "gy", down_y)

    def diagonal(piece, step_x, step_y):
        pairs = [
            (i * sy + j, ((i + step_x) % sx) * sy + (j + step_y) % sy)
            for i in range(sx)
            for j in range(sy)
        ]
        return lax.ppermute(piece, ("gx", "gy"), pairs)

    corner = jnp.concatenate(
        [
            diagonal(field[nx - 1, ny - 1:], 1, 1),
            diagonal(field[nx - 1, :1], 1, -1),
            diagonal(field[0, ny - 1:], -1, 1),
            diagonal(field[0, :1], -1, -1),
        ]
    )
    return two_steps(
        field, west, east, south[:, 0], south[:, 1], north[:, 0], north[:, 1],
        field[:, 0], field[:, ny - 1], corner,
    )


def product(left, right):
    return jnp.dot(left, right, precision=lax.Precision.HIGHEST, preferred_element_type=jnp.float32)


def mix_kernel(rows_ref, mix_ref, out_ref):
    width = mix_ref.shape[0]
    for block in range(rows_ref.shape[1] // width):
        lanes = slice(block * width, (block + 1) * width)
        out_ref[:, lanes] = product(rows_ref[:, lanes], mix_ref[...])


def mixed_once(rows, mix):
    count, features = rows.shape
    width = mix.shape[0]
    tile = 512
    return pl.pallas_call(
        mix_kernel,
        out_shape=jax.ShapeDtypeStruct(rows.shape, rows.dtype),
        grid=(count // tile,),
        in_specs=[
            pl.BlockSpec((tile, features), lambda i: (i, 0)),
            pl.BlockSpec((width, width), lambda i: (0, 0)),
        ],
        out_specs=pl.BlockSpec((tile, features), lambda i: (i, 0)),
    )(rows, mix)


def summed_everywhere(rows):
    axes = ("gx", "gy")
    devices = lax.axis_size("gx") * lax.axis_size("gy")
    parts = lax.all_to_all(rows, axes, 0, 0, tiled=True)
    chunk = parts.reshape((devices, rows.shape[0] // devices) + rows.shape[1:]).sum(axis=0)
    copies = jnp.broadcast_to(chunk[None], (devices,) + chunk.shape).reshape(rows.shape)
    return lax.all_to_all(copies, axes, 0, 0, tiled=True)


def localize(
    owners,
    obs_cells,
    block_mask,
    tile_east,
    tile_north,
    span_east,
    span_north,
    tiles_north,
    grid_east,
    grid_north,
):
    place_east = (owners // tiles_north * span_east + obs_cells // span_north).astype(jnp.float32)
    place_north = (owners % tiles_north * span_north + obs_cells % span_north).astype(jnp.float32)
    centre_east = (tile_east * span_east).astype(jnp.float32) + (span_east - 1) / 2.0
    centre_north = (tile_north * span_north).astype(jnp.float32) + (span_north - 1) / 2.0
    gap_east = (
        jnp.remainder(place_east - centre_east + grid_east / 2.0, grid_east) - grid_east / 2.0
    )
    gap_north = (
        jnp.remainder(place_north - centre_north + grid_north / 2.0, grid_north) - grid_north / 2.0
    )
    scale_east = gap_east / (radius_share * grid_east)
    scale_north = gap_north / (radius_share * grid_north)
    weight = jnp.exp(-0.5 * (scale_east * scale_east + scale_north * scale_north))
    blocks = block_mask.shape[0]
    return (weight.reshape(blocks, -1) * block_mask.astype(jnp.float32)[:, None]).reshape(-1)


def transform(predicted, obs_value, obs_error, weight_obs):
    rows, width = predicted.shape
    groups = width // ENS
    members = ENS

    def spread(per_obs):
        return jnp.broadcast_to(per_obs.reshape(rows, groups, 1), (rows, groups, ENS)).reshape(rows, width)

    lane_in = lax.broadcasted_iota(jnp.int32, (width, width), 0) // ENS
    lane_out = lax.broadcasted_iota(jnp.int32, (width, width), 1) // ENS
    averaging = jnp.where(lane_in == lane_out, 1.0 / members, 0.0).astype(jnp.float32)
    centre_obs = product(predicted, averaging)
    error = spread(obs_error)
    deviation = (predicted - centre_obs) / error
    innovation = (spread(obs_value) - centre_obs) / error
    weighted = deviation * spread(weight_obs)
    blocks = product(weighted.T, deviation)
    covariance = sum(blocks[k * ENS:(k + 1) * ENS, k * ENS:(k + 1) * ENS] for k in range(groups))
    projected = jnp.sum(weighted * innovation, axis=0)
    projection = sum(projected[k * ENS:(k + 1) * ENS] for k in range(groups))
    unit_matrix = jnp.eye(members, dtype=jnp.float32)
    system = (members - 1.0) * unit_matrix + covariance
    row_bound = jnp.max(jnp.sum(jnp.abs(system), axis=1))

    def refine(sweep_index, iterates):
        approach, inverse_root = iterates
        middle = 1.5 * unit_matrix - 0.5 * product(inverse_root, approach)
        return (product(approach, middle), product(middle, inverse_root))

    approach, inverse_root = lax.fori_loop(0, NSIT, refine, (system / row_bound, unit_matrix))
    inverse = product(inverse_root, inverse_root) / row_bound
    weights = product(inverse, projection[:, None])[:, 0]
    centring = unit_matrix - 1.0 / members
    shifts = weights[:, None] + math.sqrt(members - 1.0) * inverse_root / jnp.sqrt(row_bound)
    return 1.0 / members + product(centring, shifts)


def block_diagonal(mix, copies):
    return jnp.kron(jnp.eye(copies, dtype=mix.dtype), mix)


def local(state, obs_owner, obs_cell, obs_level, obs_coef, obs_value, obs_error, pattern):
    span_east, span_north, features = state.shape
    tiles_east = lax.axis_size("gx")
    tiles_north = lax.axis_size("gy")
    tile_east = lax.axis_index("gx")
    tile_north = lax.axis_index("gy")
    own_tile = tile_east * tiles_north + tile_north
    field = advance_twice(state)
    cells = field.reshape(span_east * span_north, features)
    width = features // COMP
    groups = width // ENS
    owned = (obs_owner == own_tile).astype(jnp.float32)
    lane_in = lax.broadcasted_iota(jnp.int32, (groups, width, groups * ENS), 0)
    level_lane = lax.broadcasted_iota(jnp.int32, (groups, width, groups * ENS), 1)
    dense_lane = lax.broadcasted_iota(jnp.int32, (groups, width, groups * ENS), 2)
    fold = ((lane_in == dense_lane // ENS) & (level_lane % ENS == dense_lane % ENS)).astype(jnp.float32)

    def folded(spread):
        return jnp.einsum(
            "krl,klo->ro", spread, fold, precision=lax.Precision.HIGHEST,
            preferred_element_type=jnp.float32,
        )

    def observed(batch_index):
        masked_coefs = obs_coef[batch_index] * owned[batch_index][None, :]
        spread = gather_rows(
            owned[batch_index].astype(jnp.int32),
            obs_cell[batch_index],
            obs_level[batch_index],
            masked_coefs,
            cells,
        )
        return folded(spread)

    def mixing(local_terms, batch_index):
        predicted = summed_everywhere(local_terms)
        weight_obs = localize(
            obs_owner[batch_index],
            obs_cell[batch_index],
            pattern[0, 0, batch_index],
            tile_east,
            tile_north,
            span_east,
            span_north,
            tiles_north,
            span_east * tiles_east,
            span_north * tiles_north,
        )
        return transform(predicted, obs_value[batch_index], obs_error[batch_index], weight_obs)

    first_mix = mixing(observed(0), 0)
    second_terms = product(observed(1), block_diagonal(first_mix, groups))
    second_mix = mixing(second_terms, 1)
    rows = mixed_once(cells, block_diagonal(product(first_mix, second_mix), groups))
    return rows.reshape(span_east, span_north, features)


def solution(mesh):
    placed = (P("gx", "gy", None), P(), P(), P(), P(), P(), P(), P("gx", "gy", None, None))
    return jax.shard_map(
        local, mesh=mesh, in_specs=placed, out_specs=P("gx", "gy", None), check_vma=False
    )
```

```python
import math

import jax
import jax.numpy as jnp
from jax import lax
from jax.experimental import pallas as pl
from jax.experimental.pallas import tpu as pltpu
from jax.sharding import PartitionSpec as P

ENS = 32
LEV = 4
COMP = 3
NSIT = 4


courant = 0.1
diffusion = 0.08
radius_share = 0.25


def gather_kernel(flag_ref, cell_ref, level_ref, coef_ref, field_ref, out_ref, chosen_ref):
    count = cell_ref.shape[0]
    groups, rows, width = out_ref.shape
    lane_level = lax.broadcasted_iota(jnp.int32, (1, width), 1) // ENS
    sublane = lax.broadcasted_iota(jnp.int32, (8, width), 0)
    out_ref[...] = jnp.zeros(out_ref.shape, out_ref.dtype)

    def choose(j, taken):
        chosen_ref[taken] = j
        return taken + flag_ref[j]

    taken = lax.fori_loop(0, count, choose, 0, unroll=8)

    def body(i, carry):
        j = chosen_ref[i]
        picked = field_ref[pl.ds(cell_ref[j], 1), :]
        value = (
            coef_ref[j] * picked[:, 0:width]
            + coef_ref[count + j] * picked[:, width:2 * width]
            + coef_ref[2 * count + j] * picked[:, 2 * width:3 * width]
        )
        value = jnp.where(lane_level == level_ref[j], value, 0.0)
        row = j // groups
        first = pl.multiple_of((row // 8) * 8, 8)
        tile = out_ref[j % groups, pl.ds(first, 8), :]
        out_ref[j % groups, pl.ds(first, 8), :] = jnp.where(sublane == row % 8, value, tile)
        return carry

    lax.fori_loop(0, taken, body, 0)


def gather_rows(flags, cells, levels, coefs, field):
    count = cells.shape[0]
    width = field.shape[1] // 3
    groups = width // ENS
    smem = pl.BlockSpec(memory_space=pltpu.SMEM)
    vmem = pl.BlockSpec(memory_space=pltpu.VMEM)
    return pl.pallas_call(
        gather_kernel,
        out_shape=jax.ShapeDtypeStruct((groups, count // groups, width), jnp.float32),
        in_specs=[smem, smem, smem, smem, vmem],
        out_specs=vmem,
        scratch_shapes=[pltpu.SMEM((count,), jnp.int32)],
    )(flags, cells, levels, coefs.reshape(-1), field)


def advect_update(c, w, e, s, n, width):
    u = c[:, 0:width]
    v = c[:, width:2 * width]
    pu, mu = jnp.maximum(u, 0.0), jnp.minimum(u, 0.0)
    pv, mv = jnp.maximum(v, 0.0), jnp.minimum(v, 0.0)
    blocks = []
    for b in range(3):
        lanes = slice(b * width, (b + 1) * width)
        cc, ww, ee, ss, nn = c[:, lanes], w[:, lanes], e[:, lanes], s[:, lanes], n[:, lanes]
        flux = pu * (cc - ww) + mu * (ee - cc) + pv * (cc - ss) + mv * (nn - cc)
        blocks.append(cc - courant * flux + diffusion * (ww + ee + (ss + nn) - 4.0 * cc))
    return blocks


def shifted(values, edge, shift):
    count = values.shape[0]
    row = lax.broadcasted_iota(jnp.int32, values.shape, 0)
    fresh = 0 if shift == 1 else count - 1
    return jnp.where(row == fresh, edge, pltpu.roll(values, shift % count, 0))


def two_steps_kernel(
    field_ref, west_ref, east_ref, south0_ref, south1_ref, north0_ref, north1_ref,
    first_col_ref, last_col_ref, corner_ref, out_ref, mid_ref, ring_ref,
):
    nx, ny, feat = field_ref.shape
    width = feat // 3

    def store(ref, index, blocks):
        for b in range(3):
            ref[index, :, b * width:(b + 1) * width] = blocks[b]

    def first_pass(x, carry):
        centre = field_ref[x]
        west = jnp.where(x == 0, west_ref[1], field_ref[jnp.maximum(x - 1, 0)])
        east = jnp.where(x == nx - 1, east_ref[0], field_ref[jnp.minimum(x + 1, nx - 1)])
        south = shifted(centre, south1_ref[pl.ds(x, 1), :], 1)
        north = shifted(centre, north0_ref[pl.ds(x, 1), :], -1)
        store(mid_ref, x, advect_update(centre, west, east, south, north, width))
        return carry

    lax.fori_loop(0, nx, first_pass, 0)
    corner = corner_ref[...]
    centre = west_ref[1]
    ring_w = advect_update(centre, west_ref[0], field_ref[0], shifted(centre, corner[0:1], 1), shifted(centre, corner[1:2], -1), width)
    centre = east_ref[0]
    ring_e = advect_update(centre, field_ref[nx - 1], east_ref[1], shifted(centre, corner[2:3], 1), shifted(centre, corner[3:4], -1), width)
    centre = south1_ref[...]
    ring_s = advect_update(centre, shifted(centre, corner[0:1], 1), shifted(centre, corner[2:3], -1), south0_ref[...], first_col_ref[...], width)
    centre = north0_ref[...]
    ring_n = advect_update(centre, shifted(centre, corner[1:2], 1), shifted(centre, corner[3:4], -1), last_col_ref[...], north1_ref[...], width)
    store(ring_ref, 0, ring_w)
    store(ring_ref, 1, ring_e)
    for b in range(3):
        ring_ref[2, 0:nx, b * width:(b + 1) * width] = ring_s[b]
        ring_ref[3, 0:nx, b * width:(b + 1) * width] = ring_n[b]

    def second_pass(x, carry):
        centre = mid_ref[x]
        west = jnp.where(x == 0, ring_ref[0], mid_ref[jnp.maximum(x - 1, 0)])
        east = jnp.where(x == nx - 1, ring_ref[1], mid_ref[jnp.minimum(x + 1, nx - 1)])
        south = shifted(centre, ring_ref[2, pl.ds(x, 1), :], 1)
        north = shifted(centre, ring_ref[3, pl.ds(x, 1), :], -1)
        store(out_ref, x, advect_update(centre, west, east, south, north, width))
        return carry

    lax.fori_loop(0, nx, second_pass, 0)


def two_steps(field, west, east, south0, south1, north0, north1, first_col, last_col, corner):
    nx, ny, feat = field.shape
    vmem = pl.BlockSpec(memory_space=pltpu.VMEM)
    return pl.pallas_call(
        two_steps_kernel,
        out_shape=jax.ShapeDtypeStruct(field.shape, field.dtype),
        in_specs=[vmem] * 10,
        out_specs=vmem,
        scratch_shapes=[
            pltpu.VMEM(field.shape, jnp.float32),
            pltpu.VMEM((4, max(nx, ny), feat), jnp.float32),
        ],
    )(field, west, east, south0, south1, north0, north1, first_col, last_col, corner)


def advance_twice(field):
    nx, ny, feat = field.shape
    sx, sy = lax.axis_size("gx"), lax.axis_size("gy")
    up_x = [(i, (i + 1) % sx) for i in range(sx)]
    down_x = [(j, i) for i, j in up_x]
    up_y = [(i, (i + 1) % sy) for i in range(sy)]
    down_y = [(j, i) for i, j in up_y]
    west = lax.ppermute(field[nx - 2:], "gx", up_x)
    east = lax.ppermute(field[:2], "gx", down_x)
    last_cols = jnp.concatenate([west[:, ny - 2:], field[:, ny - 2:], east[:, ny - 2:]])
    first_cols = jnp.concatenate([west[:, :2], field[:, :2], east[:, :2]])
    south = lax.ppermute(last_cols, "gy", up_y)
    north = lax.ppermute(first_cols, "gy", down_y)
    corner = jnp.stack([south[1, 1], north[1, 0], south[nx + 2, 1], north[nx + 2, 0]])
    return two_steps(
        field, west, east, south[2:nx + 2, 0], south[2:nx + 2, 1], north[2:nx + 2, 0], north[2:nx + 2, 1],
        field[:, 0], field[:, ny - 1], corner,
    )


def product(left, right):
    return jnp.dot(left, right, precision=lax.Precision.HIGHEST, preferred_element_type=jnp.float32)


def mix_kernel(rows_ref, mix_ref, out_ref):
    width = mix_ref.shape[0]
    for block in range(rows_ref.shape[1] // width):
        lanes = slice(block * width, (block + 1) * width)
        out_ref[:, lanes] = product(rows_ref[:, lanes], mix_ref[...])


def mixed_once(rows, mix):
    count, features = rows.shape
    width = mix.shape[0]
    tile = 512
    return pl.pallas_call(
        mix_kernel,
        out_shape=jax.ShapeDtypeStruct(rows.shape, rows.dtype),
        grid=(count // tile,),
        in_specs=[
            pl.BlockSpec((tile, features), lambda i: (i, 0)),
            pl.BlockSpec((width, width), lambda i: (0, 0)),
        ],
        out_specs=pl.BlockSpec((tile, features), lambda i: (i, 0)),
    )(rows, mix)


def summed_everywhere(rows):
    axes = ("gx", "gy")
    devices = lax.axis_size("gx") * lax.axis_size("gy")
    parts = lax.all_to_all(rows, axes, 0, 0, tiled=True)
    chunk = parts.reshape((devices, rows.shape[0] // devices) + rows.shape[1:]).sum(axis=0)
    copies = jnp.broadcast_to(chunk[None], (devices,) + chunk.shape).reshape(rows.shape)
    return lax.all_to_all(copies, axes, 0, 0, tiled=True)


def localize(
    owners,
    obs_cells,
    block_mask,
    tile_east,
    tile_north,
    span_east,
    span_north,
    tiles_north,
    grid_east,
    grid_north,
):
    place_east = (owners // tiles_north * span_east + obs_cells // span_north).astype(jnp.float32)
    place_north = (owners % tiles_north * span_north + obs_cells % span_north).astype(jnp.float32)
    centre_east = (tile_east * span_east).astype(jnp.float32) + (span_east - 1) / 2.0
    centre_north = (tile_north * span_north).astype(jnp.float32) + (span_north - 1) / 2.0
    gap_east = (
        jnp.remainder(place_east - centre_east + grid_east / 2.0, grid_east) - grid_east / 2.0
    )
    gap_north = (
        jnp.remainder(place_north - centre_north + grid_north / 2.0, grid_north) - grid_north / 2.0
    )
    scale_east = gap_east / (radius_share * grid_east)
    scale_north = gap_north / (radius_share * grid_north)
    weight = jnp.exp(-0.5 * (scale_east * scale_east + scale_north * scale_north))
    blocks = block_mask.shape[0]
    return (weight.reshape(blocks, -1) * block_mask.astype(jnp.float32)[:, None]).reshape(-1)


def transform(predicted, obs_value, obs_error, weight_obs):
    rows, width = predicted.shape
    groups = width // ENS
    members = ENS

    def spread(per_obs):
        return jnp.broadcast_to(per_obs.reshape(rows, groups, 1), (rows, groups, ENS)).reshape(rows, width)

    lane_in = lax.broadcasted_iota(jnp.int32, (width, width), 0) // ENS
    lane_out = lax.broadcasted_iota(jnp.int32, (width, width), 1) // ENS
    averaging = jnp.where(lane_in == lane_out, 1.0 / members, 0.0).astype(jnp.float32)
    centre_obs = product(predicted, averaging)
    error = spread(obs_error)
    deviation = (predicted - centre_obs) / error
    innovation = (spread(obs_value) - centre_obs) / error
    weighted = deviation * spread(weight_obs)
    blocks = product(weighted.T, deviation)
    covariance = sum(blocks[k * ENS:(k + 1) * ENS, k * ENS:(k + 1) * ENS] for k in range(groups))
    projected = jnp.sum(weighted * innovation, axis=0)
    projection = sum(projected[k * ENS:(k + 1) * ENS] for k in range(groups))
    unit_matrix = jnp.eye(members, dtype=jnp.float32)
    system = (members - 1.0) * unit_matrix + covariance
    row_bound = jnp.max(jnp.sum(jnp.abs(system), axis=1))

    def refine(sweep_index, iterates):
        approach, inverse_root = iterates
        middle = 1.5 * unit_matrix - 0.5 * product(inverse_root, approach)
        return (product(approach, middle), product(middle, inverse_root))

    approach, inverse_root = lax.fori_loop(0, NSIT, refine, (system / row_bound, unit_matrix))
    inverse = product(inverse_root, inverse_root) / row_bound
    weights = product(inverse, projection[:, None])[:, 0]
    centring = unit_matrix - 1.0 / members
    shifts = weights[:, None] + math.sqrt(members - 1.0) * inverse_root / jnp.sqrt(row_bound)
    return 1.0 / members + product(centring, shifts)


def block_diagonal(mix, copies):
    return jnp.kron(jnp.eye(copies, dtype=mix.dtype), mix)


def local(state, obs_owner, obs_cell, obs_level, obs_coef, obs_value, obs_error, pattern):
    span_east, span_north, features = state.shape
    tiles_east = lax.axis_size("gx")
    tiles_north = lax.axis_size("gy")
    tile_east = lax.axis_index("gx")
    tile_north = lax.axis_index("gy")
    own_tile = tile_east * tiles_north + tile_north
    field = advance_twice(state)
    cells = field.reshape(span_east * span_north, features)
    width = features // COMP
    groups = width // ENS
    owned = (obs_owner == own_tile).astype(jnp.float32)
    lane_in = lax.broadcasted_iota(jnp.int32, (groups, width, groups * ENS), 0)
    level_lane = lax.broadcasted_iota(jnp.int32, (groups, width, groups * ENS), 1)
    dense_lane = lax.broadcasted_iota(jnp.int32, (groups, width, groups * ENS), 2)
    fold = ((lane_in == dense_lane // ENS) & (level_lane % ENS == dense_lane % ENS)).astype(jnp.float32)

    def folded(spread):
        return jnp.einsum(
            "krl,klo->ro", spread, fold, precision=lax.Precision.HIGHEST,
            preferred_element_type=jnp.float32,
        )

    def observed(batch_index):
        masked_coefs = obs_coef[batch_index] * owned[batch_index][None, :]
        spread = gather_rows(
            owned[batch_index].astype(jnp.int32),
            obs_cell[batch_index],
            obs_level[batch_index],
            masked_coefs,
            cells,
        )
        return folded(spread)

    def mixing(local_terms, batch_index):
        predicted = summed_everywhere(local_terms)
        weight_obs = localize(
            obs_owner[batch_index],
            obs_cell[batch_index],
            pattern[0, 0, batch_index],
            tile_east,
            tile_north,
            span_east,
            span_north,
            tiles_north,
            span_east * tiles_east,
            span_north * tiles_north,
        )
        return transform(predicted, obs_value[batch_index], obs_error[batch_index], weight_obs)

    first_mix = mixing(observed(0), 0)
    second_terms = product(observed(1), block_diagonal(first_mix, groups))
    second_mix = mixing(second_terms, 1)
    rows = mixed_once(cells, block_diagonal(product(first_mix, second_mix), groups))
    return rows.reshape(span_east, span_north, features)


def solution(mesh):
    placed = (P("gx", "gy", None), P(), P(), P(), P(), P(), P(), P("gx", "gy", None, None))
    return jax.shard_map(
        local, mesh=mesh, in_specs=placed, out_specs=P("gx", "gy", None), check_vma=False
    )
```

```python
import math

import jax
import jax.numpy as jnp
from jax import lax
from jax.experimental import pallas as pl
from jax.experimental.pallas import tpu as pltpu
from jax.sharding import PartitionSpec as P

ENS = 32
LEV = 4
COMP = 3
NSIT = 4


courant = 0.1
diffusion = 0.08
radius_share = 0.25


def gather_kernel(slot_ref, taken_ref, cell_ref, level_ref, coef_ref, field_ref, out_ref, chosen_ref):
    count = cell_ref.shape[0]
    groups, rows, width = out_ref.shape
    lane_level = lax.broadcasted_iota(jnp.int32, (1, width), 1) // ENS
    sublane = lax.broadcasted_iota(jnp.int32, (8, width), 0)
    out_ref[...] = jnp.zeros(out_ref.shape, out_ref.dtype)

    def choose(j, carry):
        chosen_ref[slot_ref[j]] = j
        return carry

    lax.fori_loop(0, count, choose, 0, unroll=8)
    taken = taken_ref[0]

    def body(i, carry):
        j = chosen_ref[i]
        picked = field_ref[pl.ds(cell_ref[j], 1), :]
        value = (
            coef_ref[j] * picked[:, 0:width]
            + coef_ref[count + j] * picked[:, width:2 * width]
            + coef_ref[2 * count + j] * picked[:, 2 * width:3 * width]
        )
        value = jnp.where(lane_level == level_ref[j], value, 0.0)
        row = j // groups
        first = pl.multiple_of((row // 8) * 8, 8)
        tile = out_ref[j % groups, pl.ds(first, 8), :]
        out_ref[j % groups, pl.ds(first, 8), :] = jnp.where(sublane == row % 8, value, tile)
        return carry

    lax.fori_loop(0, taken, body, 0)


def gather_rows(flags, cells, levels, coefs, field):
    slots = jnp.cumsum(flags) - flags
    taken = jnp.sum(flags, keepdims=True)
    count = cells.shape[0]
    width = field.shape[1] // 3
    groups = width // ENS
    smem = pl.BlockSpec(memory_space=pltpu.SMEM)
    vmem = pl.BlockSpec(memory_space=pltpu.VMEM)
    return pl.pallas_call(
        gather_kernel,
        out_shape=jax.ShapeDtypeStruct((groups, count // groups, width), jnp.float32),
        in_specs=[smem, smem, smem, smem, smem, vmem],
        out_specs=vmem,
        scratch_shapes=[pltpu.SMEM((count,), jnp.int32)],
    )(slots, taken, cells, levels, coefs.reshape(-1), field)


def advect_update(c, w, e, s, n, width):
    u = c[:, 0:width]
    v = c[:, width:2 * width]
    pu, mu = jnp.maximum(u, 0.0), jnp.minimum(u, 0.0)
    pv, mv = jnp.maximum(v, 0.0), jnp.minimum(v, 0.0)
    blocks = []
    for b in range(3):
        lanes = slice(b * width, (b + 1) * width)
        cc, ww, ee, ss, nn = c[:, lanes], w[:, lanes], e[:, lanes], s[:, lanes], n[:, lanes]
        flux = pu * (cc - ww) + mu * (ee - cc) + pv * (cc - ss) + mv * (nn - cc)
        blocks.append(cc - courant * flux + diffusion * (ww + ee + (ss + nn) - 4.0 * cc))
    return blocks


def shifted(values, edge, shift):
    count = values.shape[0]
    row = lax.broadcasted_iota(jnp.int32, values.shape, 0)
    fresh = 0 if shift == 1 else count - 1
    return jnp.where(row == fresh, edge, pltpu.roll(values, shift % count, 0))


def two_steps_kernel(
    field_ref, west_ref, east_ref, south0_ref, south1_ref, north0_ref, north1_ref,
    first_col_ref, last_col_ref, corner_ref, out_ref, mid_ref, ring_ref,
):
    nx, ny, feat = field_ref.shape
    width = feat // 3

    def store(ref, index, blocks):
        for b in range(3):
            ref[index, :, b * width:(b + 1) * width] = blocks[b]

    def first_pass(x, carry):
        centre = field_ref[x]
        west = jnp.where(x == 0, west_ref[1], field_ref[jnp.maximum(x - 1, 0)])
        east = jnp.where(x == nx - 1, east_ref[0], field_ref[jnp.minimum(x + 1, nx - 1)])
        south = shifted(centre, south1_ref[pl.ds(x, 1), :], 1)
        north = shifted(centre, north0_ref[pl.ds(x, 1), :], -1)
        store(mid_ref, x, advect_update(centre, west, east, south, north, width))
        return carry

    lax.fori_loop(0, nx, first_pass, 0)
    corner = corner_ref[...]
    centre = west_ref[1]
    ring_w = advect_update(centre, west_ref[0], field_ref[0], shifted(centre, corner[0:1], 1), shifted(centre, corner[1:2], -1), width)
    centre = east_ref[0]
    ring_e = advect_update(centre, field_ref[nx - 1], east_ref[1], shifted(centre, corner[2:3], 1), shifted(centre, corner[3:4], -1), width)
    centre = south1_ref[...]
    ring_s = advect_update(centre, shifted(centre, corner[0:1], 1), shifted(centre, corner[2:3], -1), south0_ref[...], first_col_ref[...], width)
    centre = north0_ref[...]
    ring_n = advect_update(centre, shifted(centre, corner[1:2], 1), shifted(centre, corner[3:4], -1), last_col_ref[...], north1_ref[...], width)
    store(ring_ref, 0, ring_w)
    store(ring_ref, 1, ring_e)
    for b in range(3):
        ring_ref[2, 0:nx, b * width:(b + 1) * width] = ring_s[b]
        ring_ref[3, 0:nx, b * width:(b + 1) * width] = ring_n[b]

    def second_pass(x, carry):
        centre = mid_ref[x]
        west = jnp.where(x == 0, ring_ref[0], mid_ref[jnp.maximum(x - 1, 0)])
        east = jnp.where(x == nx - 1, ring_ref[1], mid_ref[jnp.minimum(x + 1, nx - 1)])
        south = shifted(centre, ring_ref[2, pl.ds(x, 1), :], 1)
        north = shifted(centre, ring_ref[3, pl.ds(x, 1), :], -1)
        store(out_ref, x, advect_update(centre, west, east, south, north, width))
        return carry

    lax.fori_loop(0, nx, second_pass, 0)


def two_steps(field, west, east, south0, south1, north0, north1, first_col, last_col, corner):
    nx, ny, feat = field.shape
    vmem = pl.BlockSpec(memory_space=pltpu.VMEM)
    return pl.pallas_call(
        two_steps_kernel,
        out_shape=jax.ShapeDtypeStruct(field.shape, field.dtype),
        in_specs=[vmem] * 10,
        out_specs=vmem,
        scratch_shapes=[
            pltpu.VMEM(field.shape, jnp.float32),
            pltpu.VMEM((4, max(nx, ny), feat), jnp.float32),
        ],
    )(field, west, east, south0, south1, north0, north1, first_col, last_col, corner)


def advance_twice(field):
    nx, ny, feat = field.shape
    sx, sy = lax.axis_size("gx"), lax.axis_size("gy")
    up_x = [(i, (i + 1) % sx) for i in range(sx)]
    down_x = [(j, i) for i, j in up_x]
    up_y = [(i, (i + 1) % sy) for i in range(sy)]
    down_y = [(j, i) for i, j in up_y]
    west = lax.ppermute(field[nx - 2:], "gx", up_x)
    east = lax.ppermute(field[:2], "gx", down_x)
    last_cols = jnp.concatenate([west[:, ny - 2:], field[:, ny - 2:], east[:, ny - 2:]])
    first_cols = jnp.concatenate([west[:, :2], field[:, :2], east[:, :2]])
    south = lax.ppermute(last_cols, "gy", up_y)
    north = lax.ppermute(first_cols, "gy", down_y)
    corner = jnp.stack([south[1, 1], north[1, 0], south[nx + 2, 1], north[nx + 2, 0]])
    return two_steps(
        field, west, east, south[2:nx + 2, 0], south[2:nx + 2, 1], north[2:nx + 2, 0], north[2:nx + 2, 1],
        field[:, 0], field[:, ny - 1], corner,
    )


def product(left, right):
    return jnp.dot(left, right, precision=lax.Precision.HIGHEST, preferred_element_type=jnp.float32)


def mix_kernel(rows_ref, mix_ref, out_ref):
    width = mix_ref.shape[0]
    for block in range(rows_ref.shape[1] // width):
        lanes = slice(block * width, (block + 1) * width)
        out_ref[:, lanes] = product(rows_ref[:, lanes], mix_ref[...])


def mixed_once(rows, mix):
    count, features = rows.shape
    width = mix.shape[0]
    tile = 512
    return pl.pallas_call(
        mix_kernel,
        out_shape=jax.ShapeDtypeStruct(rows.shape, rows.dtype),
        grid=(count // tile,),
        in_specs=[
            pl.BlockSpec((tile, features), lambda i: (i, 0)),
            pl.BlockSpec((width, width), lambda i: (0, 0)),
        ],
        out_specs=pl.BlockSpec((tile, features), lambda i: (i, 0)),
    )(rows, mix)


def summed_everywhere(rows):
    axes = ("gx", "gy")
    devices = lax.axis_size("gx") * lax.axis_size("gy")
    parts = lax.all_to_all(rows, axes, 0, 0, tiled=True)
    chunk = parts.reshape((devices, rows.shape[0] // devices) + rows.shape[1:]).sum(axis=0)
    copies = jnp.broadcast_to(chunk[None], (devices,) + chunk.shape).reshape(rows.shape)
    return lax.all_to_all(copies, axes, 0, 0, tiled=True)


def localize(
    owners,
    obs_cells,
    block_mask,
    tile_east,
    tile_north,
    span_east,
    span_north,
    tiles_north,
    grid_east,
    grid_north,
):
    place_east = (owners // tiles_north * span_east + obs_cells // span_north).astype(jnp.float32)
    place_north = (owners % tiles_north * span_north + obs_cells % span_north).astype(jnp.float32)
    centre_east = (tile_east * span_east).astype(jnp.float32) + (span_east - 1) / 2.0
    centre_north = (tile_north * span_north).astype(jnp.float32) + (span_north - 1) / 2.0
    gap_east = (
        jnp.remainder(place_east - centre_east + grid_east / 2.0, grid_east) - grid_east / 2.0
    )
    gap_north = (
        jnp.remainder(place_north - centre_north + grid_north / 2.0, grid_north) - grid_north / 2.0
    )
    scale_east = gap_east / (radius_share * grid_east)
    scale_north = gap_north / (radius_share * grid_north)
    weight = jnp.exp(-0.5 * (scale_east * scale_east + scale_north * scale_north))
    blocks = block_mask.shape[0]
    return (weight.reshape(blocks, -1) * block_mask.astype(jnp.float32)[:, None]).reshape(-1)


def transform(predicted, obs_value, obs_error, weight_obs):
    rows, width = predicted.shape
    groups = width // ENS
    members = ENS

    def spread(per_obs):
        return jnp.broadcast_to(per_obs.reshape(rows, groups, 1), (rows, groups, ENS)).reshape(rows, width)

    lane_in = lax.broadcasted_iota(jnp.int32, (width, width), 0) // ENS
    lane_out = lax.broadcasted_iota(jnp.int32, (width, width), 1) // ENS
    averaging = jnp.where(lane_in == lane_out, 1.0 / members, 0.0).astype(jnp.float32)
    centre_obs = product(predicted, averaging)
    error = spread(obs_error)
    deviation = (predicted - centre_obs) / error
    innovation = (spread(obs_value) - centre_obs) / error
    weighted = deviation * spread(weight_obs)
    blocks = product(weighted.T, deviation)
    covariance = sum(blocks[k * ENS:(k + 1) * ENS, k * ENS:(k + 1) * ENS] for k in range(groups))
    projected = jnp.sum(weighted * innovation, axis=0)
    projection = sum(projected[k * ENS:(k + 1) * ENS] for k in range(groups))
    unit_matrix = jnp.eye(members, dtype=jnp.float32)
    system = (members - 1.0) * unit_matrix + covariance
    row_bound = jnp.max(jnp.sum(jnp.abs(system), axis=1))

    def refine(sweep_index, iterates):
        approach, inverse_root = iterates
        middle = 1.5 * unit_matrix - 0.5 * product(inverse_root, approach)
        return (product(approach, middle), product(middle, inverse_root))

    approach, inverse_root = lax.fori_loop(0, NSIT, refine, (system / row_bound, unit_matrix))
    inverse = product(inverse_root, inverse_root) / row_bound
    weights = product(inverse, projection[:, None])[:, 0]
    centring = unit_matrix - 1.0 / members
    shifts = weights[:, None] + math.sqrt(members - 1.0) * inverse_root / jnp.sqrt(row_bound)
    return 1.0 / members + product(centring, shifts)


def block_diagonal(mix, copies):
    return jnp.kron(jnp.eye(copies, dtype=mix.dtype), mix)


def local(state, obs_owner, obs_cell, obs_level, obs_coef, obs_value, obs_error, pattern):
    span_east, span_north, features = state.shape
    tiles_east = lax.axis_size("gx")
    tiles_north = lax.axis_size("gy")
    tile_east = lax.axis_index("gx")
    tile_north = lax.axis_index("gy")
    own_tile = tile_east * tiles_north + tile_north
    field = advance_twice(state)
    cells = field.reshape(span_east * span_north, features)
    width = features // COMP
    groups = width // ENS
    owned = (obs_owner == own_tile).astype(jnp.float32)
    lane_in = lax.broadcasted_iota(jnp.int32, (groups, width, groups * ENS), 0)
    level_lane = lax.broadcasted_iota(jnp.int32, (groups, width, groups * ENS), 1)
    dense_lane = lax.broadcasted_iota(jnp.int32, (groups, width, groups * ENS), 2)
    fold = ((lane_in == dense_lane // ENS) & (level_lane % ENS == dense_lane % ENS)).astype(jnp.float32)

    def folded(spread):
        return jnp.einsum(
            "krl,klo->ro", spread, fold, precision=lax.Precision.HIGHEST,
            preferred_element_type=jnp.float32,
        )

    def observed(batch_index):
        masked_coefs = obs_coef[batch_index] * owned[batch_index][None, :]
        spread = gather_rows(
            owned[batch_index].astype(jnp.int32),
            obs_cell[batch_index],
            obs_level[batch_index],
            masked_coefs,
            cells,
        )
        return folded(spread)

    def mixing(local_terms, batch_index):
        predicted = summed_everywhere(local_terms)
        weight_obs = localize(
            obs_owner[batch_index],
            obs_cell[batch_index],
            pattern[0, 0, batch_index],
            tile_east,
            tile_north,
            span_east,
            span_north,
            tiles_north,
            span_east * tiles_east,
            span_north * tiles_north,
        )
        return transform(predicted, obs_value[batch_index], obs_error[batch_index], weight_obs)

    first_mix = mixing(observed(0), 0)
    second_terms = product(observed(1), block_diagonal(first_mix, groups))
    second_mix = mixing(second_terms, 1)
    rows = mixed_once(cells, block_diagonal(product(first_mix, second_mix), groups))
    return rows.reshape(span_east, span_north, features)


def solution(mesh):
    placed = (P("gx", "gy", None), P(), P(), P(), P(), P(), P(), P("gx", "gy", None, None))
    return jax.shard_map(
        local, mesh=mesh, in_specs=placed, out_specs=P("gx", "gy", None), check_vma=False
    )
```

```python
import math

import jax
import jax.numpy as jnp
from jax import lax
from jax.experimental import pallas as pl
from jax.experimental.pallas import tpu as pltpu
from jax.sharding import PartitionSpec as P

ENS = 32
LEV = 4
COMP = 3
NSIT = 4


courant = 0.1
diffusion = 0.08
radius_share = 0.25


def gather_kernel(flag_ref, cell_ref, level_ref, coef_ref, field_ref, out_ref, chosen_ref):
    count = cell_ref.shape[0]
    rows, width = out_ref.shape
    groups = width // ENS
    lane_group = lax.broadcasted_iota(jnp.int32, (8, width), 1) // ENS
    sublane = lax.broadcasted_iota(jnp.int32, (8, width), 0)
    out_ref[...] = jnp.zeros(out_ref.shape, out_ref.dtype)

    def choose(j, taken):
        chosen_ref[taken] = j
        return taken + flag_ref[j]

    taken = lax.fori_loop(0, count, choose, 0, unroll=8)

    def body(i, carry):
        j = chosen_ref[i]
        picked = field_ref[pl.ds(cell_ref[j], 1), :]
        value = (
            coef_ref[j] * picked[:, 0:width]
            + coef_ref[count + j] * picked[:, width:2 * width]
            + coef_ref[2 * count + j] * picked[:, 2 * width:3 * width]
        )
        group = j % groups
        turned = pltpu.roll(value, ((group - level_ref[j]) % groups) * ENS, 1)
        row = j // groups
        first = pl.multiple_of((row // 8) * 8, 8)
        tile = out_ref[pl.ds(first, 8), :]
        keep = (sublane == row % 8) & (lane_group == group)
        out_ref[pl.ds(first, 8), :] = jnp.where(keep, turned, tile)
        return carry

    lax.fori_loop(0, taken, body, 0)


def gather_rows(flags, cells, levels, coefs, field):
    count = cells.shape[0]
    width = field.shape[1] // 3
    groups = width // ENS
    smem = pl.BlockSpec(memory_space=pltpu.SMEM)
    vmem = pl.BlockSpec(memory_space=pltpu.VMEM)
    return pl.pallas_call(
        gather_kernel,
        out_shape=jax.ShapeDtypeStruct((count // groups, width), jnp.float32),
        in_specs=[smem, smem, smem, smem, vmem],
        out_specs=vmem,
        scratch_shapes=[pltpu.SMEM((count,), jnp.int32)],
    )(flags, cells, levels, coefs.reshape(-1), field)


def advect_update(c, w, e, s, n, width):
    u = c[:, 0:width]
    v = c[:, width:2 * width]
    pu, mu = jnp.maximum(u, 0.0), jnp.minimum(u, 0.0)
    pv, mv = jnp.maximum(v, 0.0), jnp.minimum(v, 0.0)
    blocks = []
    for b in range(3):
        lanes = slice(b * width, (b + 1) * width)
        cc, ww, ee, ss, nn = c[:, lanes], w[:, lanes], e[:, lanes], s[:, lanes], n[:, lanes]
        flux = pu * (cc - ww) + mu * (ee - cc) + pv * (cc - ss) + mv * (nn - cc)
        blocks.append(cc - courant * flux + diffusion * (ww + ee + (ss + nn) - 4.0 * cc))
    return blocks


def shifted(values, edge, shift):
    count = values.shape[0]
    row = lax.broadcasted_iota(jnp.int32, values.shape, 0)
    fresh = 0 if shift == 1 else count - 1
    return jnp.where(row == fresh, edge, pltpu.roll(values, shift % count, 0))


def two_steps_kernel(
    field_ref, west_ref, east_ref, south0_ref, south1_ref, north0_ref, north1_ref,
    first_col_ref, last_col_ref, corner_ref, out_ref, mid_ref, ring_ref,
):
    nx, ny, feat = field_ref.shape
    width = feat // 3

    def store(ref, index, blocks):
        for b in range(3):
            ref[index, :, b * width:(b + 1) * width] = blocks[b]

    def first_pass(x, carry):
        centre = field_ref[x]
        west = jnp.where(x == 0, west_ref[1], field_ref[jnp.maximum(x - 1, 0)])
        east = jnp.where(x == nx - 1, east_ref[0], field_ref[jnp.minimum(x + 1, nx - 1)])
        south = shifted(centre, south1_ref[pl.ds(x, 1), :], 1)
        north = shifted(centre, north0_ref[pl.ds(x, 1), :], -1)
        store(mid_ref, x, advect_update(centre, west, east, south, north, width))
        return carry

    lax.fori_loop(0, nx, first_pass, 0)
    corner = corner_ref[...]
    centre = west_ref[1]
    ring_w = advect_update(centre, west_ref[0], field_ref[0], shifted(centre, corner[0:1], 1), shifted(centre, corner[1:2], -1), width)
    centre = east_ref[0]
    ring_e = advect_update(centre, field_ref[nx - 1], east_ref[1], shifted(centre, corner[2:3], 1), shifted(centre, corner[3:4], -1), width)
    centre = south1_ref[...]
    ring_s = advect_update(centre, shifted(centre, corner[0:1], 1), shifted(centre, corner[2:3], -1), south0_ref[...], first_col_ref[...], width)
    centre = north0_ref[...]
    ring_n = advect_update(centre, shifted(centre, corner[1:2], 1), shifted(centre, corner[3:4], -1), last_col_ref[...], north1_ref[...], width)
    store(ring_ref, 0, ring_w)
    store(ring_ref, 1, ring_e)
    for b in range(3):
        ring_ref[2, 0:nx, b * width:(b + 1) * width] = ring_s[b]
        ring_ref[3, 0:nx, b * width:(b + 1) * width] = ring_n[b]

    def second_pass(x, carry):
        centre = mid_ref[x]
        west = jnp.where(x == 0, ring_ref[0], mid_ref[jnp.maximum(x - 1, 0)])
        east = jnp.where(x == nx - 1, ring_ref[1], mid_ref[jnp.minimum(x + 1, nx - 1)])
        south = shifted(centre, ring_ref[2, pl.ds(x, 1), :], 1)
        north = shifted(centre, ring_ref[3, pl.ds(x, 1), :], -1)
        store(out_ref, x, advect_update(centre, west, east, south, north, width))
        return carry

    lax.fori_loop(0, nx, second_pass, 0)


def two_steps(field, west, east, south0, south1, north0, north1, first_col, last_col, corner):
    nx, ny, feat = field.shape
    vmem = pl.BlockSpec(memory_space=pltpu.VMEM)
    return pl.pallas_call(
        two_steps_kernel,
        out_shape=jax.ShapeDtypeStruct(field.shape, field.dtype),
        in_specs=[vmem] * 10,
        out_specs=vmem,
        scratch_shapes=[
            pltpu.VMEM(field.shape, jnp.float32),
            pltpu.VMEM((4, max(nx, ny), feat), jnp.float32),
        ],
    )(field, west, east, south0, south1, north0, north1, first_col, last_col, corner)


def advance_twice(field):
    nx, ny, feat = field.shape
    sx, sy = lax.axis_size("gx"), lax.axis_size("gy")
    up_x = [(i, (i + 1) % sx) for i in range(sx)]
    down_x = [(j, i) for i, j in up_x]
    up_y = [(i, (i + 1) % sy) for i in range(sy)]
    down_y = [(j, i) for i, j in up_y]
    west = lax.ppermute(field[nx - 2:], "gx", up_x)
    east = lax.ppermute(field[:2], "gx", down_x)
    last_cols = jnp.concatenate([west[:, ny - 2:], field[:, ny - 2:], east[:, ny - 2:]])
    first_cols = jnp.concatenate([west[:, :2], field[:, :2], east[:, :2]])
    south = lax.ppermute(last_cols, "gy", up_y)
    north = lax.ppermute(first_cols, "gy", down_y)
    corner = jnp.stack([south[1, 1], north[1, 0], south[nx + 2, 1], north[nx + 2, 0]])
    return two_steps(
        field, west, east, south[2:nx + 2, 0], south[2:nx + 2, 1], north[2:nx + 2, 0], north[2:nx + 2, 1],
        field[:, 0], field[:, ny - 1], corner,
    )


def product(left, right):
    return jnp.dot(left, right, precision=lax.Precision.HIGHEST, preferred_element_type=jnp.float32)


def mix_kernel(rows_ref, mix_ref, out_ref):
    width = mix_ref.shape[0]
    for block in range(rows_ref.shape[1] // width):
        lanes = slice(block * width, (block + 1) * width)
        out_ref[:, lanes] = product(rows_ref[:, lanes], mix_ref[...])


def mixed_once(rows, mix):
    count, features = rows.shape
    width = mix.shape[0]
    tile = 512
    return pl.pallas_call(
        mix_kernel,
        out_shape=jax.ShapeDtypeStruct(rows.shape, rows.dtype),
        grid=(count // tile,),
        in_specs=[
            pl.BlockSpec((tile, features), lambda i: (i, 0)),
            pl.BlockSpec((width, width), lambda i: (0, 0)),
        ],
        out_specs=pl.BlockSpec((tile, features), lambda i: (i, 0)),
    )(rows, mix)


def summed_everywhere(rows):
    axes = ("gx", "gy")
    devices = lax.axis_size("gx") * lax.axis_size("gy")
    parts = lax.all_to_all(rows, axes, 0, 0, tiled=True)
    chunk = parts.reshape((devices, rows.shape[0] // devices) + rows.shape[1:]).sum(axis=0)
    copies = jnp.broadcast_to(chunk[None], (devices,) + chunk.shape).reshape(rows.shape)
    return lax.all_to_all(copies, axes, 0, 0, tiled=True)


def localize(
    owners,
    obs_cells,
    block_mask,
    tile_east,
    tile_north,
    span_east,
    span_north,
    tiles_north,
    grid_east,
    grid_north,
):
    place_east = (owners // tiles_north * span_east + obs_cells // span_north).astype(jnp.float32)
    place_north = (owners % tiles_north * span_north + obs_cells % span_north).astype(jnp.float32)
    centre_east = (tile_east * span_east).astype(jnp.float32) + (span_east - 1) / 2.0
    centre_north = (tile_north * span_north).astype(jnp.float32) + (span_north - 1) / 2.0
    gap_east = (
        jnp.remainder(place_east - centre_east + grid_east / 2.0, grid_east) - grid_east / 2.0
    )
    gap_north = (
        jnp.remainder(place_north - centre_north + grid_north / 2.0, grid_north) - grid_north / 2.0
    )
    scale_east = gap_east / (radius_share * grid_east)
    scale_north = gap_north / (radius_share * grid_north)
    weight = jnp.exp(-0.5 * (scale_east * scale_east + scale_north * scale_north))
    blocks = block_mask.shape[0]
    return (weight.reshape(blocks, -1) * block_mask.astype(jnp.float32)[:, None]).reshape(-1)


def transform(predicted, obs_value, obs_error, weight_obs):
    rows, width = predicted.shape
    groups = width // ENS
    members = ENS

    def spread(per_obs):
        return jnp.broadcast_to(per_obs.reshape(rows, groups, 1), (rows, groups, ENS)).reshape(rows, width)

    lane_in = lax.broadcasted_iota(jnp.int32, (width, width), 0) // ENS
    lane_out = lax.broadcasted_iota(jnp.int32, (width, width), 1) // ENS
    averaging = jnp.where(lane_in == lane_out, 1.0 / members, 0.0).astype(jnp.float32)
    centre_obs = product(predicted, averaging)
    error = spread(obs_error)
    deviation = (predicted - centre_obs) / error
    innovation = (spread(obs_value) - centre_obs) / error
    weighted = deviation * spread(weight_obs)
    blocks = product(weighted.T, deviation)
    covariance = sum(blocks[k * ENS:(k + 1) * ENS, k * ENS:(k + 1) * ENS] for k in range(groups))
    projected = jnp.sum(weighted * innovation, axis=0)
    projection = sum(projected[k * ENS:(k + 1) * ENS] for k in range(groups))
    unit_matrix = jnp.eye(members, dtype=jnp.float32)
    system = (members - 1.0) * unit_matrix + covariance
    row_bound = jnp.max(jnp.sum(jnp.abs(system), axis=1))

    def refine(sweep_index, iterates):
        approach, inverse_root = iterates
        middle = 1.5 * unit_matrix - 0.5 * product(inverse_root, approach)
        return (product(approach, middle), product(middle, inverse_root))

    approach, inverse_root = lax.fori_loop(0, NSIT, refine, (system / row_bound, unit_matrix))
    inverse = product(inverse_root, inverse_root) / row_bound
    weights = product(inverse, projection[:, None])[:, 0]
    centring = unit_matrix - 1.0 / members
    shifts = weights[:, None] + math.sqrt(members - 1.0) * inverse_root / jnp.sqrt(row_bound)
    return 1.0 / members + product(centring, shifts)


def block_diagonal(mix, copies):
    return jnp.kron(jnp.eye(copies, dtype=mix.dtype), mix)


def local(state, obs_owner, obs_cell, obs_level, obs_coef, obs_value, obs_error, pattern):
    span_east, span_north, features = state.shape
    tiles_east = lax.axis_size("gx")
    tiles_north = lax.axis_size("gy")
    tile_east = lax.axis_index("gx")
    tile_north = lax.axis_index("gy")
    own_tile = tile_east * tiles_north + tile_north
    field = advance_twice(state)
    cells = field.reshape(span_east * span_north, features)
    width = features // COMP
    groups = width // ENS
    owned = (obs_owner == own_tile).astype(jnp.float32)
    def observed(batch_index):
        masked_coefs = obs_coef[batch_index] * owned[batch_index][None, :]
        spread = gather_rows(
            owned[batch_index].astype(jnp.int32),
            obs_cell[batch_index],
            obs_level[batch_index],
            masked_coefs,
            cells,
        )
        return spread

    def mixing(local_terms, batch_index):
        predicted = summed_everywhere(local_terms)
        weight_obs = localize(
            obs_owner[batch_index],
            obs_cell[batch_index],
            pattern[0, 0, batch_index],
            tile_east,
            tile_north,
            span_east,
            span_north,
            tiles_north,
            span_east * tiles_east,
            span_north * tiles_north,
        )
        return transform(predicted, obs_value[batch_index], obs_error[batch_index], weight_obs)

    first_mix = mixing(observed(0), 0)
    second_terms = product(observed(1), block_diagonal(first_mix, groups))
    second_mix = mixing(second_terms, 1)
    rows = mixed_once(cells, block_diagonal(product(first_mix, second_mix), groups))
    return rows.reshape(span_east, span_north, features)


def solution(mesh):
    placed = (P("gx", "gy", None), P(), P(), P(), P(), P(), P(), P("gx", "gy", None, None))
    return jax.shard_map(
        local, mesh=mesh, in_specs=placed, out_specs=P("gx", "gy", None), check_vma=False
    )
```

```python
import math

import jax
import jax.numpy as jnp
from jax import lax
from jax.experimental import pallas as pl
from jax.experimental.pallas import tpu as pltpu
from jax.sharding import PartitionSpec as P

ENS = 32
LEV = 4
COMP = 3
NSIT = 4


courant = 0.1
diffusion = 0.08
radius_share = 0.25


def gather_kernel(busy_ref, cell_ref, level_ref, coef_ref, field_ref, out_ref):
    count = cell_ref.shape[0]
    width = field_ref.shape[1] // 3
    lane_level = lax.broadcasted_iota(jnp.int32, (1, width), 1) // ENS
    sublane = lax.broadcasted_iota(jnp.int32, (8, width), 0)
    groups = width // ENS
    out_ref[...] = jnp.zeros(out_ref.shape, out_ref.dtype)

    def body(block, carry):
        @pl.when(busy_ref[block] > 0)
        def _():
            gathered = [jnp.zeros((8, width), jnp.float32) for k in range(groups)]
            for i in range(8):
                for k in range(groups):
                    j = (block * 8 + i) * groups + k
                    picked = field_ref[pl.ds(cell_ref[j], 1), :]
                    value = (
                        coef_ref[j] * picked[:, 0:width]
                        + coef_ref[count + j] * picked[:, width:2 * width]
                        + coef_ref[2 * count + j] * picked[:, 2 * width:3 * width]
                    )
                    value = jnp.where(lane_level == level_ref[j], value, 0.0)
                    gathered[k] = jnp.where(sublane == i, value, gathered[k])
            first = pl.multiple_of(block * 8, 8)
            for k in range(groups):
                out_ref[pl.ds(first, 8), k * width:(k + 1) * width] = gathered[k]

        return carry

    lax.fori_loop(0, count // (8 * groups), body, 0)


def gather_rows(flags, cells, levels, coefs, field):
    count = cells.shape[0]
    width = field.shape[1] // 3
    groups = width // ENS
    busy = jnp.max(flags.reshape(-1, 8 * groups), axis=1)
    smem = pl.BlockSpec(memory_space=pltpu.SMEM)
    vmem = pl.BlockSpec(memory_space=pltpu.VMEM)
    return pl.pallas_call(
        gather_kernel,
        out_shape=jax.ShapeDtypeStruct((count // groups, groups * width), jnp.float32),
        in_specs=[smem, smem, smem, smem, vmem],
        out_specs=vmem,
    )(busy, cells, levels, coefs.reshape(-1), field)


def advect_update(c, w, e, s, n, width):
    u = c[:, 0:width]
    v = c[:, width:2 * width]
    pu, mu = jnp.maximum(u, 0.0), jnp.minimum(u, 0.0)
    pv, mv = jnp.maximum(v, 0.0), jnp.minimum(v, 0.0)
    blocks = []
    for b in range(3):
        lanes = slice(b * width, (b + 1) * width)
        cc, ww, ee, ss, nn = c[:, lanes], w[:, lanes], e[:, lanes], s[:, lanes], n[:, lanes]
        flux = pu * (cc - ww) + mu * (ee - cc) + pv * (cc - ss) + mv * (nn - cc)
        blocks.append(cc - courant * flux + diffusion * (ww + ee + (ss + nn) - 4.0 * cc))
    return blocks


def shifted(values, edge, shift):
    count = values.shape[0]
    row = lax.broadcasted_iota(jnp.int32, values.shape, 0)
    fresh = 0 if shift == 1 else count - 1
    return jnp.where(row == fresh, edge, pltpu.roll(values, shift % count, 0))


def two_steps_kernel(
    field_ref, west_ref, east_ref, south0_ref, south1_ref, north0_ref, north1_ref,
    first_col_ref, last_col_ref, corner_ref, out_ref, mid_ref, ring_ref,
):
    nx, ny, feat = field_ref.shape
    width = feat // 3

    def store(ref, index, blocks):
        for b in range(3):
            ref[index, :, b * width:(b + 1) * width] = blocks[b]

    def first_pass(x, carry):
        centre = field_ref[x]
        west = jnp.where(x == 0, west_ref[1], field_ref[jnp.maximum(x - 1, 0)])
        east = jnp.where(x == nx - 1, east_ref[0], field_ref[jnp.minimum(x + 1, nx - 1)])
        south = shifted(centre, south1_ref[pl.ds(x, 1), :], 1)
        north = shifted(centre, north0_ref[pl.ds(x, 1), :], -1)
        store(mid_ref, x, advect_update(centre, west, east, south, north, width))
        return carry

    lax.fori_loop(0, nx, first_pass, 0)
    corner = corner_ref[...]
    centre = west_ref[1]
    ring_w = advect_update(centre, west_ref[0], field_ref[0], shifted(centre, corner[0:1], 1), shifted(centre, corner[1:2], -1), width)
    centre = east_ref[0]
    ring_e = advect_update(centre, field_ref[nx - 1], east_ref[1], shifted(centre, corner[2:3], 1), shifted(centre, corner[3:4], -1), width)
    centre = south1_ref[...]
    ring_s = advect_update(centre, shifted(centre, corner[0:1], 1), shifted(centre, corner[2:3], -1), south0_ref[...], first_col_ref[...], width)
    centre = north0_ref[...]
    ring_n = advect_update(centre, shifted(centre, corner[1:2], 1), shifted(centre, corner[3:4], -1), last_col_ref[...], north1_ref[...], width)
    store(ring_ref, 0, ring_w)
    store(ring_ref, 1, ring_e)
    for b in range(3):
        ring_ref[2, 0:nx, b * width:(b + 1) * width] = ring_s[b]
        ring_ref[3, 0:nx, b * width:(b + 1) * width] = ring_n[b]

    def second_pass(x, carry):
        centre = mid_ref[x]
        west = jnp.where(x == 0, ring_ref[0], mid_ref[jnp.maximum(x - 1, 0)])
        east = jnp.where(x == nx - 1, ring_ref[1], mid_ref[jnp.minimum(x + 1, nx - 1)])
        south = shifted(centre, ring_ref[2, pl.ds(x, 1), :], 1)
        north = shifted(centre, ring_ref[3, pl.ds(x, 1), :], -1)
        store(out_ref, x, advect_update(centre, west, east, south, north, width))
        return carry

    lax.fori_loop(0, nx, second_pass, 0)


def two_steps(field, west, east, south0, south1, north0, north1, first_col, last_col, corner):
    nx, ny, feat = field.shape
    vmem = pl.BlockSpec(memory_space=pltpu.VMEM)
    return pl.pallas_call(
        two_steps_kernel,
        out_shape=jax.ShapeDtypeStruct(field.shape, field.dtype),
        in_specs=[vmem] * 10,
        out_specs=vmem,
        scratch_shapes=[
            pltpu.VMEM(field.shape, jnp.float32),
            pltpu.VMEM((4, max(nx, ny), feat), jnp.float32),
        ],
    )(field, west, east, south0, south1, north0, north1, first_col, last_col, corner)


def advance_twice(field):
    nx, ny, feat = field.shape
    sx, sy = lax.axis_size("gx"), lax.axis_size("gy")
    up_x = [(i, (i + 1) % sx) for i in range(sx)]
    down_x = [(j, i) for i, j in up_x]
    up_y = [(i, (i + 1) % sy) for i in range(sy)]
    down_y = [(j, i) for i, j in up_y]
    west = lax.ppermute(field[nx - 2:], "gx", up_x)
    east = lax.ppermute(field[:2], "gx", down_x)
    last_cols = jnp.concatenate([west[:, ny - 2:], field[:, ny - 2:], east[:, ny - 2:]])
    first_cols = jnp.concatenate([west[:, :2], field[:, :2], east[:, :2]])
    south = lax.ppermute(last_cols, "gy", up_y)
    north = lax.ppermute(first_cols, "gy", down_y)
    corner = jnp.stack([south[1, 1], north[1, 0], south[nx + 2, 1], north[nx + 2, 0]])
    return two_steps(
        field, west, east, south[2:nx + 2, 0], south[2:nx + 2, 1], north[2:nx + 2, 0], north[2:nx + 2, 1],
        field[:, 0], field[:, ny - 1], corner,
    )


def product(left, right):
    return jnp.dot(left, right, precision=lax.Precision.HIGHEST, preferred_element_type=jnp.float32)


def mix_kernel(rows_ref, mix_ref, out_ref):
    width = mix_ref.shape[0]
    for block in range(rows_ref.shape[1] // width):
        lanes = slice(block * width, (block + 1) * width)
        out_ref[:, lanes] = product(rows_ref[:, lanes], mix_ref[...])


def mixed_once(rows, mix):
    count, features = rows.shape
    width = mix.shape[0]
    tile = 512
    return pl.pallas_call(
        mix_kernel,
        out_shape=jax.ShapeDtypeStruct(rows.shape, rows.dtype),
        grid=(count // tile,),
        in_specs=[
            pl.BlockSpec((tile, features), lambda i: (i, 0)),
            pl.BlockSpec((width, width), lambda i: (0, 0)),
        ],
        out_specs=pl.BlockSpec((tile, features), lambda i: (i, 0)),
    )(rows, mix)


def summed_everywhere(rows):
    axes = ("gx", "gy")
    devices = lax.axis_size("gx") * lax.axis_size("gy")
    parts = lax.all_to_all(rows, axes, 0, 0, tiled=True)
    chunk = parts.reshape((devices, rows.shape[0] // devices) + rows.shape[1:]).sum(axis=0)
    copies = jnp.broadcast_to(chunk[None], (devices,) + chunk.shape).reshape(rows.shape)
    return lax.all_to_all(copies, axes, 0, 0, tiled=True)


def localize(
    owners,
    obs_cells,
    block_mask,
    tile_east,
    tile_north,
    span_east,
    span_north,
    tiles_north,
    grid_east,
    grid_north,
):
    place_east = (owners // tiles_north * span_east + obs_cells // span_north).astype(jnp.float32)
    place_north = (owners % tiles_north * span_north + obs_cells % span_north).astype(jnp.float32)
    centre_east = (tile_east * span_east).astype(jnp.float32) + (span_east - 1) / 2.0
    centre_north = (tile_north * span_north).astype(jnp.float32) + (span_north - 1) / 2.0
    gap_east = (
        jnp.remainder(place_east - centre_east + grid_east / 2.0, grid_east) - grid_east / 2.0
    )
    gap_north = (
        jnp.remainder(place_north - centre_north + grid_north / 2.0, grid_north) - grid_north / 2.0
    )
    scale_east = gap_east / (radius_share * grid_east)
    scale_north = gap_north / (radius_share * grid_north)
    weight = jnp.exp(-0.5 * (scale_east * scale_east + scale_north * scale_north))
    blocks = block_mask.shape[0]
    return (weight.reshape(blocks, -1) * block_mask.astype(jnp.float32)[:, None]).reshape(-1)


def transform(predicted, obs_value, obs_error, weight_obs):
    rows, width = predicted.shape
    groups = width // ENS
    members = ENS

    def spread(per_obs):
        return jnp.broadcast_to(per_obs.reshape(rows, groups, 1), (rows, groups, ENS)).reshape(rows, width)

    lane_in = lax.broadcasted_iota(jnp.int32, (width, width), 0) // ENS
    lane_out = lax.broadcasted_iota(jnp.int32, (width, width), 1) // ENS
    averaging = jnp.where(lane_in == lane_out, 1.0 / members, 0.0).astype(jnp.float32)
    centre_obs = product(predicted, averaging)
    error = spread(obs_error)
    deviation = (predicted - centre_obs) / error
    innovation = (spread(obs_value) - centre_obs) / error
    weighted = deviation * spread(weight_obs)
    blocks = product(weighted.T, deviation)
    covariance = sum(blocks[k * ENS:(k + 1) * ENS, k * ENS:(k + 1) * ENS] for k in range(groups))
    projected = jnp.sum(weighted * innovation, axis=0)
    projection = sum(projected[k * ENS:(k + 1) * ENS] for k in range(groups))
    unit_matrix = jnp.eye(members, dtype=jnp.float32)
    system = (members - 1.0) * unit_matrix + covariance
    row_bound = jnp.max(jnp.sum(jnp.abs(system), axis=1))

    def refine(sweep_index, iterates):
        approach, inverse_root = iterates
        middle = 1.5 * unit_matrix - 0.5 * product(inverse_root, approach)
        return (product(approach, middle), product(middle, inverse_root))

    approach, inverse_root = lax.fori_loop(0, NSIT, refine, (system / row_bound, unit_matrix))
    inverse = product(inverse_root, inverse_root) / row_bound
    weights = product(inverse, projection[:, None])[:, 0]
    centring = unit_matrix - 1.0 / members
    shifts = weights[:, None] + math.sqrt(members - 1.0) * inverse_root / jnp.sqrt(row_bound)
    return 1.0 / members + product(centring, shifts)


def block_diagonal(mix, copies):
    return jnp.kron(jnp.eye(copies, dtype=mix.dtype), mix)


def local(state, obs_owner, obs_cell, obs_level, obs_coef, obs_value, obs_error, pattern):
    span_east, span_north, features = state.shape
    tiles_east = lax.axis_size("gx")
    tiles_north = lax.axis_size("gy")
    tile_east = lax.axis_index("gx")
    tile_north = lax.axis_index("gy")
    own_tile = tile_east * tiles_north + tile_north
    field = advance_twice(state)
    cells = field.reshape(span_east * span_north, features)
    width = features // COMP
    groups = width // ENS
    owned = (obs_owner == own_tile).astype(jnp.float32)
    spread_lane = lax.broadcasted_iota(jnp.int32, (groups * width, groups * ENS), 0)
    dense_lane = lax.broadcasted_iota(jnp.int32, (groups * width, groups * ENS), 1)
    fold = (
        (spread_lane // width == dense_lane // ENS) & (spread_lane % ENS == dense_lane % ENS)
    ).astype(jnp.float32)

    def observed(batch_index):
        masked_coefs = obs_coef[batch_index] * owned[batch_index][None, :]
        spread = gather_rows(
            owned[batch_index].astype(jnp.int32),
            obs_cell[batch_index],
            obs_level[batch_index],
            masked_coefs,
            cells,
        )
        return product(spread, fold)

    def mixing(local_terms, batch_index):
        predicted = summed_everywhere(local_terms)
        weight_obs = localize(
            obs_owner[batch_index],
            obs_cell[batch_index],
            pattern[0, 0, batch_index],
            tile_east,
            tile_north,
            span_east,
            span_north,
            tiles_north,
            span_east * tiles_east,
            span_north * tiles_north,
        )
        return transform(predicted, obs_value[batch_index], obs_error[batch_index], weight_obs)

    first_mix = mixing(observed(0), 0)
    second_terms = product(observed(1), block_diagonal(first_mix, groups))
    second_mix = mixing(second_terms, 1)
    rows = mixed_once(cells, block_diagonal(product(first_mix, second_mix), groups))
    return rows.reshape(span_east, span_north, features)


def solution(mesh):
    placed = (P("gx", "gy", None), P(), P(), P(), P(), P(), P(), P("gx", "gy", None, None))
    return jax.shard_map(
        local, mesh=mesh, in_specs=placed, out_specs=P("gx", "gy", None), check_vma=False
    )
```

```python
import math

import jax
import jax.numpy as jnp
from jax import lax
from jax.experimental import pallas as pl
from jax.experimental.pallas import tpu as pltpu
from jax.sharding import PartitionSpec as P

ENS = 32
LEV = 4
COMP = 3
NSIT = 4


courant = 0.1
diffusion = 0.08
radius_share = 0.25


def gather_kernel(busy_ref, row_busy_ref, cell_ref, level_ref, coef_ref, field_ref, out_ref, stage_ref):
    count = cell_ref.shape[0]
    width = field_ref.shape[1] // 3
    lane_level = lax.broadcasted_iota(jnp.int32, (1, width), 1) // ENS
    groups = width // ENS
    out_ref[...] = jnp.zeros(out_ref.shape, out_ref.dtype)

    def body(block, carry):
        @pl.when(busy_ref[block] > 0)
        def _():
            for i in range(8):
                row = block * 8 + i

                @pl.when(row_busy_ref[row] > 0)
                def _():
                    for k in range(groups):
                        j = row * groups + k
                        picked = field_ref[pl.ds(cell_ref[j], 1), :]
                        value = (
                            coef_ref[j] * picked[:, 0:width]
                            + coef_ref[count + j] * picked[:, width:2 * width]
                            + coef_ref[2 * count + j] * picked[:, 2 * width:3 * width]
                        )
                        stage_ref[i:i + 1, k * width:(k + 1) * width] = jnp.where(
                            lane_level == level_ref[j], value, 0.0
                        )

                @pl.when(row_busy_ref[row] == 0)
                def _():
                    stage_ref[i:i + 1, :] = jnp.zeros((1, groups * width), jnp.float32)

            out_ref[pl.ds(pl.multiple_of(block * 8, 8), 8), :] = stage_ref[...]

        return carry

    lax.fori_loop(0, count // (8 * groups), body, 0)


def gather_rows(flags, cells, levels, coefs, field):
    count = cells.shape[0]
    width = field.shape[1] // 3
    groups = width // ENS
    row_busy = jnp.max(flags.reshape(-1, groups), axis=1)
    busy = jnp.max(row_busy.reshape(-1, 8), axis=1)
    smem = pl.BlockSpec(memory_space=pltpu.SMEM)
    vmem = pl.BlockSpec(memory_space=pltpu.VMEM)
    return pl.pallas_call(
        gather_kernel,
        out_shape=jax.ShapeDtypeStruct((count // groups, groups * width), jnp.float32),
        in_specs=[smem, smem, smem, smem, smem, vmem],
        out_specs=vmem,
        scratch_shapes=[pltpu.VMEM((8, groups * width), jnp.float32)],
    )(busy, row_busy, cells, levels, coefs.reshape(-1), field)


def advect_update(c, w, e, s, n, width):
    u = c[:, 0:width]
    v = c[:, width:2 * width]
    pu, mu = jnp.maximum(u, 0.0), jnp.minimum(u, 0.0)
    pv, mv = jnp.maximum(v, 0.0), jnp.minimum(v, 0.0)
    blocks = []
    for b in range(3):
        lanes = slice(b * width, (b + 1) * width)
        cc, ww, ee, ss, nn = c[:, lanes], w[:, lanes], e[:, lanes], s[:, lanes], n[:, lanes]
        flux = pu * (cc - ww) + mu * (ee - cc) + pv * (cc - ss) + mv * (nn - cc)
        blocks.append(cc - courant * flux + diffusion * (ww + ee + (ss + nn) - 4.0 * cc))
    return blocks


def shifted(values, edge, shift):
    count = values.shape[0]
    row = lax.broadcasted_iota(jnp.int32, values.shape, 0)
    fresh = 0 if shift == 1 else count - 1
    return jnp.where(row == fresh, edge, pltpu.roll(values, shift % count, 0))


def two_steps_kernel(
    field_ref, west_ref, east_ref, south0_ref, south1_ref, north0_ref, north1_ref,
    first_col_ref, last_col_ref, corner_ref, out_ref, mid_ref, ring_ref,
):
    nx, ny, feat = field_ref.shape
    width = feat // 3

    def store(ref, index, blocks):
        for b in range(3):
            ref[index, :, b * width:(b + 1) * width] = blocks[b]

    def first_pass(x, carry):
        centre = field_ref[x]
        west = jnp.where(x == 0, west_ref[1], field_ref[jnp.maximum(x - 1, 0)])
        east = jnp.where(x == nx - 1, east_ref[0], field_ref[jnp.minimum(x + 1, nx - 1)])
        south = shifted(centre, south1_ref[pl.ds(x, 1), :], 1)
        north = shifted(centre, north0_ref[pl.ds(x, 1), :], -1)
        store(mid_ref, x, advect_update(centre, west, east, south, north, width))
        return carry

    lax.fori_loop(0, nx, first_pass, 0)
    corner = corner_ref[...]
    centre = west_ref[1]
    ring_w = advect_update(centre, west_ref[0], field_ref[0], shifted(centre, corner[0:1], 1), shifted(centre, corner[1:2], -1), width)
    centre = east_ref[0]
    ring_e = advect_update(centre, field_ref[nx - 1], east_ref[1], shifted(centre, corner[2:3], 1), shifted(centre, corner[3:4], -1), width)
    centre = south1_ref[...]
    ring_s = advect_update(centre, shifted(centre, corner[0:1], 1), shifted(centre, corner[2:3], -1), south0_ref[...], first_col_ref[...], width)
    centre = north0_ref[...]
    ring_n = advect_update(centre, shifted(centre, corner[1:2], 1), shifted(centre, corner[3:4], -1), last_col_ref[...], north1_ref[...], width)
    store(ring_ref, 0, ring_w)
    store(ring_ref, 1, ring_e)
    for b in range(3):
        ring_ref[2, 0:nx, b * width:(b + 1) * width] = ring_s[b]
        ring_ref[3, 0:nx, b * width:(b + 1) * width] = ring_n[b]

    def second_pass(x, carry):
        centre = mid_ref[x]
        west = jnp.where(x == 0, ring_ref[0], mid_ref[jnp.maximum(x - 1, 0)])
        east = jnp.where(x == nx - 1, ring_ref[1], mid_ref[jnp.minimum(x + 1, nx - 1)])
        south = shifted(centre, ring_ref[2, pl.ds(x, 1), :], 1)
        north = shifted(centre, ring_ref[3, pl.ds(x, 1), :], -1)
        store(out_ref, x, advect_update(centre, west, east, south, north, width))
        return carry

    lax.fori_loop(0, nx, second_pass, 0)


def two_steps(field, west, east, south0, south1, north0, north1, first_col, last_col, corner):
    nx, ny, feat = field.shape
    vmem = pl.BlockSpec(memory_space=pltpu.VMEM)
    return pl.pallas_call(
        two_steps_kernel,
        out_shape=jax.ShapeDtypeStruct(field.shape, field.dtype),
        in_specs=[vmem] * 10,
        out_specs=vmem,
        scratch_shapes=[
            pltpu.VMEM(field.shape, jnp.float32),
            pltpu.VMEM((4, max(nx, ny), feat), jnp.float32),
        ],
    )(field, west, east, south0, south1, north0, north1, first_col, last_col, corner)


def advance_twice(field):
    nx, ny, feat = field.shape
    sx, sy = lax.axis_size("gx"), lax.axis_size("gy")
    up_x = [(i, (i + 1) % sx) for i in range(sx)]
    down_x = [(j, i) for i, j in up_x]
    up_y = [(i, (i + 1) % sy) for i in range(sy)]
    down_y = [(j, i) for i, j in up_y]
    west = lax.ppermute(field[nx - 2:], "gx", up_x)
    east = lax.ppermute(field[:2], "gx", down_x)
    last_cols = jnp.concatenate([west[:, ny - 2:], field[:, ny - 2:], east[:, ny - 2:]])
    first_cols = jnp.concatenate([west[:, :2], field[:, :2], east[:, :2]])
    south = lax.ppermute(last_cols, "gy", up_y)
    north = lax.ppermute(first_cols, "gy", down_y)
    corner = jnp.stack([south[1, 1], north[1, 0], south[nx + 2, 1], north[nx + 2, 0]])
    return two_steps(
        field, west, east, south[2:nx + 2, 0], south[2:nx + 2, 1], north[2:nx + 2, 0], north[2:nx + 2, 1],
        field[:, 0], field[:, ny - 1], corner,
    )


def product(left, right):
    return jnp.dot(left, right, precision=lax.Precision.HIGHEST, preferred_element_type=jnp.float32)


def mix_kernel(rows_ref, mix_ref, out_ref):
    width = mix_ref.shape[0]
    for block in range(rows_ref.shape[1] // width):
        lanes = slice(block * width, (block + 1) * width)
        out_ref[:, lanes] = product(rows_ref[:, lanes], mix_ref[...])


def mixed_once(rows, mix):
    count, features = rows.shape
    width = mix.shape[0]
    tile = 512
    return pl.pallas_call(
        mix_kernel,
        out_shape=jax.ShapeDtypeStruct(rows.shape, rows.dtype),
        grid=(count // tile,),
        in_specs=[
            pl.BlockSpec((tile, features), lambda i: (i, 0)),
            pl.BlockSpec((width, width), lambda i: (0, 0)),
        ],
        out_specs=pl.BlockSpec((tile, features), lambda i: (i, 0)),
    )(rows, mix)


def summed_everywhere(rows):
    axes = ("gx", "gy")
    devices = lax.axis_size("gx") * lax.axis_size("gy")
    parts = lax.all_to_all(rows, axes, 0, 0, tiled=True)
    chunk = parts.reshape((devices, rows.shape[0] // devices) + rows.shape[1:]).sum(axis=0)
    copies = jnp.broadcast_to(chunk[None], (devices,) + chunk.shape).reshape(rows.shape)
    return lax.all_to_all(copies, axes, 0, 0, tiled=True)


def localize(
    owners,
    obs_cells,
    block_mask,
    tile_east,
    tile_north,
    span_east,
    span_north,
    tiles_north,
    grid_east,
    grid_north,
):
    place_east = (owners // tiles_north * span_east + obs_cells // span_north).astype(jnp.float32)
    place_north = (owners % tiles_north * span_north + obs_cells % span_north).astype(jnp.float32)
    centre_east = (tile_east * span_east).astype(jnp.float32) + (span_east - 1) / 2.0
    centre_north = (tile_north * span_north).astype(jnp.float32) + (span_north - 1) / 2.0
    gap_east = (
        jnp.remainder(place_east - centre_east + grid_east / 2.0, grid_east) - grid_east / 2.0
    )
    gap_north = (
        jnp.remainder(place_north - centre_north + grid_north / 2.0, grid_north) - grid_north / 2.0
    )
    scale_east = gap_east / (radius_share * grid_east)
    scale_north = gap_north / (radius_share * grid_north)
    weight = jnp.exp(-0.5 * (scale_east * scale_east + scale_north * scale_north))
    blocks = block_mask.shape[0]
    return (weight.reshape(blocks, -1) * block_mask.astype(jnp.float32)[:, None]).reshape(-1)


def transform(predicted, obs_value, obs_error, weight_obs):
    rows, width = predicted.shape
    groups = width // ENS
    members = ENS

    def spread(per_obs):
        return jnp.broadcast_to(per_obs.reshape(rows, groups, 1), (rows, groups, ENS)).reshape(rows, width)

    lane_in = lax.broadcasted_iota(jnp.int32, (width, width), 0) // ENS
    lane_out = lax.broadcasted_iota(jnp.int32, (width, width), 1) // ENS
    averaging = jnp.where(lane_in == lane_out, 1.0 / members, 0.0).astype(jnp.float32)
    centre_obs = product(predicted, averaging)
    error = spread(obs_error)
    deviation = (predicted - centre_obs) / error
    innovation = (spread(obs_value) - centre_obs) / error
    weighted = deviation * spread(weight_obs)
    blocks = product(weighted.T, deviation)
    covariance = sum(blocks[k * ENS:(k + 1) * ENS, k * ENS:(k + 1) * ENS] for k in range(groups))
    projected = jnp.sum(weighted * innovation, axis=0)
    projection = sum(projected[k * ENS:(k + 1) * ENS] for k in range(groups))
    unit_matrix = jnp.eye(members, dtype=jnp.float32)
    system = (members - 1.0) * unit_matrix + covariance
    row_bound = jnp.max(jnp.sum(jnp.abs(system), axis=1))

    def refine(sweep_index, iterates):
        approach, inverse_root = iterates
        middle = 1.5 * unit_matrix - 0.5 * product(inverse_root, approach)
        return (product(approach, middle), product(middle, inverse_root))

    approach, inverse_root = lax.fori_loop(0, NSIT, refine, (system / row_bound, unit_matrix))
    inverse = product(inverse_root, inverse_root) / row_bound
    weights = product(inverse, projection[:, None])[:, 0]
    centring = unit_matrix - 1.0 / members
    shifts = weights[:, None] + math.sqrt(members - 1.0) * inverse_root / jnp.sqrt(row_bound)
    return 1.0 / members + product(centring, shifts)


def block_diagonal(mix, copies):
    return jnp.kron(jnp.eye(copies, dtype=mix.dtype), mix)


def local(state, obs_owner, obs_cell, obs_level, obs_coef, obs_value, obs_error, pattern):
    span_east, span_north, features = state.shape
    tiles_east = lax.axis_size("gx")
    tiles_north = lax.axis_size("gy")
    tile_east = lax.axis_index("gx")
    tile_north = lax.axis_index("gy")
    own_tile = tile_east * tiles_north + tile_north
    field = advance_twice(state)
    cells = field.reshape(span_east * span_north, features)
    width = features // COMP
    groups = width // ENS
    owned = (obs_owner == own_tile).astype(jnp.float32)
    spread_lane = lax.broadcasted_iota(jnp.int32, (groups * width, groups * ENS), 0)
    dense_lane = lax.broadcasted_iota(jnp.int32, (groups * width, groups * ENS), 1)
    fold = (
        (spread_lane // width == dense_lane // ENS) & (spread_lane % ENS == dense_lane % ENS)
    ).astype(jnp.float32)

    def observed(batch_index):
        masked_coefs = obs_coef[batch_index] * owned[batch_index][None, :]
        spread = gather_rows(
            owned[batch_index].astype(jnp.int32),
            obs_cell[batch_index],
            obs_level[batch_index],
            masked_coefs,
            cells,
        )
        return product(spread, fold)

    def mixing(local_terms, batch_index):
        predicted = summed_everywhere(local_terms)
        weight_obs = localize(
            obs_owner[batch_index],
            obs_cell[batch_index],
            pattern[0, 0, batch_index],
            tile_east,
            tile_north,
            span_east,
            span_north,
            tiles_north,
            span_east * tiles_east,
            span_north * tiles_north,
        )
        return transform(predicted, obs_value[batch_index], obs_error[batch_index], weight_obs)

    first_mix = mixing(observed(0), 0)
    second_terms = product(observed(1), block_diagonal(first_mix, groups))
    second_mix = mixing(second_terms, 1)
    rows = mixed_once(cells, block_diagonal(product(first_mix, second_mix), groups))
    return rows.reshape(span_east, span_north, features)


def solution(mesh):
    placed = (P("gx", "gy", None), P(), P(), P(), P(), P(), P(), P("gx", "gy", None, None))
    return jax.shard_map(
        local, mesh=mesh, in_specs=placed, out_specs=P("gx", "gy", None), check_vma=False
    )
```

```python
import math

import jax
import jax.numpy as jnp
from jax import lax
from jax.experimental import pallas as pl
from jax.experimental.pallas import tpu as pltpu
from jax.sharding import PartitionSpec as P

ENS = 32
LEV = 4
COMP = 3
NSIT = 4


courant = 0.1
diffusion = 0.08
radius_share = 0.25


def gather_kernel(busy_ref, cell_ref, level_ref, coef_ref, field_ref, fold_ref, out_ref, spread_ref):
    count = cell_ref.shape[0]
    width = field_ref.shape[1] // 3
    lane_level = lax.broadcasted_iota(jnp.int32, (1, width), 1) // ENS
    sublane = lax.broadcasted_iota(jnp.int32, (8, width), 0)
    groups = width // ENS
    spread_ref[...] = jnp.zeros(spread_ref.shape, spread_ref.dtype)

    def body(block, carry):
        @pl.when(busy_ref[block] > 0)
        def _():
            gathered = [jnp.zeros((8, width), jnp.float32) for k in range(groups)]
            for i in range(8):
                for k in range(groups):
                    j = (block * 8 + i) * groups + k
                    picked = field_ref[pl.ds(cell_ref[j], 1), :]
                    value = (
                        coef_ref[j] * picked[:, 0:width]
                        + coef_ref[count + j] * picked[:, width:2 * width]
                        + coef_ref[2 * count + j] * picked[:, 2 * width:3 * width]
                    )
                    value = jnp.where(lane_level == level_ref[j], value, 0.0)
                    gathered[k] = jnp.where(sublane == i, value, gathered[k])
            first = pl.multiple_of(block * 8, 8)
            for k in range(groups):
                spread_ref[pl.ds(first, 8), k * width:(k + 1) * width] = gathered[k]

        return carry

    lax.fori_loop(0, count // (8 * groups), body, 0)
    out_ref[...] = product(spread_ref[...], fold_ref[...])


def gather_rows(flags, cells, levels, coefs, field, fold):
    count = cells.shape[0]
    width = field.shape[1] // 3
    groups = width // ENS
    busy = jnp.max(flags.reshape(-1, 8 * groups), axis=1)
    smem = pl.BlockSpec(memory_space=pltpu.SMEM)
    vmem = pl.BlockSpec(memory_space=pltpu.VMEM)
    return pl.pallas_call(
        gather_kernel,
        out_shape=jax.ShapeDtypeStruct((count // groups, width), jnp.float32),
        in_specs=[smem, smem, smem, smem, vmem, vmem],
        out_specs=vmem,
        scratch_shapes=[pltpu.VMEM((count // groups, groups * width), jnp.float32)],
    )(busy, cells, levels, coefs.reshape(-1), field, fold)


def advect_update(c, w, e, s, n, width):
    u = c[:, 0:width]
    v = c[:, width:2 * width]
    pu, mu = jnp.maximum(u, 0.0), jnp.minimum(u, 0.0)
    pv, mv = jnp.maximum(v, 0.0), jnp.minimum(v, 0.0)
    blocks = []
    for b in range(3):
        lanes = slice(b * width, (b + 1) * width)
        cc, ww, ee, ss, nn = c[:, lanes], w[:, lanes], e[:, lanes], s[:, lanes], n[:, lanes]
        flux = pu * (cc - ww) + mu * (ee - cc) + pv * (cc - ss) + mv * (nn - cc)
        blocks.append(cc - courant * flux + diffusion * (ww + ee + (ss + nn) - 4.0 * cc))
    return blocks


def shifted(values, edge, shift):
    count = values.shape[0]
    row = lax.broadcasted_iota(jnp.int32, values.shape, 0)
    fresh = 0 if shift == 1 else count - 1
    return jnp.where(row == fresh, edge, pltpu.roll(values, shift % count, 0))


def two_steps_kernel(
    field_ref, west_ref, east_ref, south0_ref, south1_ref, north0_ref, north1_ref,
    first_col_ref, last_col_ref, corner_ref, out_ref, mid_ref, ring_ref,
):
    nx, ny, feat = field_ref.shape
    width = feat // 3

    def store(ref, index, blocks):
        for b in range(3):
            ref[index, :, b * width:(b + 1) * width] = blocks[b]

    def first_pass(x, carry):
        centre = field_ref[x]
        west = jnp.where(x == 0, west_ref[1], field_ref[jnp.maximum(x - 1, 0)])
        east = jnp.where(x == nx - 1, east_ref[0], field_ref[jnp.minimum(x + 1, nx - 1)])
        south = shifted(centre, south1_ref[pl.ds(x, 1), :], 1)
        north = shifted(centre, north0_ref[pl.ds(x, 1), :], -1)
        store(mid_ref, x, advect_update(centre, west, east, south, north, width))
        return carry

    lax.fori_loop(0, nx, first_pass, 0)
    corner = corner_ref[...]
    centre = west_ref[1]
    ring_w = advect_update(centre, west_ref[0], field_ref[0], shifted(centre, corner[0:1], 1), shifted(centre, corner[1:2], -1), width)
    centre = east_ref[0]
    ring_e = advect_update(centre, field_ref[nx - 1], east_ref[1], shifted(centre, corner[2:3], 1), shifted(centre, corner[3:4], -1), width)
    centre = south1_ref[...]
    ring_s = advect_update(centre, shifted(centre, corner[0:1], 1), shifted(centre, corner[2:3], -1), south0_ref[...], first_col_ref[...], width)
    centre = north0_ref[...]
    ring_n = advect_update(centre, shifted(centre, corner[1:2], 1), shifted(centre, corner[3:4], -1), last_col_ref[...], north1_ref[...], width)
    store(ring_ref, 0, ring_w)
    store(ring_ref, 1, ring_e)
    for b in range(3):
        ring_ref[2, 0:nx, b * width:(b + 1) * width] = ring_s[b]
        ring_ref[3, 0:nx, b * width:(b + 1) * width] = ring_n[b]

    def second_pass(x, carry):
        centre = mid_ref[x]
        west = jnp.where(x == 0, ring_ref[0], mid_ref[jnp.maximum(x - 1, 0)])
        east = jnp.where(x == nx - 1, ring_ref[1], mid_ref[jnp.minimum(x + 1, nx - 1)])
        south = shifted(centre, ring_ref[2, pl.ds(x, 1), :], 1)
        north = shifted(centre, ring_ref[3, pl.ds(x, 1), :], -1)
        store(out_ref, x, advect_update(centre, west, east, south, north, width))
        return carry

    lax.fori_loop(0, nx, second_pass, 0)


def two_steps(field, west, east, south0, south1, north0, north1, first_col, last_col, corner):
    nx, ny, feat = field.shape
    vmem = pl.BlockSpec(memory_space=pltpu.VMEM)
    return pl.pallas_call(
        two_steps_kernel,
        out_shape=jax.ShapeDtypeStruct(field.shape, field.dtype),
        in_specs=[vmem] * 10,
        out_specs=vmem,
        scratch_shapes=[
            pltpu.VMEM(field.shape, jnp.float32),
            pltpu.VMEM((4, max(nx, ny), feat), jnp.float32),
        ],
    )(field, west, east, south0, south1, north0, north1, first_col, last_col, corner)


def advance_twice(field):
    nx, ny, feat = field.shape
    sx, sy = lax.axis_size("gx"), lax.axis_size("gy")
    up_x = [(i, (i + 1) % sx) for i in range(sx)]
    down_x = [(j, i) for i, j in up_x]
    up_y = [(i, (i + 1) % sy) for i in range(sy)]
    down_y = [(j, i) for i, j in up_y]
    west = lax.ppermute(field[nx - 2:], "gx", up_x)
    east = lax.ppermute(field[:2], "gx", down_x)
    last_cols = jnp.concatenate([west[:, ny - 2:], field[:, ny - 2:], east[:, ny - 2:]])
    first_cols = jnp.concatenate([west[:, :2], field[:, :2], east[:, :2]])
    south = lax.ppermute(last_cols, "gy", up_y)
    north = lax.ppermute(first_cols, "gy", down_y)
    corner = jnp.stack([south[1, 1], north[1, 0], south[nx + 2, 1], north[nx + 2, 0]])
    return two_steps(
        field, west, east, south[2:nx + 2, 0], south[2:nx + 2, 1], north[2:nx + 2, 0], north[2:nx + 2, 1],
        field[:, 0], field[:, ny - 1], corner,
    )


def product(left, right):
    return jnp.dot(left, right, precision=lax.Precision.HIGHEST, preferred_element_type=jnp.float32)


def mix_kernel(rows_ref, mix_ref, out_ref):
    width = mix_ref.shape[0]
    for block in range(rows_ref.shape[1] // width):
        lanes = slice(block * width, (block + 1) * width)
        out_ref[:, lanes] = product(rows_ref[:, lanes], mix_ref[...])


def mixed_once(rows, mix):
    count, features = rows.shape
    width = mix.shape[0]
    tile = 512
    return pl.pallas_call(
        mix_kernel,
        out_shape=jax.ShapeDtypeStruct(rows.shape, rows.dtype),
        grid=(count // tile,),
        in_specs=[
            pl.BlockSpec((tile, features), lambda i: (i, 0)),
            pl.BlockSpec((width, width), lambda i: (0, 0)),
        ],
        out_specs=pl.BlockSpec((tile, features), lambda i: (i, 0)),
    )(rows, mix)


def summed_everywhere(rows):
    axes = ("gx", "gy")
    devices = lax.axis_size("gx") * lax.axis_size("gy")
    parts = lax.all_to_all(rows, axes, 0, 0, tiled=True)
    chunk = parts.reshape((devices, rows.shape[0] // devices) + rows.shape[1:]).sum(axis=0)
    copies = jnp.broadcast_to(chunk[None], (devices,) + chunk.shape).reshape(rows.shape)
    return lax.all_to_all(copies, axes, 0, 0, tiled=True)


def localize(
    owners,
    obs_cells,
    block_mask,
    tile_east,
    tile_north,
    span_east,
    span_north,
    tiles_north,
    grid_east,
    grid_north,
):
    place_east = (owners // tiles_north * span_east + obs_cells // span_north).astype(jnp.float32)
    place_north = (owners % tiles_north * span_north + obs_cells % span_north).astype(jnp.float32)
    centre_east = (tile_east * span_east).astype(jnp.float32) + (span_east - 1) / 2.0
    centre_north = (tile_north * span_north).astype(jnp.float32) + (span_north - 1) / 2.0
    gap_east = (
        jnp.remainder(place_east - centre_east + grid_east / 2.0, grid_east) - grid_east / 2.0
    )
    gap_north = (
        jnp.remainder(place_north - centre_north + grid_north / 2.0, grid_north) - grid_north / 2.0
    )
    scale_east = gap_east / (radius_share * grid_east)
    scale_north = gap_north / (radius_share * grid_north)
    weight = jnp.exp(-0.5 * (scale_east * scale_east + scale_north * scale_north))
    blocks = block_mask.shape[0]
    return (weight.reshape(blocks, -1) * block_mask.astype(jnp.float32)[:, None]).reshape(-1)


def transform(predicted, obs_value, obs_error, weight_obs):
    rows, width = predicted.shape
    groups = width // ENS
    members = ENS

    def spread(per_obs):
        return jnp.broadcast_to(per_obs.reshape(rows, groups, 1), (rows, groups, ENS)).reshape(rows, width)

    lane_in = lax.broadcasted_iota(jnp.int32, (width, width), 0) // ENS
    lane_out = lax.broadcasted_iota(jnp.int32, (width, width), 1) // ENS
    averaging = jnp.where(lane_in == lane_out, 1.0 / members, 0.0).astype(jnp.float32)
    centre_obs = product(predicted, averaging)
    error = spread(obs_error)
    deviation = (predicted - centre_obs) / error
    innovation = (spread(obs_value) - centre_obs) / error
    weighted = deviation * spread(weight_obs)
    blocks = product(weighted.T, deviation)
    covariance = sum(blocks[k * ENS:(k + 1) * ENS, k * ENS:(k + 1) * ENS] for k in range(groups))
    projected = jnp.sum(weighted * innovation, axis=0)
    projection = sum(projected[k * ENS:(k + 1) * ENS] for k in range(groups))
    unit_matrix = jnp.eye(members, dtype=jnp.float32)
    system = (members - 1.0) * unit_matrix + covariance
    row_bound = jnp.max(jnp.sum(jnp.abs(system), axis=1))

    def refine(sweep_index, iterates):
        approach, inverse_root = iterates
        middle = 1.5 * unit_matrix - 0.5 * product(inverse_root, approach)
        return (product(approach, middle), product(middle, inverse_root))

    approach, inverse_root = lax.fori_loop(0, NSIT, refine, (system / row_bound, unit_matrix))
    inverse = product(inverse_root, inverse_root) / row_bound
    weights = product(inverse, projection[:, None])[:, 0]
    centring = unit_matrix - 1.0 / members
    shifts = weights[:, None] + math.sqrt(members - 1.0) * inverse_root / jnp.sqrt(row_bound)
    return 1.0 / members + product(centring, shifts)


def block_diagonal(mix, copies):
    return jnp.kron(jnp.eye(copies, dtype=mix.dtype), mix)


def local(state, obs_owner, obs_cell, obs_level, obs_coef, obs_value, obs_error, pattern):
    span_east, span_north, features = state.shape
    tiles_east = lax.axis_size("gx")
    tiles_north = lax.axis_size("gy")
    tile_east = lax.axis_index("gx")
    tile_north = lax.axis_index("gy")
    own_tile = tile_east * tiles_north + tile_north
    field = advance_twice(state)
    cells = field.reshape(span_east * span_north, features)
    width = features // COMP
    groups = width // ENS
    owned = (obs_owner == own_tile).astype(jnp.float32)
    spread_lane = lax.broadcasted_iota(jnp.int32, (groups * width, groups * ENS), 0)
    dense_lane = lax.broadcasted_iota(jnp.int32, (groups * width, groups * ENS), 1)
    fold = (
        (spread_lane // width == dense_lane // ENS) & (spread_lane % ENS == dense_lane % ENS)
    ).astype(jnp.float32)

    def observed(batch_index):
        masked_coefs = obs_coef[batch_index] * owned[batch_index][None, :]
        spread = gather_rows(
            owned[batch_index].astype(jnp.int32),
            obs_cell[batch_index],
            obs_level[batch_index],
            masked_coefs,
            cells,
            fold,
        )
        return spread

    def mixing(local_terms, batch_index):
        predicted = summed_everywhere(local_terms)
        weight_obs = localize(
            obs_owner[batch_index],
            obs_cell[batch_index],
            pattern[0, 0, batch_index],
            tile_east,
            tile_north,
            span_east,
            span_north,
            tiles_north,
            span_east * tiles_east,
            span_north * tiles_north,
        )
        return transform(predicted, obs_value[batch_index], obs_error[batch_index], weight_obs)

    first_mix = mixing(observed(0), 0)
    second_terms = product(observed(1), block_diagonal(first_mix, groups))
    second_mix = mixing(second_terms, 1)
    rows = mixed_once(cells, block_diagonal(product(first_mix, second_mix), groups))
    return rows.reshape(span_east, span_north, features)


def solution(mesh):
    placed = (P("gx", "gy", None), P(), P(), P(), P(), P(), P(), P("gx", "gy", None, None))
    return jax.shard_map(
        local, mesh=mesh, in_specs=placed, out_specs=P("gx", "gy", None), check_vma=False
    )
```

```python
import math

import jax
import jax.numpy as jnp
from jax import lax
from jax.experimental import pallas as pl
from jax.experimental.pallas import tpu as pltpu
from jax.sharding import PartitionSpec as P

ENS = 32
LEV = 4
COMP = 3
NSIT = 4


courant = 0.1
diffusion = 0.08
radius_share = 0.25


def gather_kernel(busy_ref, cell_ref, level_ref, coef_ref, field_ref, fold_ref, out_ref, spread_ref):
    count = cell_ref.shape[0]
    width = field_ref.shape[1] // 3
    lane_level = lax.broadcasted_iota(jnp.int32, (1, width), 1) // ENS
    sublane = lax.broadcasted_iota(jnp.int32, (8, width), 0)
    groups = width // ENS
    spread_ref[...] = jnp.zeros(spread_ref.shape, spread_ref.dtype)

    def body(block, carry):
        @pl.when(busy_ref[block] > 0)
        def _():
            gathered = [jnp.zeros((8, width), jnp.float32) for k in range(groups)]
            for i in range(8):
                for k in range(groups):
                    j = (block * 8 + i) * groups + k
                    picked = field_ref[pl.ds(cell_ref[j], 1), :]
                    value = (
                        coef_ref[j] * picked[:, 0:width]
                        + coef_ref[count + j] * picked[:, width:2 * width]
                        + coef_ref[2 * count + j] * picked[:, 2 * width:3 * width]
                    )
                    value = jnp.where(lane_level == level_ref[j], value, 0.0)
                    gathered[k] = jnp.where(sublane == i, value, gathered[k])
            first = pl.multiple_of(block * 8, 8)
            for k in range(groups):
                spread_ref[pl.ds(first, 8), k * width:(k + 1) * width] = gathered[k]

        return carry

    lax.fori_loop(0, count // (8 * groups), body, 0)
    out_ref[...] = product(spread_ref[...], fold_ref[...])


def gather_rows(flags, cells, levels, coefs, field, fold):
    count = cells.shape[0]
    width = field.shape[1] // 3
    groups = width // ENS
    busy = jnp.max(flags.reshape(-1, 8 * groups), axis=1)
    smem = pl.BlockSpec(memory_space=pltpu.SMEM)
    vmem = pl.BlockSpec(memory_space=pltpu.VMEM)
    return pl.pallas_call(
        gather_kernel,
        out_shape=jax.ShapeDtypeStruct((count // groups, width), jnp.float32),
        in_specs=[smem, smem, smem, smem, vmem, vmem],
        out_specs=vmem,
        scratch_shapes=[pltpu.VMEM((count // groups, groups * width), jnp.float32)],
    )(busy, cells, levels, coefs.reshape(-1), field, fold)


def advect_update(c, w, e, s, n, width):
    u = c[:, 0:width]
    v = c[:, width:2 * width]
    pu, mu = jnp.maximum(u, 0.0), jnp.minimum(u, 0.0)
    pv, mv = jnp.maximum(v, 0.0), jnp.minimum(v, 0.0)
    blocks = []
    for b in range(3):
        lanes = slice(b * width, (b + 1) * width)
        cc, ww, ee, ss, nn = c[:, lanes], w[:, lanes], e[:, lanes], s[:, lanes], n[:, lanes]
        flux = pu * (cc - ww) + mu * (ee - cc) + pv * (cc - ss) + mv * (nn - cc)
        blocks.append(cc - courant * flux + diffusion * (ww + ee + (ss + nn) - 4.0 * cc))
    return blocks


def shifted(values, edge, shift):
    count = values.shape[0]
    row = lax.broadcasted_iota(jnp.int32, values.shape, 0)
    fresh = 0 if shift == 1 else count - 1
    return jnp.where(row == fresh, edge, pltpu.roll(values, shift % count, 0))


def two_steps_kernel(
    field_ref, west_ref, east_ref, south0_ref, south1_ref, north0_ref, north1_ref,
    first_col_ref, last_col_ref, corner_ref, out_ref, mid_ref, ring_ref,
):
    nx, ny, feat = field_ref.shape
    width = feat // 3

    def store(ref, index, blocks):
        for b in range(3):
            ref[index, :, b * width:(b + 1) * width] = blocks[b]

    def first_pass(x, carry):
        centre = field_ref[x]
        west = jnp.where(x == 0, west_ref[1], field_ref[jnp.maximum(x - 1, 0)])
        east = jnp.where(x == nx - 1, east_ref[0], field_ref[jnp.minimum(x + 1, nx - 1)])
        south = shifted(centre, south1_ref[pl.ds(x, 1), :], 1)
        north = shifted(centre, north0_ref[pl.ds(x, 1), :], -1)
        store(mid_ref, x, advect_update(centre, west, east, south, north, width))
        return carry

    lax.fori_loop(0, nx, first_pass, 0)
    corner = corner_ref[...]
    centre = west_ref[1]
    ring_w = advect_update(centre, west_ref[0], field_ref[0], shifted(centre, corner[0:1], 1), shifted(centre, corner[1:2], -1), width)
    centre = east_ref[0]
    ring_e = advect_update(centre, field_ref[nx - 1], east_ref[1], shifted(centre, corner[2:3], 1), shifted(centre, corner[3:4], -1), width)
    centre = south1_ref[...]
    ring_s = advect_update(centre, shifted(centre, corner[0:1], 1), shifted(centre, corner[2:3], -1), south0_ref[...], first_col_ref[...], width)
    centre = north0_ref[...]
    ring_n = advect_update(centre, shifted(centre, corner[1:2], 1), shifted(centre, corner[3:4], -1), last_col_ref[...], north1_ref[...], width)
    store(ring_ref, 0, ring_w)
    store(ring_ref, 1, ring_e)
    for b in range(3):
        ring_ref[2, 0:nx, b * width:(b + 1) * width] = ring_s[b]
        ring_ref[3, 0:nx, b * width:(b + 1) * width] = ring_n[b]

    def second_pass(x, carry):
        centre = mid_ref[x]
        west = jnp.where(x == 0, ring_ref[0], mid_ref[jnp.maximum(x - 1, 0)])
        east = jnp.where(x == nx - 1, ring_ref[1], mid_ref[jnp.minimum(x + 1, nx - 1)])
        south = shifted(centre, ring_ref[2, pl.ds(x, 1), :], 1)
        north = shifted(centre, ring_ref[3, pl.ds(x, 1), :], -1)
        store(out_ref, x, advect_update(centre, west, east, south, north, width))
        return carry

    lax.fori_loop(0, nx, second_pass, 0)


def two_steps(field, west, east, south0, south1, north0, north1, first_col, last_col, corner):
    nx, ny, feat = field.shape
    vmem = pl.BlockSpec(memory_space=pltpu.VMEM)
    return pl.pallas_call(
        two_steps_kernel,
        out_shape=jax.ShapeDtypeStruct(field.shape, field.dtype),
        in_specs=[vmem] * 10,
        out_specs=vmem,
        scratch_shapes=[
            pltpu.VMEM(field.shape, jnp.float32),
            pltpu.VMEM((4, max(nx, ny), feat), jnp.float32),
        ],
    )(field, west, east, south0, south1, north0, north1, first_col, last_col, corner)


def advance_twice(field):
    nx, ny, feat = field.shape
    sx, sy = lax.axis_size("gx"), lax.axis_size("gy")
    up_x = [(i, (i + 1) % sx) for i in range(sx)]
    down_x = [(j, i) for i, j in up_x]
    up_y = [(i, (i + 1) % sy) for i in range(sy)]
    down_y = [(j, i) for i, j in up_y]
    west = lax.ppermute(field[nx - 2:], "gx", up_x)
    east = lax.ppermute(field[:2], "gx", down_x)
    last_cols = jnp.concatenate([west[:, ny - 2:], field[:, ny - 2:], east[:, ny - 2:]])
    first_cols = jnp.concatenate([west[:, :2], field[:, :2], east[:, :2]])
    south = lax.ppermute(last_cols, "gy", up_y)
    north = lax.ppermute(first_cols, "gy", down_y)
    corner = jnp.stack([south[1, 1], north[1, 0], south[nx + 2, 1], north[nx + 2, 0]])
    return two_steps(
        field, west, east, south[2:nx + 2, 0], south[2:nx + 2, 1], north[2:nx + 2, 0], north[2:nx + 2, 1],
        field[:, 0], field[:, ny - 1], corner,
    )


def product(left, right):
    return jnp.dot(left, right, precision=lax.Precision.HIGHEST, preferred_element_type=jnp.float32)


def mix_kernel(rows_ref, mix_ref, out_ref):
    width = mix_ref.shape[0]
    for block in range(rows_ref.shape[1] // width):
        lanes = slice(block * width, (block + 1) * width)
        out_ref[:, lanes] = product(rows_ref[:, lanes], mix_ref[...])


def mixed_once(rows, mix):
    count, features = rows.shape
    width = mix.shape[0]
    tile = 1024
    return pl.pallas_call(
        mix_kernel,
        out_shape=jax.ShapeDtypeStruct(rows.shape, rows.dtype),
        grid=(count // tile,),
        in_specs=[
            pl.BlockSpec((tile, features), lambda i: (i, 0)),
            pl.BlockSpec((width, width), lambda i: (0, 0)),
        ],
        out_specs=pl.BlockSpec((tile, features), lambda i: (i, 0)),
    )(rows, mix)


def summed_everywhere(rows):
    axes = ("gx", "gy")
    devices = lax.axis_size("gx") * lax.axis_size("gy")
    parts = lax.all_to_all(rows, axes, 0, 0, tiled=True)
    chunk = parts.reshape((devices, rows.shape[0] // devices) + rows.shape[1:]).sum(axis=0)
    copies = jnp.broadcast_to(chunk[None], (devices,) + chunk.shape).reshape(rows.shape)
    return lax.all_to_all(copies, axes, 0, 0, tiled=True)


def localize(
    owners,
    obs_cells,
    block_mask,
    tile_east,
    tile_north,
    span_east,
    span_north,
    tiles_north,
    grid_east,
    grid_north,
):
    place_east = (owners // tiles_north * span_east + obs_cells // span_north).astype(jnp.float32)
    place_north = (owners % tiles_north * span_north + obs_cells % span_north).astype(jnp.float32)
    centre_east = (tile_east * span_east).astype(jnp.float32) + (span_east - 1) / 2.0
    centre_north = (tile_north * span_north).astype(jnp.float32) + (span_north - 1) / 2.0
    gap_east = (
        jnp.remainder(place_east - centre_east + grid_east / 2.0, grid_east) - grid_east / 2.0
    )
    gap_north = (
        jnp.remainder(place_north - centre_north + grid_north / 2.0, grid_north) - grid_north / 2.0
    )
    scale_east = gap_east / (radius_share * grid_east)
    scale_north = gap_north / (radius_share * grid_north)
    weight = jnp.exp(-0.5 * (scale_east * scale_east + scale_north * scale_north))
    blocks = block_mask.shape[0]
    return (weight.reshape(blocks, -1) * block_mask.astype(jnp.float32)[:, None]).reshape(-1)


def transform(predicted, obs_value, obs_error, weight_obs):
    rows, width = predicted.shape
    groups = width // ENS
    members = ENS

    def spread(per_obs):
        return jnp.broadcast_to(per_obs.reshape(rows, groups, 1), (rows, groups, ENS)).reshape(rows, width)

    lane_in = lax.broadcasted_iota(jnp.int32, (width, width), 0) // ENS
    lane_out = lax.broadcasted_iota(jnp.int32, (width, width), 1) // ENS
    averaging = jnp.where(lane_in == lane_out, 1.0 / members, 0.0).astype(jnp.float32)
    centre_obs = product(predicted, averaging)
    error = spread(obs_error)
    deviation = (predicted - centre_obs) / error
    innovation = (spread(obs_value) - centre_obs) / error
    weighted = deviation * spread(weight_obs)
    blocks = product(weighted.T, deviation)
    covariance = sum(blocks[k * ENS:(k + 1) * ENS, k * ENS:(k + 1) * ENS] for k in range(groups))
    projected = jnp.sum(weighted * innovation, axis=0)
    projection = sum(projected[k * ENS:(k + 1) * ENS] for k in range(groups))
    unit_matrix = jnp.eye(members, dtype=jnp.float32)
    system = (members - 1.0) * unit_matrix + covariance
    row_bound = jnp.max(jnp.sum(jnp.abs(system), axis=1))

    def refine(sweep_index, iterates):
        approach, inverse_root = iterates
        middle = 1.5 * unit_matrix - 0.5 * product(inverse_root, approach)
        return (product(approach, middle), product(middle, inverse_root))

    approach, inverse_root = lax.fori_loop(0, NSIT, refine, (system / row_bound, unit_matrix), unroll=True)
    inverse = product(inverse_root, inverse_root) / row_bound
    weights = product(inverse, projection[:, None])[:, 0]
    centring = unit_matrix - 1.0 / members
    shifts = weights[:, None] + math.sqrt(members - 1.0) * inverse_root / jnp.sqrt(row_bound)
    return 1.0 / members + product(centring, shifts)


def block_diagonal(mix, copies):
    return jnp.kron(jnp.eye(copies, dtype=mix.dtype), mix)


def local(state, obs_owner, obs_cell, obs_level, obs_coef, obs_value, obs_error, pattern):
    span_east, span_north, features = state.shape
    tiles_east = lax.axis_size("gx")
    tiles_north = lax.axis_size("gy")
    tile_east = lax.axis_index("gx")
    tile_north = lax.axis_index("gy")
    own_tile = tile_east * tiles_north + tile_north
    field = advance_twice(state)
    cells = field.reshape(span_east * span_north, features)
    width = features // COMP
    groups = width // ENS
    owned = (obs_owner == own_tile).astype(jnp.float32)
    spread_lane = lax.broadcasted_iota(jnp.int32, (groups * width, groups * ENS), 0)
    dense_lane = lax.broadcasted_iota(jnp.int32, (groups * width, groups * ENS), 1)
    fold = (
        (spread_lane // width == dense_lane // ENS) & (spread_lane % ENS == dense_lane % ENS)
    ).astype(jnp.float32)

    def observed(batch_index):
        masked_coefs = obs_coef[batch_index] * owned[batch_index][None, :]
        spread = gather_rows(
            owned[batch_index].astype(jnp.int32),
            obs_cell[batch_index],
            obs_level[batch_index],
            masked_coefs,
            cells,
            fold,
        )
        return spread

    def mixing(local_terms, batch_index):
        predicted = summed_everywhere(local_terms)
        weight_obs = localize(
            obs_owner[batch_index],
            obs_cell[batch_index],
            pattern[0, 0, batch_index],
            tile_east,
            tile_north,
            span_east,
            span_north,
            tiles_north,
            span_east * tiles_east,
            span_north * tiles_north,
        )
        return transform(predicted, obs_value[batch_index], obs_error[batch_index], weight_obs)

    first_mix = mixing(observed(0), 0)
    second_terms = product(observed(1), block_diagonal(first_mix, groups))
    second_mix = mixing(second_terms, 1)
    rows = mixed_once(cells, block_diagonal(product(first_mix, second_mix), groups))
    return rows.reshape(span_east, span_north, features)


def solution(mesh):
    placed = (P("gx", "gy", None), P(), P(), P(), P(), P(), P(), P("gx", "gy", None, None))
    return jax.shard_map(
        local, mesh=mesh, in_specs=placed, out_specs=P("gx", "gy", None), check_vma=False
    )
```

```python
import math

import jax
import jax.numpy as jnp
from jax import lax
from jax.experimental import pallas as pl
from jax.experimental.pallas import tpu as pltpu
from jax.sharding import PartitionSpec as P

ENS = 32
LEV = 4
COMP = 3
NSIT = 4


courant = 0.1
diffusion = 0.08
radius_share = 0.25


def gather_kernel(busy_ref, cell_ref, level_ref, coef_ref, field_ref, fold_ref, out_ref, spread_ref):
    count = cell_ref.shape[0]
    width = field_ref.shape[1] // 3
    lane_level = lax.broadcasted_iota(jnp.int32, (1, width), 1) // ENS
    sublane = lax.broadcasted_iota(jnp.int32, (8, width), 0)
    groups = width // ENS
    spread_ref[...] = jnp.zeros(spread_ref.shape, spread_ref.dtype)

    def body(block, carry):
        @pl.when(busy_ref[block] > 0)
        def _():
            gathered = [jnp.zeros((8, width), jnp.float32) for k in range(groups)]
            for i in range(8):
                for k in range(groups):
                    j = (block * 8 + i) * groups + k
                    picked = field_ref[pl.ds(cell_ref[j], 1), :]
                    value = (
                        coef_ref[j] * picked[:, 0:width]
                        + coef_ref[count + j] * picked[:, width:2 * width]
                        + coef_ref[2 * count + j] * picked[:, 2 * width:3 * width]
                    )
                    value = jnp.where(lane_level == level_ref[j], value, 0.0)
                    gathered[k] = jnp.where(sublane == i, value, gathered[k])
            first = pl.multiple_of(block * 8, 8)
            for k in range(groups):
                spread_ref[pl.ds(first, 8), k * width:(k + 1) * width] = gathered[k]

        return carry

    lax.fori_loop(0, count // (8 * groups), body, 0)
    out_ref[...] = product(spread_ref[...], fold_ref[...])


def gather_rows(flags, cells, levels, coefs, field, fold):
    count = cells.shape[0]
    width = field.shape[1] // 3
    groups = width // ENS
    busy = jnp.max(flags.reshape(-1, 8 * groups), axis=1)
    smem = pl.BlockSpec(memory_space=pltpu.SMEM)
    vmem = pl.BlockSpec(memory_space=pltpu.VMEM)
    return pl.pallas_call(
        gather_kernel,
        out_shape=jax.ShapeDtypeStruct((count // groups, width), jnp.float32),
        in_specs=[smem, smem, smem, smem, vmem, vmem],
        out_specs=vmem,
        scratch_shapes=[pltpu.VMEM((count // groups, groups * width), jnp.float32)],
    )(busy, cells, levels, coefs.reshape(-1), field, fold)


def advect_update(c, w, e, s, n, width):
    u = c[:, 0:width]
    v = c[:, width:2 * width]
    pu, mu = jnp.maximum(u, 0.0), jnp.minimum(u, 0.0)
    pv, mv = jnp.maximum(v, 0.0), jnp.minimum(v, 0.0)
    blocks = []
    for b in range(3):
        lanes = slice(b * width, (b + 1) * width)
        cc, ww, ee, ss, nn = c[:, lanes], w[:, lanes], e[:, lanes], s[:, lanes], n[:, lanes]
        flux = pu * (cc - ww) + mu * (ee - cc) + pv * (cc - ss) + mv * (nn - cc)
        blocks.append(cc - courant * flux + diffusion * (ww + ee + (ss + nn) - 4.0 * cc))
    return blocks


def shifted(values, edge, shift):
    count = values.shape[0]
    row = lax.broadcasted_iota(jnp.int32, values.shape, 0)
    fresh = 0 if shift == 1 else count - 1
    return jnp.where(row == fresh, edge, pltpu.roll(values, shift % count, 0))


def two_steps_kernel(
    field_ref, west_ref, east_ref, south0_ref, south1_ref, north0_ref, north1_ref,
    first_col_ref, last_col_ref, corner_ref, out_ref, mid_ref, ring_ref,
):
    nx, ny, feat = field_ref.shape
    width = feat // 3

    def store(ref, index, blocks):
        for b in range(3):
            ref[index, :, b * width:(b + 1) * width] = blocks[b]

    def first_pass(x, carry):
        centre = field_ref[x]
        west = jnp.where(x == 0, west_ref[1], field_ref[jnp.maximum(x - 1, 0)])
        east = jnp.where(x == nx - 1, east_ref[0], field_ref[jnp.minimum(x + 1, nx - 1)])
        south = shifted(centre, south1_ref[pl.ds(x, 1), :], 1)
        north = shifted(centre, north0_ref[pl.ds(x, 1), :], -1)
        store(mid_ref, x, advect_update(centre, west, east, south, north, width))
        return carry

    lax.fori_loop(0, nx, first_pass, 0)
    corner = corner_ref[...]
    centre = west_ref[1]
    ring_w = advect_update(centre, west_ref[0], field_ref[0], shifted(centre, corner[0:1], 1), shifted(centre, corner[1:2], -1), width)
    centre = east_ref[0]
    ring_e = advect_update(centre, field_ref[nx - 1], east_ref[1], shifted(centre, corner[2:3], 1), shifted(centre, corner[3:4], -1), width)
    centre = south1_ref[...]
    ring_s = advect_update(centre, shifted(centre, corner[0:1], 1), shifted(centre, corner[2:3], -1), south0_ref[...], first_col_ref[...], width)
    centre = north0_ref[...]
    ring_n = advect_update(centre, shifted(centre, corner[1:2], 1), shifted(centre, corner[3:4], -1), last_col_ref[...], north1_ref[...], width)
    store(ring_ref, 0, ring_w)
    store(ring_ref, 1, ring_e)
    for b in range(3):
        ring_ref[2, 0:nx, b * width:(b + 1) * width] = ring_s[b]
        ring_ref[3, 0:nx, b * width:(b + 1) * width] = ring_n[b]

    def second_pass(x, carry):
        centre = mid_ref[x]
        west = jnp.where(x == 0, ring_ref[0], mid_ref[jnp.maximum(x - 1, 0)])
        east = jnp.where(x == nx - 1, ring_ref[1], mid_ref[jnp.minimum(x + 1, nx - 1)])
        south = shifted(centre, ring_ref[2, pl.ds(x, 1), :], 1)
        north = shifted(centre, ring_ref[3, pl.ds(x, 1), :], -1)
        store(out_ref, x, advect_update(centre, west, east, south, north, width))
        return carry

    lax.fori_loop(0, nx, second_pass, 0)


def two_steps(field, west, east, south0, south1, north0, north1, first_col, last_col, corner):
    nx, ny, feat = field.shape
    vmem = pl.BlockSpec(memory_space=pltpu.VMEM)
    return pl.pallas_call(
        two_steps_kernel,
        out_shape=jax.ShapeDtypeStruct(field.shape, field.dtype),
        in_specs=[vmem] * 10,
        out_specs=vmem,
        scratch_shapes=[
            pltpu.VMEM(field.shape, jnp.float32),
            pltpu.VMEM((4, max(nx, ny), feat), jnp.float32),
        ],
    )(field, west, east, south0, south1, north0, north1, first_col, last_col, corner)


def advance_twice(field):
    nx, ny, feat = field.shape
    sx, sy = lax.axis_size("gx"), lax.axis_size("gy")
    up_x = [(i, (i + 1) % sx) for i in range(sx)]
    down_x = [(j, i) for i, j in up_x]
    up_y = [(i, (i + 1) % sy) for i in range(sy)]
    down_y = [(j, i) for i, j in up_y]
    west = lax.ppermute(field[nx - 2:], "gx", up_x)
    east = lax.ppermute(field[:2], "gx", down_x)
    last_cols = jnp.concatenate([west[:, ny - 2:], field[:, ny - 2:], east[:, ny - 2:]])
    first_cols = jnp.concatenate([west[:, :2], field[:, :2], east[:, :2]])
    south = lax.ppermute(last_cols, "gy", up_y)
    north = lax.ppermute(first_cols, "gy", down_y)
    corner = jnp.stack([south[1, 1], north[1, 0], south[nx + 2, 1], north[nx + 2, 0]])
    return two_steps(
        field, west, east, south[2:nx + 2, 0], south[2:nx + 2, 1], north[2:nx + 2, 0], north[2:nx + 2, 1],
        field[:, 0], field[:, ny - 1], corner,
    )


def product(left, right):
    return jnp.dot(left, right, precision=lax.Precision.HIGHEST, preferred_element_type=jnp.float32)


def mix_kernel(rows_ref, mix_ref, out_ref):
    width = mix_ref.shape[0]
    for block in range(rows_ref.shape[1] // width):
        lanes = slice(block * width, (block + 1) * width)
        out_ref[:, lanes] = product(rows_ref[:, lanes], mix_ref[...])


def mixed_once(rows, mix):
    count, features = rows.shape
    width = mix.shape[0]
    tile = 1024
    return pl.pallas_call(
        mix_kernel,
        out_shape=jax.ShapeDtypeStruct(rows.shape, rows.dtype),
        grid=(count // tile,),
        in_specs=[
            pl.BlockSpec((tile, features), lambda i: (i, 0)),
            pl.BlockSpec((width, width), lambda i: (0, 0)),
        ],
        out_specs=pl.BlockSpec((tile, features), lambda i: (i, 0)),
    )(rows, mix)


def summed_everywhere(rows):
    axes = ("gx", "gy")
    devices = lax.axis_size("gx") * lax.axis_size("gy")
    parts = lax.all_to_all(rows, axes, 0, 0, tiled=True)
    chunk = parts.reshape((devices, rows.shape[0] // devices) + rows.shape[1:]).sum(axis=0)
    copies = jnp.broadcast_to(chunk[None], (devices,) + chunk.shape).reshape(rows.shape)
    return lax.all_to_all(copies, axes, 0, 0, tiled=True)


def localize(
    owners,
    obs_cells,
    block_mask,
    tile_east,
    tile_north,
    span_east,
    span_north,
    tiles_north,
    grid_east,
    grid_north,
):
    place_east = (owners // tiles_north * span_east + obs_cells // span_north).astype(jnp.float32)
    place_north = (owners % tiles_north * span_north + obs_cells % span_north).astype(jnp.float32)
    centre_east = (tile_east * span_east).astype(jnp.float32) + (span_east - 1) / 2.0
    centre_north = (tile_north * span_north).astype(jnp.float32) + (span_north - 1) / 2.0
    gap_east = (
        jnp.remainder(place_east - centre_east + grid_east / 2.0, grid_east) - grid_east / 2.0
    )
    gap_north = (
        jnp.remainder(place_north - centre_north + grid_north / 2.0, grid_north) - grid_north / 2.0
    )
    scale_east = gap_east / (radius_share * grid_east)
    scale_north = gap_north / (radius_share * grid_north)
    weight = jnp.exp(-0.5 * (scale_east * scale_east + scale_north * scale_north))
    blocks = block_mask.shape[0]
    return (weight.reshape(blocks, -1) * block_mask.astype(jnp.float32)[:, None]).reshape(-1)


def transform(predicted, obs_value, obs_error, weight_obs):
    rows, width = predicted.shape
    groups = width // ENS
    members = ENS

    def spread(per_obs):
        return jnp.broadcast_to(per_obs.reshape(rows, groups, 1), (rows, groups, ENS)).reshape(rows, width)

    lane_in = lax.broadcasted_iota(jnp.int32, (width, width), 0) // ENS
    lane_out = lax.broadcasted_iota(jnp.int32, (width, width), 1) // ENS
    averaging = jnp.where(lane_in == lane_out, 1.0 / members, 0.0).astype(jnp.float32)
    centre_obs = product(predicted, averaging)
    error = spread(obs_error)
    deviation = (predicted - centre_obs) / error
    innovation = (spread(obs_value) - centre_obs) / error
    weighted = deviation * spread(weight_obs)
    blocks = product(weighted.T, deviation)
    covariance = sum(blocks[k * ENS:(k + 1) * ENS, k * ENS:(k + 1) * ENS] for k in range(groups))
    projected = jnp.sum(weighted * innovation, axis=0)
    projection = sum(projected[k * ENS:(k + 1) * ENS] for k in range(groups))
    unit_matrix = jnp.eye(members, dtype=jnp.float32)
    system = (members - 1.0) * unit_matrix + covariance
    row_bound = jnp.max(jnp.sum(jnp.abs(system), axis=1))

    def refine(sweep_index, iterates):
        approach, inverse_root = iterates
        middle = 1.5 * unit_matrix - 0.5 * product(inverse_root, approach)
        return (product(approach, middle), product(middle, inverse_root))

    approach, inverse_root = lax.fori_loop(0, NSIT, refine, (system / row_bound, unit_matrix))
    inverse = product(inverse_root, inverse_root) / row_bound
    weights = product(inverse, projection[:, None])[:, 0]
    centring = unit_matrix - 1.0 / members
    shifts = weights[:, None] + math.sqrt(members - 1.0) * inverse_root / jnp.sqrt(row_bound)
    return 1.0 / members + product(centring, shifts)


def block_diagonal(mix, copies):
    return jnp.kron(jnp.eye(copies, dtype=mix.dtype), mix)


def local(state, obs_owner, obs_cell, obs_level, obs_coef, obs_value, obs_error, pattern):
    span_east, span_north, features = state.shape
    tiles_east = lax.axis_size("gx")
    tiles_north = lax.axis_size("gy")
    tile_east = lax.axis_index("gx")
    tile_north = lax.axis_index("gy")
    own_tile = tile_east * tiles_north + tile_north
    field = advance_twice(state)
    cells = field.reshape(span_east * span_north, features)
    width = features // COMP
    groups = width // ENS
    owned = (obs_owner == own_tile).astype(jnp.float32)
    spread_lane = lax.broadcasted_iota(jnp.int32, (groups * width, groups * ENS), 0)
    dense_lane = lax.broadcasted_iota(jnp.int32, (groups * width, groups * ENS), 1)
    fold = (
        (spread_lane // width == dense_lane // ENS) & (spread_lane % ENS == dense_lane % ENS)
    ).astype(jnp.float32)

    def observed(batch_index):
        masked_coefs = obs_coef[batch_index] * owned[batch_index][None, :]
        spread = gather_rows(
            owned[batch_index].astype(jnp.int32),
            obs_cell[batch_index],
            obs_level[batch_index],
            masked_coefs,
            cells,
            fold,
        )
        return spread

    def mixing(local_terms, batch_index):
        predicted = summed_everywhere(local_terms)
        weight_obs = localize(
            obs_owner[batch_index],
            obs_cell[batch_index],
            pattern[0, 0, batch_index],
            tile_east,
            tile_north,
            span_east,
            span_north,
            tiles_north,
            span_east * tiles_east,
            span_north * tiles_north,
        )
        return transform(predicted, obs_value[batch_index], obs_error[batch_index], weight_obs)

    first_mix = mixing(observed(0), 0)
    second_terms = product(observed(1), block_diagonal(first_mix, groups))
    second_mix = mixing(second_terms, 1)
    rows = mixed_once(cells, block_diagonal(product(first_mix, second_mix), groups))
    return rows.reshape(span_east, span_north, features)


def solution(mesh):
    placed = (P("gx", "gy", None), P(), P(), P(), P(), P(), P(), P("gx", "gy", None, None))
    return jax.shard_map(
        local, mesh=mesh, in_specs=placed, out_specs=P("gx", "gy", None), check_vma=False
    )
```

```python
import math

import jax
import jax.numpy as jnp
from jax import lax
from jax.experimental import pallas as pl
from jax.experimental.pallas import tpu as pltpu
from jax.sharding import PartitionSpec as P

ENS = 32
LEV = 4
COMP = 3
NSIT = 4


courant = 0.1
diffusion = 0.08
radius_share = 0.25


def gather_kernel(busy_ref, cell_ref, level_ref, coef_ref, field_ref, fold_ref, out_ref, spread_ref):
    count = cell_ref.shape[0]
    width = field_ref.shape[1] // 3
    lane_level = lax.broadcasted_iota(jnp.int32, (1, width), 1) // ENS
    sublane = lax.broadcasted_iota(jnp.int32, (8, width), 0)
    groups = width // ENS
    spread_ref[...] = jnp.zeros(spread_ref.shape, spread_ref.dtype)

    def body(block, carry):
        @pl.when(busy_ref[block] > 0)
        def _():
            gathered = [jnp.zeros((8, width), jnp.float32) for k in range(groups)]
            for i in range(8):
                for k in range(groups):
                    j = (block * 8 + i) * groups + k
                    picked = field_ref[pl.ds(cell_ref[j], 1), :]
                    value = (
                        coef_ref[j] * picked[:, 0:width]
                        + coef_ref[count + j] * picked[:, width:2 * width]
                        + coef_ref[2 * count + j] * picked[:, 2 * width:3 * width]
                    )
                    value = jnp.where(lane_level == level_ref[j], value, 0.0)
                    gathered[k] = jnp.where(sublane == i, value, gathered[k])
            first = pl.multiple_of(block * 8, 8)
            for k in range(groups):
                spread_ref[pl.ds(first, 8), k * width:(k + 1) * width] = gathered[k]

        return carry

    lax.fori_loop(0, count // (8 * groups), body, 0, unroll=2)
    out_ref[...] = product(spread_ref[...], fold_ref[...])


def gather_rows(flags, cells, levels, coefs, field, fold):
    count = cells.shape[0]
    width = field.shape[1] // 3
    groups = width // ENS
    busy = jnp.max(flags.reshape(-1, 8 * groups), axis=1)
    smem = pl.BlockSpec(memory_space=pltpu.SMEM)
    vmem = pl.BlockSpec(memory_space=pltpu.VMEM)
    return pl.pallas_call(
        gather_kernel,
        out_shape=jax.ShapeDtypeStruct((count // groups, width), jnp.float32),
        in_specs=[smem, smem, smem, smem, vmem, vmem],
        out_specs=vmem,
        scratch_shapes=[pltpu.VMEM((count // groups, groups * width), jnp.float32)],
    )(busy, cells, levels, coefs.reshape(-1), field, fold)


def advect_update(c, w, e, s, n, width):
    u = c[:, 0:width]
    v = c[:, width:2 * width]
    pu, mu = jnp.maximum(u, 0.0), jnp.minimum(u, 0.0)
    pv, mv = jnp.maximum(v, 0.0), jnp.minimum(v, 0.0)
    blocks = []
    for b in range(3):
        lanes = slice(b * width, (b + 1) * width)
        cc, ww, ee, ss, nn = c[:, lanes], w[:, lanes], e[:, lanes], s[:, lanes], n[:, lanes]
        flux = pu * (cc - ww) + mu * (ee - cc) + pv * (cc - ss) + mv * (nn - cc)
        blocks.append(cc - courant * flux + diffusion * (ww + ee + (ss + nn) - 4.0 * cc))
    return blocks


def shifted(values, edge, shift):
    count = values.shape[0]
    row = lax.broadcasted_iota(jnp.int32, values.shape, 0)
    fresh = 0 if shift == 1 else count - 1
    return jnp.where(row == fresh, edge, pltpu.roll(values, shift % count, 0))


def two_steps_kernel(
    field_ref, west_ref, east_ref, south0_ref, south1_ref, north0_ref, north1_ref,
    first_col_ref, last_col_ref, corner_ref, out_ref, mid_ref, ring_ref,
):
    nx, ny, feat = field_ref.shape
    width = feat // 3

    def store(ref, index, blocks):
        for b in range(3):
            ref[index, :, b * width:(b + 1) * width] = blocks[b]

    def first_pass(x, carry):
        centre = field_ref[x]
        west = jnp.where(x == 0, west_ref[1], field_ref[jnp.maximum(x - 1, 0)])
        east = jnp.where(x == nx - 1, east_ref[0], field_ref[jnp.minimum(x + 1, nx - 1)])
        south = shifted(centre, south1_ref[pl.ds(x, 1), :], 1)
        north = shifted(centre, north0_ref[pl.ds(x, 1), :], -1)
        store(mid_ref, x, advect_update(centre, west, east, south, north, width))
        return carry

    lax.fori_loop(0, nx, first_pass, 0)
    corner = corner_ref[...]
    centre = west_ref[1]
    ring_w = advect_update(centre, west_ref[0], field_ref[0], shifted(centre, corner[0:1], 1), shifted(centre, corner[1:2], -1), width)
    centre = east_ref[0]
    ring_e = advect_update(centre, field_ref[nx - 1], east_ref[1], shifted(centre, corner[2:3], 1), shifted(centre, corner[3:4], -1), width)
    centre = south1_ref[...]
    ring_s = advect_update(centre, shifted(centre, corner[0:1], 1), shifted(centre, corner[2:3], -1), south0_ref[...], first_col_ref[...], width)
    centre = north0_ref[...]
    ring_n = advect_update(centre, shifted(centre, corner[1:2], 1), shifted(centre, corner[3:4], -1), last_col_ref[...], north1_ref[...], width)
    store(ring_ref, 0, ring_w)
    store(ring_ref, 1, ring_e)
    for b in range(3):
        ring_ref[2, 0:nx, b * width:(b + 1) * width] = ring_s[b]
        ring_ref[3, 0:nx, b * width:(b + 1) * width] = ring_n[b]

    def second_pass(x, carry):
        centre = mid_ref[x]
        west = jnp.where(x == 0, ring_ref[0], mid_ref[jnp.maximum(x - 1, 0)])
        east = jnp.where(x == nx - 1, ring_ref[1], mid_ref[jnp.minimum(x + 1, nx - 1)])
        south = shifted(centre, ring_ref[2, pl.ds(x, 1), :], 1)
        north = shifted(centre, ring_ref[3, pl.ds(x, 1), :], -1)
        store(out_ref, x, advect_update(centre, west, east, south, north, width))
        return carry

    lax.fori_loop(0, nx, second_pass, 0)


def two_steps(field, west, east, south0, south1, north0, north1, first_col, last_col, corner):
    nx, ny, feat = field.shape
    vmem = pl.BlockSpec(memory_space=pltpu.VMEM)
    return pl.pallas_call(
        two_steps_kernel,
        out_shape=jax.ShapeDtypeStruct(field.shape, field.dtype),
        in_specs=[vmem] * 10,
        out_specs=vmem,
        scratch_shapes=[
            pltpu.VMEM(field.shape, jnp.float32),
            pltpu.VMEM((4, max(nx, ny), feat), jnp.float32),
        ],
    )(field, west, east, south0, south1, north0, north1, first_col, last_col, corner)


def advance_twice(field):
    nx, ny, feat = field.shape
    sx, sy = lax.axis_size("gx"), lax.axis_size("gy")
    up_x = [(i, (i + 1) % sx) for i in range(sx)]
    down_x = [(j, i) for i, j in up_x]
    up_y = [(i, (i + 1) % sy) for i in range(sy)]
    down_y = [(j, i) for i, j in up_y]
    west = lax.ppermute(field[nx - 2:], "gx", up_x)
    east = lax.ppermute(field[:2], "gx", down_x)
    last_cols = jnp.concatenate([west[:, ny - 2:], field[:, ny - 2:], east[:, ny - 2:]])
    first_cols = jnp.concatenate([west[:, :2], field[:, :2], east[:, :2]])
    south = lax.ppermute(last_cols, "gy", up_y)
    north = lax.ppermute(first_cols, "gy", down_y)
    corner = jnp.stack([south[1, 1], north[1, 0], south[nx + 2, 1], north[nx + 2, 0]])
    return two_steps(
        field, west, east, south[2:nx + 2, 0], south[2:nx + 2, 1], north[2:nx + 2, 0], north[2:nx + 2, 1],
        field[:, 0], field[:, ny - 1], corner,
    )


def product(left, right):
    return jnp.dot(left, right, precision=lax.Precision.HIGHEST, preferred_element_type=jnp.float32)


def mix_kernel(rows_ref, mix_ref, out_ref):
    width = mix_ref.shape[0]
    for block in range(rows_ref.shape[1] // width):
        lanes = slice(block * width, (block + 1) * width)
        out_ref[:, lanes] = product(rows_ref[:, lanes], mix_ref[...])


def mixed_once(rows, mix):
    count, features = rows.shape
    width = mix.shape[0]
    tile = 512
    return pl.pallas_call(
        mix_kernel,
        out_shape=jax.ShapeDtypeStruct(rows.shape, rows.dtype),
        grid=(count // tile,),
        in_specs=[
            pl.BlockSpec((tile, features), lambda i: (i, 0)),
            pl.BlockSpec((width, width), lambda i: (0, 0)),
        ],
        out_specs=pl.BlockSpec((tile, features), lambda i: (i, 0)),
    )(rows, mix)


def summed_everywhere(rows):
    axes = ("gx", "gy")
    devices = lax.axis_size("gx") * lax.axis_size("gy")
    parts = lax.all_to_all(rows, axes, 0, 0, tiled=True)
    chunk = parts.reshape((devices, rows.shape[0] // devices) + rows.shape[1:]).sum(axis=0)
    copies = jnp.broadcast_to(chunk[None], (devices,) + chunk.shape).reshape(rows.shape)
    return lax.all_to_all(copies, axes, 0, 0, tiled=True)


def localize(
    owners,
    obs_cells,
    block_mask,
    tile_east,
    tile_north,
    span_east,
    span_north,
    tiles_north,
    grid_east,
    grid_north,
):
    place_east = (owners // tiles_north * span_east + obs_cells // span_north).astype(jnp.float32)
    place_north = (owners % tiles_north * span_north + obs_cells % span_north).astype(jnp.float32)
    centre_east = (tile_east * span_east).astype(jnp.float32) + (span_east - 1) / 2.0
    centre_north = (tile_north * span_north).astype(jnp.float32) + (span_north - 1) / 2.0
    gap_east = (
        jnp.remainder(place_east - centre_east + grid_east / 2.0, grid_east) - grid_east / 2.0
    )
    gap_north = (
        jnp.remainder(place_north - centre_north + grid_north / 2.0, grid_north) - grid_north / 2.0
    )
    scale_east = gap_east / (radius_share * grid_east)
    scale_north = gap_north / (radius_share * grid_north)
    weight = jnp.exp(-0.5 * (scale_east * scale_east + scale_north * scale_north))
    blocks = block_mask.shape[0]
    return (weight.reshape(blocks, -1) * block_mask.astype(jnp.float32)[:, None]).reshape(-1)


def transform(predicted, obs_value, obs_error, weight_obs):
    rows, width = predicted.shape
    groups = width // ENS
    members = ENS

    def spread(per_obs):
        return jnp.broadcast_to(per_obs.reshape(rows, groups, 1), (rows, groups, ENS)).reshape(rows, width)

    lane_in = lax.broadcasted_iota(jnp.int32, (width, width), 0) // ENS
    lane_out = lax.broadcasted_iota(jnp.int32, (width, width), 1) // ENS
    averaging = jnp.where(lane_in == lane_out, 1.0 / members, 0.0).astype(jnp.float32)
    centre_obs = product(predicted, averaging)
    error = spread(obs_error)
    deviation = (predicted - centre_obs) / error
    innovation = (spread(obs_value) - centre_obs) / error
    weighted = deviation * spread(weight_obs)
    blocks = product(weighted.T, deviation)
    covariance = sum(blocks[k * ENS:(k + 1) * ENS, k * ENS:(k + 1) * ENS] for k in range(groups))
    projected = jnp.sum(weighted * innovation, axis=0)
    projection = sum(projected[k * ENS:(k + 1) * ENS] for k in range(groups))
    unit_matrix = jnp.eye(members, dtype=jnp.float32)
    system = (members - 1.0) * unit_matrix + covariance
    row_bound = jnp.max(jnp.sum(jnp.abs(system), axis=1))

    def refine(sweep_index, iterates):
        approach, inverse_root = iterates
        middle = 1.5 * unit_matrix - 0.5 * product(inverse_root, approach)
        return (product(approach, middle), product(middle, inverse_root))

    approach, inverse_root = lax.fori_loop(0, NSIT, refine, (system / row_bound, unit_matrix))
    inverse = product(inverse_root, inverse_root) / row_bound
    weights = product(inverse, projection[:, None])[:, 0]
    centring = unit_matrix - 1.0 / members
    shifts = weights[:, None] + math.sqrt(members - 1.0) * inverse_root / jnp.sqrt(row_bound)
    return 1.0 / members + product(centring, shifts)


def block_diagonal(mix, copies):
    return jnp.kron(jnp.eye(copies, dtype=mix.dtype), mix)


def local(state, obs_owner, obs_cell, obs_level, obs_coef, obs_value, obs_error, pattern):
    span_east, span_north, features = state.shape
    tiles_east = lax.axis_size("gx")
    tiles_north = lax.axis_size("gy")
    tile_east = lax.axis_index("gx")
    tile_north = lax.axis_index("gy")
    own_tile = tile_east * tiles_north + tile_north
    field = advance_twice(state)
    cells = field.reshape(span_east * span_north, features)
    width = features // COMP
    groups = width // ENS
    owned = (obs_owner == own_tile).astype(jnp.float32)
    spread_lane = lax.broadcasted_iota(jnp.int32, (groups * width, groups * ENS), 0)
    dense_lane = lax.broadcasted_iota(jnp.int32, (groups * width, groups * ENS), 1)
    fold = (
        (spread_lane // width == dense_lane // ENS) & (spread_lane % ENS == dense_lane % ENS)
    ).astype(jnp.float32)

    def observed(batch_index):
        masked_coefs = obs_coef[batch_index] * owned[batch_index][None, :]
        spread = gather_rows(
            owned[batch_index].astype(jnp.int32),
            obs_cell[batch_index],
            obs_level[batch_index],
            masked_coefs,
            cells,
            fold,
        )
        return spread

    def mixing(local_terms, batch_index):
        predicted = summed_everywhere(local_terms)
        weight_obs = localize(
            obs_owner[batch_index],
            obs_cell[batch_index],
            pattern[0, 0, batch_index],
            tile_east,
            tile_north,
            span_east,
            span_north,
            tiles_north,
            span_east * tiles_east,
            span_north * tiles_north,
        )
        return transform(predicted, obs_value[batch_index], obs_error[batch_index], weight_obs)

    first_mix = mixing(observed(0), 0)
    second_terms = product(observed(1), block_diagonal(first_mix, groups))
    second_mix = mixing(second_terms, 1)
    rows = mixed_once(cells, block_diagonal(product(first_mix, second_mix), groups))
    return rows.reshape(span_east, span_north, features)


def solution(mesh):
    placed = (P("gx", "gy", None), P(), P(), P(), P(), P(), P(), P("gx", "gy", None, None))
    return jax.shard_map(
        local, mesh=mesh, in_specs=placed, out_specs=P("gx", "gy", None), check_vma=False
    )
```

```python
import math

import jax
import jax.numpy as jnp
from jax import lax
from jax.experimental import pallas as pl
from jax.experimental.pallas import tpu as pltpu
from jax.sharding import PartitionSpec as P

ENS = 32
LEV = 4
COMP = 3
NSIT = 4


courant = 0.1
diffusion = 0.08
radius_share = 0.25


def gather_kernel(busy_ref, cell_ref, level_ref, coef_ref, field_ref, fold_ref, out_ref, spread_ref):
    count = cell_ref.shape[0]
    width = field_ref.shape[1] // 3
    lane_level = lax.broadcasted_iota(jnp.int32, (1, width), 1) // ENS
    sublane = lax.broadcasted_iota(jnp.int32, (8, width), 0)
    groups = width // ENS

    def body(block, carry):
        @pl.when(busy_ref[block] == 0)
        def _():
            first = pl.multiple_of(block * 8, 8)
            spread_ref[pl.ds(first, 8), :] = jnp.zeros((8, spread_ref.shape[1]), jnp.float32)

        @pl.when(busy_ref[block] > 0)
        def _():
            gathered = [jnp.zeros((8, width), jnp.float32) for k in range(groups)]
            for i in range(8):
                for k in range(groups):
                    j = (block * 8 + i) * groups + k
                    picked = field_ref[pl.ds(cell_ref[j], 1), :]
                    value = (
                        coef_ref[j] * picked[:, 0:width]
                        + coef_ref[count + j] * picked[:, width:2 * width]
                        + coef_ref[2 * count + j] * picked[:, 2 * width:3 * width]
                    )
                    value = jnp.where(lane_level == level_ref[j], value, 0.0)
                    gathered[k] = jnp.where(sublane == i, value, gathered[k])
            first = pl.multiple_of(block * 8, 8)
            for k in range(groups):
                spread_ref[pl.ds(first, 8), k * width:(k + 1) * width] = gathered[k]

        return carry

    lax.fori_loop(0, count // (8 * groups), body, 0)
    out_ref[...] = product(spread_ref[...], fold_ref[...])


def gather_rows(flags, cells, levels, coefs, field, fold):
    count = cells.shape[0]
    width = field.shape[1] // 3
    groups = width // ENS
    busy = jnp.max(flags.reshape(-1, 8 * groups), axis=1)
    smem = pl.BlockSpec(memory_space=pltpu.SMEM)
    vmem = pl.BlockSpec(memory_space=pltpu.VMEM)
    return pl.pallas_call(
        gather_kernel,
        out_shape=jax.ShapeDtypeStruct((count // groups, width), jnp.float32),
        in_specs=[smem, smem, smem, smem, vmem, vmem],
        out_specs=vmem,
        scratch_shapes=[pltpu.VMEM((count // groups, groups * width), jnp.float32)],
    )(busy, cells, levels, coefs.reshape(-1), field, fold)


def advect_update(c, w, e, s, n, width):
    u = c[:, 0:width]
    v = c[:, width:2 * width]
    pu, mu = jnp.maximum(u, 0.0), jnp.minimum(u, 0.0)
    pv, mv = jnp.maximum(v, 0.0), jnp.minimum(v, 0.0)
    blocks = []
    for b in range(3):
        lanes = slice(b * width, (b + 1) * width)
        cc, ww, ee, ss, nn = c[:, lanes], w[:, lanes], e[:, lanes], s[:, lanes], n[:, lanes]
        flux = pu * (cc - ww) + mu * (ee - cc) + pv * (cc - ss) + mv * (nn - cc)
        blocks.append(cc - courant * flux + diffusion * (ww + ee + (ss + nn) - 4.0 * cc))
    return blocks


def shifted(values, edge, shift):
    count = values.shape[0]
    row = lax.broadcasted_iota(jnp.int32, values.shape, 0)
    fresh = 0 if shift == 1 else count - 1
    return jnp.where(row == fresh, edge, pltpu.roll(values, shift % count, 0))


def two_steps_kernel(
    field_ref, west_ref, east_ref, south0_ref, south1_ref, north0_ref, north1_ref,
    first_col_ref, last_col_ref, corner_ref, out_ref, mid_ref, ring_ref,
):
    nx, ny, feat = field_ref.shape
    width = feat // 3

    def store(ref, index, blocks):
        for b in range(3):
            ref[index, :, b * width:(b + 1) * width] = blocks[b]

    def first_pass(x, carry):
        centre = field_ref[x]
        west = jnp.where(x == 0, west_ref[1], field_ref[jnp.maximum(x - 1, 0)])
        east = jnp.where(x == nx - 1, east_ref[0], field_ref[jnp.minimum(x + 1, nx - 1)])
        south = shifted(centre, south1_ref[pl.ds(x, 1), :], 1)
        north = shifted(centre, north0_ref[pl.ds(x, 1), :], -1)
        store(mid_ref, x, advect_update(centre, west, east, south, north, width))
        return carry

    lax.fori_loop(0, nx, first_pass, 0)
    corner = corner_ref[...]
    centre = west_ref[1]
    ring_w = advect_update(centre, west_ref[0], field_ref[0], shifted(centre, corner[0:1], 1), shifted(centre, corner[1:2], -1), width)
    centre = east_ref[0]
    ring_e = advect_update(centre, field_ref[nx - 1], east_ref[1], shifted(centre, corner[2:3], 1), shifted(centre, corner[3:4], -1), width)
    centre = south1_ref[...]
    ring_s = advect_update(centre, shifted(centre, corner[0:1], 1), shifted(centre, corner[2:3], -1), south0_ref[...], first_col_ref[...], width)
    centre = north0_ref[...]
    ring_n = advect_update(centre, shifted(centre, corner[1:2], 1), shifted(centre, corner[3:4], -1), last_col_ref[...], north1_ref[...], width)
    store(ring_ref, 0, ring_w)
    store(ring_ref, 1, ring_e)
    for b in range(3):
        ring_ref[2, 0:nx, b * width:(b + 1) * width] = ring_s[b]
        ring_ref[3, 0:nx, b * width:(b + 1) * width] = ring_n[b]

    def second_pass(x, carry):
        centre = mid_ref[x]
        west = jnp.where(x == 0, ring_ref[0], mid_ref[jnp.maximum(x - 1, 0)])
        east = jnp.where(x == nx - 1, ring_ref[1], mid_ref[jnp.minimum(x + 1, nx - 1)])
        south = shifted(centre, ring_ref[2, pl.ds(x, 1), :], 1)
        north = shifted(centre, ring_ref[3, pl.ds(x, 1), :], -1)
        store(out_ref, x, advect_update(centre, west, east, south, north, width))
        return carry

    lax.fori_loop(0, nx, second_pass, 0)


def two_steps(field, west, east, south0, south1, north0, north1, first_col, last_col, corner):
    nx, ny, feat = field.shape
    vmem = pl.BlockSpec(memory_space=pltpu.VMEM)
    return pl.pallas_call(
        two_steps_kernel,
        out_shape=jax.ShapeDtypeStruct(field.shape, field.dtype),
        in_specs=[vmem] * 10,
        out_specs=vmem,
        scratch_shapes=[
            pltpu.VMEM(field.shape, jnp.float32),
            pltpu.VMEM((4, max(nx, ny), feat), jnp.float32),
        ],
    )(field, west, east, south0, south1, north0, north1, first_col, last_col, corner)


def advance_twice(field):
    nx, ny, feat = field.shape
    sx, sy = lax.axis_size("gx"), lax.axis_size("gy")
    up_x = [(i, (i + 1) % sx) for i in range(sx)]
    down_x = [(j, i) for i, j in up_x]
    up_y = [(i, (i + 1) % sy) for i in range(sy)]
    down_y = [(j, i) for i, j in up_y]
    west = lax.ppermute(field[nx - 2:], "gx", up_x)
    east = lax.ppermute(field[:2], "gx", down_x)
    last_cols = jnp.concatenate([west[:, ny - 2:], field[:, ny - 2:], east[:, ny - 2:]])
    first_cols = jnp.concatenate([west[:, :2], field[:, :2], east[:, :2]])
    south = lax.ppermute(last_cols, "gy", up_y)
    north = lax.ppermute(first_cols, "gy", down_y)
    corner = jnp.stack([south[1, 1], north[1, 0], south[nx + 2, 1], north[nx + 2, 0]])
    return two_steps(
        field, west, east, south[2:nx + 2, 0], south[2:nx + 2, 1], north[2:nx + 2, 0], north[2:nx + 2, 1],
        field[:, 0], field[:, ny - 1], corner,
    )


def product(left, right):
    return jnp.dot(left, right, precision=lax.Precision.HIGHEST, preferred_element_type=jnp.float32)


def mix_kernel(rows_ref, mix_ref, out_ref):
    width = mix_ref.shape[0]
    for block in range(rows_ref.shape[1] // width):
        lanes = slice(block * width, (block + 1) * width)
        out_ref[:, lanes] = product(rows_ref[:, lanes], mix_ref[...])


def mixed_once(rows, mix):
    count, features = rows.shape
    width = mix.shape[0]
    tile = 512
    return pl.pallas_call(
        mix_kernel,
        out_shape=jax.ShapeDtypeStruct(rows.shape, rows.dtype),
        grid=(count // tile,),
        in_specs=[
            pl.BlockSpec((tile, features), lambda i: (i, 0)),
            pl.BlockSpec((width, width), lambda i: (0, 0)),
        ],
        out_specs=pl.BlockSpec((tile, features), lambda i: (i, 0)),
    )(rows, mix)


def summed_everywhere(rows):
    axes = ("gx", "gy")
    devices = lax.axis_size("gx") * lax.axis_size("gy")
    parts = lax.all_to_all(rows, axes, 0, 0, tiled=True)
    chunk = parts.reshape((devices, rows.shape[0] // devices) + rows.shape[1:]).sum(axis=0)
    copies = jnp.broadcast_to(chunk[None], (devices,) + chunk.shape).reshape(rows.shape)
    return lax.all_to_all(copies, axes, 0, 0, tiled=True)


def localize(
    owners,
    obs_cells,
    block_mask,
    tile_east,
    tile_north,
    span_east,
    span_north,
    tiles_north,
    grid_east,
    grid_north,
):
    place_east = (owners // tiles_north * span_east + obs_cells // span_north).astype(jnp.float32)
    place_north = (owners % tiles_north * span_north + obs_cells % span_north).astype(jnp.float32)
    centre_east = (tile_east * span_east).astype(jnp.float32) + (span_east - 1) / 2.0
    centre_north = (tile_north * span_north).astype(jnp.float32) + (span_north - 1) / 2.0
    gap_east = (
        jnp.remainder(place_east - centre_east + grid_east / 2.0, grid_east) - grid_east / 2.0
    )
    gap_north = (
        jnp.remainder(place_north - centre_north + grid_north / 2.0, grid_north) - grid_north / 2.0
    )
    scale_east = gap_east / (radius_share * grid_east)
    scale_north = gap_north / (radius_share * grid_north)
    weight = jnp.exp(-0.5 * (scale_east * scale_east + scale_north * scale_north))
    blocks = block_mask.shape[0]
    return (weight.reshape(blocks, -1) * block_mask.astype(jnp.float32)[:, None]).reshape(-1)


def transform(predicted, obs_value, obs_error, weight_obs):
    rows, width = predicted.shape
    groups = width // ENS
    members = ENS

    def spread(per_obs):
        return jnp.broadcast_to(per_obs.reshape(rows, groups, 1), (rows, groups, ENS)).reshape(rows, width)

    lane_in = lax.broadcasted_iota(jnp.int32, (width, width), 0) // ENS
    lane_out = lax.broadcasted_iota(jnp.int32, (width, width), 1) // ENS
    averaging = jnp.where(lane_in == lane_out, 1.0 / members, 0.0).astype(jnp.float32)
    centre_obs = product(predicted, averaging)
    error = spread(obs_error)
    deviation = (predicted - centre_obs) / error
    innovation = (spread(obs_value) - centre_obs) / error
    weighted = deviation * spread(weight_obs)
    blocks = product(weighted.T, deviation)
    covariance = sum(blocks[k * ENS:(k + 1) * ENS, k * ENS:(k + 1) * ENS] for k in range(groups))
    projected = jnp.sum(weighted * innovation, axis=0)
    projection = sum(projected[k * ENS:(k + 1) * ENS] for k in range(groups))
    unit_matrix = jnp.eye(members, dtype=jnp.float32)
    system = (members - 1.0) * unit_matrix + covariance
    row_bound = jnp.max(jnp.sum(jnp.abs(system), axis=1))

    def refine(sweep_index, iterates):
        approach, inverse_root = iterates
        middle = 1.5 * unit_matrix - 0.5 * product(inverse_root, approach)
        return (product(approach, middle), product(middle, inverse_root))

    approach, inverse_root = lax.fori_loop(0, NSIT, refine, (system / row_bound, unit_matrix))
    inverse = product(inverse_root, inverse_root) / row_bound
    weights = product(inverse, projection[:, None])[:, 0]
    centring = unit_matrix - 1.0 / members
    shifts = weights[:, None] + math.sqrt(members - 1.0) * inverse_root / jnp.sqrt(row_bound)
    return 1.0 / members + product(centring, shifts)


def block_diagonal(mix, copies):
    return jnp.kron(jnp.eye(copies, dtype=mix.dtype), mix)


def local(state, obs_owner, obs_cell, obs_level, obs_coef, obs_value, obs_error, pattern):
    span_east, span_north, features = state.shape
    tiles_east = lax.axis_size("gx")
    tiles_north = lax.axis_size("gy")
    tile_east = lax.axis_index("gx")
    tile_north = lax.axis_index("gy")
    own_tile = tile_east * tiles_north + tile_north
    field = advance_twice(state)
    cells = field.reshape(span_east * span_north, features)
    width = features // COMP
    groups = width // ENS
    owned = (obs_owner == own_tile).astype(jnp.float32)
    spread_lane = lax.broadcasted_iota(jnp.int32, (groups * width, groups * ENS), 0)
    dense_lane = lax.broadcasted_iota(jnp.int32, (groups * width, groups * ENS), 1)
    fold = (
        (spread_lane // width == dense_lane // ENS) & (spread_lane % ENS == dense_lane % ENS)
    ).astype(jnp.float32)

    def observed(batch_index):
        masked_coefs = obs_coef[batch_index] * owned[batch_index][None, :]
        spread = gather_rows(
            owned[batch_index].astype(jnp.int32),
            obs_cell[batch_index],
            obs_level[batch_index],
            masked_coefs,
            cells,
            fold,
        )
        return spread

    def mixing(local_terms, batch_index):
        predicted = summed_everywhere(local_terms)
        weight_obs = localize(
            obs_owner[batch_index],
            obs_cell[batch_index],
            pattern[0, 0, batch_index],
            tile_east,
            tile_north,
            span_east,
            span_north,
            tiles_north,
            span_east * tiles_east,
            span_north * tiles_north,
        )
        return transform(predicted, obs_value[batch_index], obs_error[batch_index], weight_obs)

    first_mix = mixing(observed(0), 0)
    second_terms = product(observed(1), block_diagonal(first_mix, groups))
    second_mix = mixing(second_terms, 1)
    rows = mixed_once(cells, block_diagonal(product(first_mix, second_mix), groups))
    return rows.reshape(span_east, span_north, features)


def solution(mesh):
    placed = (P("gx", "gy", None), P(), P(), P(), P(), P(), P(), P("gx", "gy", None, None))
    return jax.shard_map(
        local, mesh=mesh, in_specs=placed, out_specs=P("gx", "gy", None), check_vma=False
    )
```
